512 devices in a mesh: row: 32 (over z, y_lo), col: 16 (over x, y_hi, core).
Axes of the slice: x: 4, y: 4 (y_hi: 2, y_lo: 2; y = y_hi * 2 + y_lo), z: 16, core: 2. Of those that a mesh axis runs over, the one named last changes fastest.
Arguments:
- inputs: bfloat16 [1, 256, 256, 1024], P(None, 'row', 'col'), may hold values from -6 to 6
- norm_gain: float32 [1024], replicated, may hold values from 0.1 to 1.9
- w_query: bfloat16 [1024, 512], P('row'), may hold values from -8 to 8
- w_keyvalue: bfloat16 [1024, 1024], P('row'), may hold values from -0.1875 to 0.1875
- w_output: bfloat16 [512, 1024], P('row'), may hold values from -0.25 to 0.25
- out_grad: bfloat16 [1, 256, 256, 1024], P(None, 'row', 'col'), may hold values from -6 to 6
Outputs:
- layer_out: bfloat16 [1, 256, 256, 1024], P(None, 'row', 'col')
- in_grad: bfloat16 [1, 256, 256, 1024], P(None, 'row', 'col')
- keyvalue_grad: float32 [1024, 1024], P('row')
The draws below stay inside these ranges and needn't reach their ends.
All inputs are finite; a program needn't handle non-finite values.
Results may differ from the reference program's by a relative error of at most 0.012.
The reference program's roundings to bfloat16 on the way count: a program that leaves them out, or rounds other values in their place, can miss the bound.
Values may be sent and summed in bfloat16 or wider, within the bound.
No kernel may reach another device: no remote copies, remote signals or barrier semaphores. Data moves between devices by JAX's collectives and lax.ppermute only.
A program may use at most 64 MiB of HBM per device.

```python
import math
import jax
import jax.numpy as jnp
from jax import lax

D = 1024
HEADS = 8
HSIZE = 64
RADIUS = 6
BATCH = 1
TR = 8
TC = 16
HD = 512
HEIGHT = 256
WIDTH = 256
N_ROW = 32
N_COL = 16


def draw_w_query(key, part):
    first_key = jax.random.fold_in(key, 11)
    values = jax.random.normal(first_key, (D, HEADS * HSIZE), jnp.float32) / math.sqrt(D)
    return jnp.clip(values, -8.0, 8.0).astype(jnp.bfloat16)


def strengthened(values, key, source, target, blocks, factor):
    owner, partner = [(jnp.arange(values.shape[axis_at]) // (values.shape[axis_at] // blocks)).reshape([-1 if axis == axis_at else 1 for axis in range(values.ndim)]) for axis_at in (source, target)]
    chosen = jax.random.permutation(key, blocks)[partner]
    strong = (owner == chosen) | (owner == (partner + blocks // 2) % blocks)
    return jnp.where(strong, factor * values, values)


def level_of(key, dims, pieces, least, top_value):
    def one(dim, blocks):
        steps = jax.random.uniform(jax.random.fold_in(jax.random.fold_in(key, 6), dim), (blocks,), jnp.float32, least / len(pieces), top_value / len(pieces))
        return jnp.repeat(jnp.exp(steps), dims[dim] // blocks).reshape((-1,) + (1,) * (len(dims) - dim - 1))

    loudness = one(*pieces[0])
    for cut in pieces[1:]:
        loudness = loudness * one(*cut)
    return loudness


def gaussian(stream_key, dims, deviation, limit, cuts=(), kind=jnp.bfloat16):
    values = deviation * jax.random.normal(stream_key, dims, jnp.float32)
    if cuts:
        values = values * level_of(stream_key, dims, cuts, -0.22, 0.18)
    return jnp.clip(values, -limit, limit).astype(kind)


def bell_draw_with(stream_key, shape, deviation, reach, shards, heavy, held_as=jnp.bfloat16):
    values = deviation * jax.random.normal(stream_key, shape, jnp.float32)
    if shards:
        values = values * level_of(stream_key, shape, shards, -0.22, 0.18)
    return jnp.clip(strengthened(values, jax.random.fold_in(stream_key, 3), *heavy), -reach, reach).astype(held_as)


def setup_inputs(seed: int = 0) -> dict:
    arg_keys = jax.random.split(jax.random.key(seed), 7)
    inputs = bell_draw_with(arg_keys[0], (BATCH, HEIGHT, WIDTH, D), 1.0, 6.0, ((1, 32), (2, 16)), (1, 3, 32, 2.75))
    norm_gain = jnp.clip(1.0 + 0.18 * jax.random.normal(arg_keys[1], (D,), jnp.float32), 0.1, 1.9)
    w_query = draw_w_query(jax.random.fold_in(arg_keys[6], 71), 0)
    w_keyvalue = gaussian(arg_keys[3], (D, 2 * HD), D ** -0.5, 0.1875, ((0, 32),))
    w_output = gaussian(arg_keys[4], (HD, D), HD ** -0.5, 0.25, ((0, 32),))
    out_grad = gaussian(arg_keys[5], (BATCH, HEIGHT, WIDTH, D), 1.0, 6.0, ((1, 32), (2, 16)))
    return dict(inputs=inputs, norm_gain=norm_gain, w_query=w_query, w_keyvalue=w_keyvalue, w_output=w_output, out_grad=out_grad)


EPS = 1e-05
MASKED = -1e+30

def normalize(inputs, norm_gain):
    values = inputs.astype(jnp.float32)
    center = values - lax.optimization_barrier(jnp.mean(values, axis=-1, keepdims=True))
    spread = lax.rsqrt(lax.optimization_barrier(jnp.mean(center * center, axis=-1, keepdims=True)) + EPS)
    standard = center * spread
    return (standard, spread, (standard * norm_gain).astype(jnp.bfloat16))

def window_mask(row_start, col_start, tile_rows, tile_cols, height, map_width):
    ext_rows = tile_rows + 2 * RADIUS
    ext_cols = tile_cols + 2 * RADIUS
    query_pos = jnp.arange(tile_rows * tile_cols, dtype=jnp.int32)
    query_row = query_pos // tile_cols
    query_col = query_pos % tile_cols
    ext_pos = jnp.arange(ext_rows * ext_cols, dtype=jnp.int32)
    ext_row = ext_pos // ext_cols
    ext_col = ext_pos % ext_cols
    nearby = (jnp.abs(ext_row[None, :] - RADIUS - query_row[:, None]) <= RADIUS) & (jnp.abs(ext_col[None, :] - RADIUS - query_col[:, None]) <= RADIUS)
    global_row = row_start + ext_row - RADIUS
    global_col = col_start + ext_col - RADIUS
    inside = (global_row >= 0) & (global_row < height) & (global_col >= 0) & (global_col < map_width)
    return nearby & inside[None, :]

def tile_forward(queries, keyvalue_ext, allowed):
    batches, query_count, inner_width = queries.shape
    head_size = inner_width // HEADS
    query_heads = queries.reshape(batches, query_count, HEADS, head_size).astype(jnp.float32)
    key_heads = keyvalue_ext[:, :, :inner_width].reshape(batches, -1, HEADS, head_size).astype(jnp.float32)
    value_heads = keyvalue_ext[:, :, inner_width:].reshape(batches, -1, HEADS, head_size).astype(jnp.float32)
    scores = jnp.einsum('bqhd,bkhd->bhqk', query_heads, key_heads) / math.sqrt(head_size)
    scores = jnp.where(allowed, scores, MASKED)
    row_max = lax.optimization_barrier(jnp.max(scores, axis=-1, keepdims=True))
    exponent = jnp.exp(scores - row_max)
    soft = exponent / lax.optimization_barrier(jnp.sum(exponent, axis=-1, keepdims=True))
    rounded = soft.astype(jnp.bfloat16)
    attended = jnp.einsum('bhqk,bkhd->bqhd', rounded.astype(jnp.float32), value_heads)
    return (attended.astype(jnp.bfloat16).reshape(batches, query_count, inner_width), soft, rounded)

def tile_backward(queries, keyvalue_ext, soft, rounded, inner_grad):
    batches, query_count, inner_width = queries.shape
    head_size = inner_width // HEADS
    query_heads = queries.reshape(batches, query_count, HEADS, head_size).astype(jnp.float32)
    key_heads = keyvalue_ext[:, :, :inner_width].reshape(batches, -1, HEADS, head_size).astype(jnp.float32)
    value_heads = keyvalue_ext[:, :, inner_width:].reshape(batches, -1, HEADS, head_size).astype(jnp.float32)
    grad_heads = inner_grad.reshape(batches, query_count, HEADS, head_size).astype(jnp.float32)
    prob_grad = jnp.einsum('bqhd,bkhd->bhqk', grad_heads, value_heads)
    row_dot = lax.optimization_barrier(jnp.sum(soft * prob_grad, axis=-1, keepdims=True))
    score_grad = (soft * (prob_grad - row_dot) / math.sqrt(head_size)).astype(jnp.bfloat16).astype(jnp.float32)
    query_grad = jnp.einsum('bhqk,bkhd->bqhd', score_grad, key_heads)
    key_grad = jnp.einsum('bhqk,bqhd->bkhd', score_grad, query_heads)
    value_grad = jnp.einsum('bhqk,bqhd->bkhd', rounded.astype(jnp.float32), grad_heads)
    ext_count = key_grad.shape[1]
    joined = jnp.concatenate([key_grad.reshape(batches, ext_count, inner_width), value_grad.reshape(batches, ext_count, inner_width)], axis=-1)
    return (query_grad.astype(jnp.bfloat16).reshape(batches, query_count, inner_width), joined)

def reference(inputs, norm_gain, w_query, w_keyvalue, w_output, out_grad):
    batches, height, map_width, model_width = inputs.shape
    inner_width = w_query.shape[1]
    ext_rows = TR + 2 * RADIUS
    ext_cols = TC + 2 * RADIUS
    standard, spread, normed = normalize(inputs, norm_gain)
    flat_norm = normed.reshape(-1, model_width)
    queries = jnp.dot(flat_norm, w_query, preferred_element_type=jnp.float32).astype(jnp.bfloat16)
    queries = queries.reshape(batches, height, map_width, inner_width)
    keyvalue = jnp.dot(flat_norm, w_keyvalue, preferred_element_type=jnp.float32).astype(jnp.bfloat16)
    keyvalue = keyvalue.reshape(batches, height, map_width, 2 * inner_width)
    inner_grad = jnp.dot(out_grad.reshape(-1, model_width), w_output.T, preferred_element_type=jnp.float32).astype(jnp.bfloat16)
    inner_grad = inner_grad.reshape(batches, height, map_width, inner_width)
    padded = jnp.pad(keyvalue, ((0, 0), (RADIUS, RADIUS), (RADIUS, RADIUS), (0, 0)))
    zero = jnp.zeros((), jnp.int32)

    def visit(tile_index, carry):
        attended_map, query_grad_map, grad_pad = carry
        tile_index = tile_index.astype(jnp.int32)
        row_start = (tile_index // N_COL * TR).astype(jnp.int32)
        col_start = (tile_index % N_COL * TC).astype(jnp.int32)
        tile_query = lax.dynamic_slice(queries, (zero, row_start, col_start, zero), (batches, TR, TC, inner_width)).reshape(batches, TR * TC, inner_width)
        tile_grad = lax.dynamic_slice(inner_grad, (zero, row_start, col_start, zero), (batches, TR, TC, inner_width)).reshape(batches, TR * TC, inner_width)
        tile_keyvalue = lax.dynamic_slice(padded, (zero, row_start, col_start, zero), (batches, ext_rows, ext_cols, 2 * inner_width))
        tile_keyvalue = tile_keyvalue.reshape(batches, ext_rows * ext_cols, 2 * inner_width)
        allowed = window_mask(row_start, col_start, TR, TC, height, map_width)
        attended, soft, rounded = tile_forward(tile_query, tile_keyvalue, allowed)
        query_grad, keyvalue_part = tile_backward(tile_query, tile_keyvalue, soft, rounded, tile_grad)
        attended_map = lax.dynamic_update_slice(attended_map, attended.reshape(batches, TR, TC, inner_width), (zero, row_start, col_start, zero))
        query_grad_map = lax.dynamic_update_slice(query_grad_map, query_grad.reshape(batches, TR, TC, inner_width), (zero, row_start, col_start, zero))
        current = lax.dynamic_slice(grad_pad, (zero, row_start, col_start, zero), (batches, ext_rows, ext_cols, 2 * inner_width))
        current = current + keyvalue_part.reshape(batches, ext_rows, ext_cols, 2 * inner_width)
        grad_pad = lax.dynamic_update_slice(grad_pad, current, (zero, row_start, col_start, zero))
        return (attended_map, query_grad_map, grad_pad)
    start_carry = (jnp.zeros((batches, height, map_width, inner_width), jnp.bfloat16), jnp.zeros((batches, height, map_width, inner_width), jnp.bfloat16), jnp.zeros((batches, height + 2 * RADIUS, map_width + 2 * RADIUS, 2 * inner_width), jnp.float32))
    attended_map, query_grad_map, grad_pad = lax.fori_loop(0, N_ROW * N_COL, visit, start_carry)
    token_grad = grad_pad[:, RADIUS:RADIUS + height, RADIUS:RADIUS + map_width].astype(jnp.bfloat16)
    token_grad = token_grad.reshape(-1, 2 * inner_width)
    projected = jnp.dot(attended_map.reshape(-1, inner_width), w_output, preferred_element_type=jnp.float32)
    layer_out = (inputs.astype(jnp.float32) + projected.reshape(inputs.shape)).astype(jnp.bfloat16)
    keyvalue_grad = jnp.dot(flat_norm.T, token_grad, preferred_element_type=jnp.float32)
    normed_grad = jnp.dot(query_grad_map.reshape(-1, inner_width), w_query.T, preferred_element_type=jnp.float32)
    normed_grad = normed_grad + jnp.dot(token_grad, w_keyvalue.T, preferred_element_type=jnp.float32)
    gained = normed_grad.reshape(inputs.shape) * norm_gain
    in_grad = out_grad.astype(jnp.float32) + spread * (gained - lax.optimization_barrier(jnp.mean(gained, axis=-1, keepdims=True)) - standard * lax.optimization_barrier(jnp.mean(gained * standard, axis=-1, keepdims=True)))
    return (layer_out, in_grad.astype(jnp.bfloat16), keyvalue_grad)
```

```python
import math

import jax
import jax.numpy as jnp
from jax import lax
from jax.sharding import PartitionSpec as P

HEADS = 8
RADIUS = 6


EPS = 1e-05
MASKED = -1e30


def shifted(value, axis, steps):
    count = lax.axis_size(axis)
    first, last = (max(0, -steps), min(count, count - steps))
    return lax.ppermute(value, axis, [(source, source + steps) for source in range(first, last)])


def with_halo(block, sides, width):
    for axis, dim in sides:
        count = lax.axis_size(axis)
        forward = [(i, i + 1) for i in range(count - 1)]
        backward = [(target, source) for source, target in forward]
        low = lax.ppermute(
            lax.slice_in_dim(block, block.shape[dim] - width, None, axis=dim), axis, forward
        )
        high = lax.ppermute(lax.slice_in_dim(block, 0, width, axis=dim), axis, backward)
        block = jnp.concatenate([low, block, high], axis=dim)
    return block


def partner_swap(value, axis, bit):
    count = lax.axis_size(axis)
    return lax.ppermute(value, axis, [(i, i ^ (1 << bit)) for i in range(count)])


def low_half(axis, bit):
    return (lax.axis_index(axis) // (1 << bit)) % 2 == 0


def gather_by_bits(block, axis, bits, dim=0):
    count = lax.axis_size(axis)
    levels = count.bit_length() - 1
    shape = block.shape
    held = block.reshape(shape[:dim] + (1,) * levels + shape[dim:])
    for bit in bits:
        place = dim + levels - 1 - bit
        other = partner_swap(held, axis, bit)
        held = jnp.where(
            low_half(axis, bit),
            jnp.concatenate([held, other], place),
            jnp.concatenate([other, held], place),
        )
    return held.reshape(shape[:dim] + (count * shape[dim],) + shape[dim + 1 :])


def scatter_by_bits(total, axis, bits, dim=0):
    count = lax.axis_size(axis)
    levels = count.bit_length() - 1
    shape = total.shape
    piece = shape[dim] // count
    held = total.reshape(shape[:dim] + (2,) * levels + (piece,) + shape[dim + 1 :])
    for bit in bits:
        place = dim + levels - 1 - bit
        first = lax.index_in_dim(held, 0, place)
        second = lax.index_in_dim(held, 1, place)
        low = low_half(axis, bit)
        keep = jnp.where(low, first, second)
        send = jnp.where(low, second, first)
        held = keep + partner_swap(send, axis, bit)
    return held.reshape(shape[:dim] + (piece,) + shape[dim + 1 :])


def normalize(inputs, norm_gain):
    values = inputs.astype(jnp.float32)
    center = values - jnp.mean(values, axis=-1, keepdims=True)
    spread = lax.rsqrt(jnp.mean(center * center, axis=-1, keepdims=True) + EPS)
    standard = center * spread
    return (standard, spread, (standard * norm_gain).astype(jnp.bfloat16))


def window_mask(row_start, col_start, tile_rows, tile_cols, height, map_width):
    ext_rows = tile_rows + 2 * RADIUS
    ext_cols = tile_cols + 2 * RADIUS
    query_pos = jnp.arange(tile_rows * tile_cols, dtype=jnp.int32)
    query_row = query_pos // tile_cols
    query_col = query_pos % tile_cols
    ext_pos = jnp.arange(ext_rows * ext_cols, dtype=jnp.int32)
    ext_row = ext_pos // ext_cols
    ext_col = ext_pos % ext_cols
    nearby = (jnp.abs(ext_row[None, :] - RADIUS - query_row[:, None]) <= RADIUS) & (
        jnp.abs(ext_col[None, :] - RADIUS - query_col[:, None]) <= RADIUS
    )
    global_row = row_start + ext_row - RADIUS
    global_col = col_start + ext_col - RADIUS
    inside = (
        (global_row >= 0) & (global_row < height) & (global_col >= 0) & (global_col < map_width)
    )
    return nearby & inside[None, :]


def tile_forward(queries, keyvalue_ext, allowed):
    batches, query_count, inner_width = queries.shape
    head_size = inner_width // HEADS
    query_heads = queries.reshape(batches, query_count, HEADS, head_size)
    key_heads = keyvalue_ext[:, :, :inner_width].reshape(batches, -1, HEADS, head_size)
    value_heads = keyvalue_ext[:, :, inner_width:].reshape(batches, -1, HEADS, head_size)
    scores = jnp.einsum(
        "bqhd,bkhd->bhqk", query_heads, key_heads, preferred_element_type=jnp.float32
    ) / math.sqrt(head_size)
    scores = jnp.where(allowed, scores, MASKED)
    row_max = jnp.max(scores, axis=-1, keepdims=True)
    exponent = jnp.exp(scores - row_max)
    soft = exponent / jnp.sum(exponent, axis=-1, keepdims=True)
    rounded = soft.astype(jnp.bfloat16)
    attended = jnp.einsum(
        "bhqk,bkhd->bqhd", rounded, value_heads, preferred_element_type=jnp.float32
    )
    return (attended.astype(jnp.bfloat16).reshape(batches, query_count, inner_width), soft, rounded)


def tile_backward(queries, keyvalue_ext, soft, rounded, inner_grad):
    batches, query_count, inner_width = queries.shape
    head_size = inner_width // HEADS
    query_heads = queries.reshape(batches, query_count, HEADS, head_size)
    key_heads = keyvalue_ext[:, :, :inner_width].reshape(batches, -1, HEADS, head_size)
    value_heads = keyvalue_ext[:, :, inner_width:].reshape(batches, -1, HEADS, head_size)
    grad_heads = inner_grad.reshape(batches, query_count, HEADS, head_size)
    prob_grad = jnp.einsum(
        "bqhd,bkhd->bhqk", grad_heads, value_heads, preferred_element_type=jnp.float32
    )
    row_dot = jnp.sum(soft * prob_grad, axis=-1, keepdims=True)
    score_grad = (soft * (prob_grad - row_dot) / math.sqrt(head_size)).astype(jnp.bfloat16)
    query_grad = jnp.einsum(
        "bhqk,bkhd->bqhd", score_grad, key_heads, preferred_element_type=jnp.float32
    )
    key_grad = jnp.einsum(
        "bhqk,bqhd->bkhd", score_grad, query_heads, preferred_element_type=jnp.float32
    )
    value_grad = jnp.einsum(
        "bhqk,bqhd->bkhd", rounded, grad_heads, preferred_element_type=jnp.float32
    )
    ext_count = key_grad.shape[1]
    joined = jnp.concatenate(
        [
            key_grad.reshape(batches, ext_count, inner_width),
            value_grad.reshape(batches, ext_count, inner_width),
        ],
        axis=-1,
    )
    return (query_grad.astype(jnp.bfloat16).reshape(batches, query_count, inner_width), joined)


def fold_cols(extended):
    left_strip = extended[:, :, :RADIUS]
    right_strip = extended[:, :, extended.shape[2] - RADIUS :]
    middle = extended[:, :, RADIUS : extended.shape[2] - RADIUS]
    from_right = shifted(left_strip, "col", -1)
    from_left = shifted(right_strip, "col", 1)
    inner_cols = middle.shape[2]
    return (
        middle
        + jnp.pad(from_left, ((0, 0), (0, 0), (0, inner_cols - RADIUS), (0, 0)))
        + jnp.pad(from_right, ((0, 0), (0, 0), (inner_cols - RADIUS, 0), (0, 0)))
    )


def fold_rows(extended):
    upper_strip = extended[:, :RADIUS]
    lower_strip = extended[:, extended.shape[1] - RADIUS :]
    middle = extended[:, RADIUS : extended.shape[1] - RADIUS]
    from_below = shifted(upper_strip, "row", -1)
    from_above = shifted(lower_strip, "row", 1)
    inner_rows = middle.shape[1]
    return (
        middle
        + jnp.pad(from_above, ((0, 0), (0, inner_rows - RADIUS), (0, 0), (0, 0)))
        + jnp.pad(from_below, ((0, 0), (inner_rows - RADIUS, 0), (0, 0), (0, 0)))
    )


def local(inputs, norm_gain, w_query, w_keyvalue, w_output, out_grad):
    batches, tile_rows, tile_cols, model_width = inputs.shape
    ext_rows = tile_rows + 2 * RADIUS
    ext_cols = tile_cols + 2 * RADIUS
    standard, spread, normed = normalize(inputs, norm_gain)
    flat_norm = normed.reshape(-1, model_width)
    row_count = lax.axis_size("row")
    packed = jnp.concatenate(
        [w_query.reshape(-1), w_keyvalue.reshape(-1), w_output.reshape(-1)]
    )
    row_bits = list(range(row_count.bit_length() - 1))
    gathered = gather_by_bits(packed, "row", row_bits[::-1]).reshape(row_count, -1)
    query_size, keyvalue_size = w_query.size, w_keyvalue.size
    full_query = gathered[:, :query_size].reshape(-1, w_query.shape[1])
    full_keyvalue = gathered[:, query_size : query_size + keyvalue_size].reshape(
        -1, w_keyvalue.shape[1]
    )
    full_output = gathered[:, query_size + keyvalue_size :].reshape(-1, w_output.shape[1])
    inner_width = full_query.shape[1]
    queries = jnp.dot(flat_norm, full_query, preferred_element_type=jnp.float32).astype(
        jnp.bfloat16
    )
    queries = queries.reshape(batches, tile_rows * tile_cols, inner_width)
    keyvalue = jnp.dot(flat_norm, full_keyvalue, preferred_element_type=jnp.float32).astype(
        jnp.bfloat16
    )
    keyvalue = keyvalue.reshape(batches, tile_rows, tile_cols, 2 * inner_width)
    keyvalue_ext = with_halo(keyvalue, (("row", 1), ("col", 2)), RADIUS)
    keyvalue_ext = keyvalue_ext.reshape(batches, ext_rows * ext_cols, 2 * inner_width)
    allowed = window_mask(
        lax.axis_index("row") * tile_rows,
        lax.axis_index("col") * tile_cols,
        tile_rows,
        tile_cols,
        tile_rows * lax.axis_size("row"),
        tile_cols * lax.axis_size("col"),
    )
    attended, soft, rounded = tile_forward(queries, keyvalue_ext, allowed)
    projected = jnp.dot(
        attended.reshape(-1, inner_width), full_output, preferred_element_type=jnp.float32
    )
    layer_out = (inputs.astype(jnp.float32) + projected.reshape(inputs.shape)).astype(jnp.bfloat16)
    flat_grad = out_grad.reshape(-1, model_width)
    inner_grad = lax.dot_general(
        flat_grad, full_output, (((1,), (1,)), ((), ())), preferred_element_type=jnp.float32
    ).astype(jnp.bfloat16)
    inner_grad = inner_grad.reshape(batches, tile_rows * tile_cols, inner_width)
    query_grad, keyvalue_part = tile_backward(queries, keyvalue_ext, soft, rounded, inner_grad)
    keyvalue_part = keyvalue_part.reshape(batches, ext_rows, ext_cols, 2 * inner_width)
    owned = fold_rows(fold_cols(keyvalue_part))
    token_grad = owned.astype(jnp.bfloat16).reshape(-1, 2 * inner_width)
    partial = lax.dot_general(
        flat_norm, token_grad, (((0,), (0,)), ((), ())), preferred_element_type=jnp.float32
    )
    col_bits = list(range(lax.axis_size("col").bit_length() - 1))
    col_part = scatter_by_bits(partial, "col", col_bits, dim=1)
    rows_part = scatter_by_bits(col_part, "row", row_bits, dim=0)
    keyvalue_grad = gather_by_bits(rows_part, "col", col_bits[::-1], dim=1)
    normed_grad = lax.dot_general(
        query_grad.reshape(-1, inner_width),
        full_query,
        (((1,), (1,)), ((), ())),
        preferred_element_type=jnp.float32,
    )
    normed_grad = normed_grad + lax.dot_general(
        token_grad, full_keyvalue, (((1,), (1,)), ((), ())), preferred_element_type=jnp.float32
    )
    gained = normed_grad.reshape(inputs.shape) * norm_gain
    in_grad = out_grad.astype(jnp.float32) + spread * (
        gained
        - jnp.mean(gained, axis=-1, keepdims=True)
        - standard * jnp.mean(gained * standard, axis=-1, keepdims=True)
    )
    return (layer_out, in_grad.astype(jnp.bfloat16), keyvalue_grad)


def solution(mesh):
    return jax.shard_map(
        local,
        mesh=mesh,
        in_specs=(
            P(None, "row", "col", None),
            P(),
            P("row", None),
            P("row", None),
            P("row", None),
            P(None, "row", "col", None),
        ),
        out_specs=(P(None, "row", "col", None), P(None, "row", "col", None), P("row", None)),
        check_vma=False,
    )
```

```python
import math

import jax
import jax.numpy as jnp
from jax import lax
from jax.sharding import PartitionSpec as P

HEADS = 8
RADIUS = 6


EPS = 1e-05
MASKED = -1e30


def shifted(value, axis, steps):
    count = lax.axis_size(axis)
    first, last = (max(0, -steps), min(count, count - steps))
    return lax.ppermute(value, axis, [(source, source + steps) for source in range(first, last)])


def with_halo(block, sides, width):
    for axis, dim in sides:
        count = lax.axis_size(axis)
        forward = [(i, i + 1) for i in range(count - 1)]
        backward = [(target, source) for source, target in forward]
        low = lax.ppermute(
            lax.slice_in_dim(block, block.shape[dim] - width, None, axis=dim), axis, forward
        )
        high = lax.ppermute(lax.slice_in_dim(block, 0, width, axis=dim), axis, backward)
        block = jnp.concatenate([low, block, high], axis=dim)
    return block


def partner_swap(value, axis, bit):
    count = lax.axis_size(axis)
    return lax.ppermute(value, axis, [(i, i ^ (1 << bit)) for i in range(count)])


def axis_bit(axis, bit):
    return (lax.axis_index(axis) // (1 << bit)) % 2


def gather_by_bits(block, axis, bits):
    levels = lax.axis_size(axis).bit_length() - 1
    mine = [axis_bit(axis, bit) for bit in range(levels)]
    zero = [0] * block.ndim
    held = jnp.zeros((2,) * levels + block.shape, block.dtype)
    held = lax.dynamic_update_slice(
        held, block.reshape((1,) * levels + block.shape), mine[::-1] + zero
    )
    done = set()
    for bit in bits:
        start = [0 if b in done else mine[b] for b in range(levels)]
        size = [2 if b in done else 1 for b in range(levels)]
        region = lax.dynamic_slice(held, start[::-1] + zero, size[::-1] + list(block.shape))
        other = partner_swap(region, axis, bit)
        start[bit] = 1 - mine[bit]
        held = lax.dynamic_update_slice(held, other, start[::-1] + zero)
        done.add(bit)
    return held.reshape((-1,) + block.shape)


def scatter_by_bits(total, axis, bits):
    levels = lax.axis_size(axis).bit_length() - 1
    held = total.reshape((2,) * levels + (total.shape[0] // 2**levels,) + total.shape[1:])
    for bit in bits:
        place = levels - 1 - bit
        own = axis_bit(axis, bit)
        keep = lax.dynamic_index_in_dim(held, own, place)
        send = lax.dynamic_index_in_dim(held, 1 - own, place)
        held = keep + partner_swap(send, axis, bit)
    return held.reshape(held.shape[levels:])


def gather_weight(shard, row_bits):
    half = shard.shape[1] // 2
    own = axis_bit("col", 0)
    piece = lax.dynamic_slice_in_dim(shard, own * half, half, axis=1)
    rows = gather_by_bits(piece, "row", row_bits)
    rows = rows.reshape(-1, half)
    held = jnp.zeros((2,) + rows.shape, rows.dtype)
    held = lax.dynamic_update_slice(held, rows[None], (own, 0, 0))
    held = lax.dynamic_update_slice(held, partner_swap(rows, "col", 0)[None], (1 - own, 0, 0))
    return jnp.concatenate([held[0], held[1]], axis=1)


def normalize(inputs, norm_gain):
    values = inputs.astype(jnp.float32)
    center = values - jnp.mean(values, axis=-1, keepdims=True)
    spread = lax.rsqrt(jnp.mean(center * center, axis=-1, keepdims=True) + EPS)
    standard = center * spread
    return (standard, spread, (standard * norm_gain).astype(jnp.bfloat16))


def window_mask(row_start, col_start, tile_rows, tile_cols, height, map_width):
    ext_rows = tile_rows + 2 * RADIUS
    ext_cols = tile_cols + 2 * RADIUS
    query_pos = jnp.arange(tile_rows * tile_cols, dtype=jnp.int32)
    query_row = query_pos // tile_cols
    query_col = query_pos % tile_cols
    ext_pos = jnp.arange(ext_rows * ext_cols, dtype=jnp.int32)
    ext_row = ext_pos // ext_cols
    ext_col = ext_pos % ext_cols
    nearby = (jnp.abs(ext_row[None, :] - RADIUS - query_row[:, None]) <= RADIUS) & (
        jnp.abs(ext_col[None, :] - RADIUS - query_col[:, None]) <= RADIUS
    )
    global_row = row_start + ext_row - RADIUS
    global_col = col_start + ext_col - RADIUS
    inside = (
        (global_row >= 0) & (global_row < height) & (global_col >= 0) & (global_col < map_width)
    )
    return nearby & inside[None, :]


def tile_forward(queries, keyvalue_ext, allowed):
    batches, query_count, inner_width = queries.shape
    head_size = inner_width // HEADS
    query_heads = queries.reshape(batches, query_count, HEADS, head_size)
    key_heads = keyvalue_ext[:, :, :inner_width].reshape(batches, -1, HEADS, head_size)
    value_heads = keyvalue_ext[:, :, inner_width:].reshape(batches, -1, HEADS, head_size)
    scores = jnp.einsum(
        "bqhd,bkhd->bhqk", query_heads, key_heads, preferred_element_type=jnp.float32
    ) / math.sqrt(head_size)
    scores = jnp.where(allowed, scores, MASKED)
    row_max = jnp.max(scores, axis=-1, keepdims=True)
    exponent = jnp.exp(scores - row_max)
    soft = exponent / jnp.sum(exponent, axis=-1, keepdims=True)
    rounded = soft.astype(jnp.bfloat16)
    attended = jnp.einsum(
        "bhqk,bkhd->bqhd", rounded, value_heads, preferred_element_type=jnp.float32
    )
    return (attended.astype(jnp.bfloat16).reshape(batches, query_count, inner_width), soft, rounded)


def tile_backward(queries, keyvalue_ext, soft, rounded, inner_grad):
    batches, query_count, inner_width = queries.shape
    head_size = inner_width // HEADS
    query_heads = queries.reshape(batches, query_count, HEADS, head_size)
    key_heads = keyvalue_ext[:, :, :inner_width].reshape(batches, -1, HEADS, head_size)
    value_heads = keyvalue_ext[:, :, inner_width:].reshape(batches, -1, HEADS, head_size)
    grad_heads = inner_grad.reshape(batches, query_count, HEADS, head_size)
    prob_grad = jnp.einsum(
        "bqhd,bkhd->bhqk", grad_heads, value_heads, preferred_element_type=jnp.float32
    )
    row_dot = jnp.sum(soft * prob_grad, axis=-1, keepdims=True)
    score_grad = (soft * (prob_grad - row_dot) / math.sqrt(head_size)).astype(jnp.bfloat16)
    query_grad = jnp.einsum(
        "bhqk,bkhd->bqhd", score_grad, key_heads, preferred_element_type=jnp.float32
    )
    key_grad = jnp.einsum(
        "bhqk,bqhd->bkhd", score_grad, query_heads, preferred_element_type=jnp.float32
    )
    value_grad = jnp.einsum(
        "bhqk,bqhd->bkhd", rounded, grad_heads, preferred_element_type=jnp.float32
    )
    ext_count = key_grad.shape[1]
    joined = jnp.concatenate(
        [
            key_grad.reshape(batches, ext_count, inner_width),
            value_grad.reshape(batches, ext_count, inner_width),
        ],
        axis=-1,
    )
    return (query_grad.astype(jnp.bfloat16).reshape(batches, query_count, inner_width), joined)


def fold_cols(extended):
    left_strip = extended[:, :, :RADIUS]
    right_strip = extended[:, :, extended.shape[2] - RADIUS :]
    middle = extended[:, :, RADIUS : extended.shape[2] - RADIUS]
    from_right = shifted(left_strip, "col", -1)
    from_left = shifted(right_strip, "col", 1)
    inner_cols = middle.shape[2]
    return (
        middle
        + jnp.pad(from_left, ((0, 0), (0, 0), (0, inner_cols - RADIUS), (0, 0)))
        + jnp.pad(from_right, ((0, 0), (0, 0), (inner_cols - RADIUS, 0), (0, 0)))
    )


def fold_rows(extended):
    upper_strip = extended[:, :RADIUS]
    lower_strip = extended[:, extended.shape[1] - RADIUS :]
    middle = extended[:, RADIUS : extended.shape[1] - RADIUS]
    from_below = shifted(upper_strip, "row", -1)
    from_above = shifted(lower_strip, "row", 1)
    inner_rows = middle.shape[1]
    return (
        middle
        + jnp.pad(from_above, ((0, 0), (0, inner_rows - RADIUS), (0, 0), (0, 0)))
        + jnp.pad(from_below, ((0, 0), (inner_rows - RADIUS, 0), (0, 0), (0, 0)))
    )


def local(inputs, norm_gain, w_query, w_keyvalue, w_output, out_grad):
    batches, tile_rows, tile_cols, model_width = inputs.shape
    ext_rows = tile_rows + 2 * RADIUS
    ext_cols = tile_cols + 2 * RADIUS
    standard, spread, normed = normalize(inputs, norm_gain)
    flat_norm = normed.reshape(-1, model_width)
    row_bits = list(range(lax.axis_size("row").bit_length() - 1))
    full_keyvalue = gather_weight(w_keyvalue, row_bits[::-1])
    full_query = gather_weight(w_query, row_bits[::-1])
    full_output = gather_weight(w_output, row_bits[::-1])
    inner_width = full_query.shape[1]
    queries = jnp.dot(flat_norm, full_query, preferred_element_type=jnp.float32).astype(
        jnp.bfloat16
    )
    queries = queries.reshape(batches, tile_rows * tile_cols, inner_width)
    keyvalue = jnp.dot(flat_norm, full_keyvalue, preferred_element_type=jnp.float32).astype(
        jnp.bfloat16
    )
    keyvalue = keyvalue.reshape(batches, tile_rows, tile_cols, 2 * inner_width)
    keyvalue_ext = with_halo(keyvalue, (("row", 1), ("col", 2)), RADIUS)
    keyvalue_ext = keyvalue_ext.reshape(batches, ext_rows * ext_cols, 2 * inner_width)
    allowed = window_mask(
        lax.axis_index("row") * tile_rows,
        lax.axis_index("col") * tile_cols,
        tile_rows,
        tile_cols,
        tile_rows * lax.axis_size("row"),
        tile_cols * lax.axis_size("col"),
    )
    attended, soft, rounded = tile_forward(queries, keyvalue_ext, allowed)
    projected = jnp.dot(
        attended.reshape(-1, inner_width), full_output, preferred_element_type=jnp.float32
    )
    layer_out = (inputs.astype(jnp.float32) + projected.reshape(inputs.shape)).astype(jnp.bfloat16)
    flat_grad = out_grad.reshape(-1, model_width)
    inner_grad = lax.dot_general(
        flat_grad, full_output, (((1,), (1,)), ((), ())), preferred_element_type=jnp.float32
    ).astype(jnp.bfloat16)
    inner_grad = inner_grad.reshape(batches, tile_rows * tile_cols, inner_width)
    query_grad, keyvalue_part = tile_backward(queries, keyvalue_ext, soft, rounded, inner_grad)
    keyvalue_part = keyvalue_part.reshape(batches, ext_rows, ext_cols, 2 * inner_width)
    owned = fold_rows(fold_cols(keyvalue_part))
    token_grad = owned.astype(jnp.bfloat16).reshape(-1, 2 * inner_width)
    row_count, col_count = lax.axis_size("row"), lax.axis_size("col")
    col_bits = list(range(col_count.bit_length() - 1))
    feature_part = model_width // row_count
    column_part = token_grad.shape[1] // col_count
    partial = jnp.einsum(
        "tra,tcb->crab",
        flat_norm.reshape(-1, row_count, feature_part),
        token_grad.reshape(-1, col_count, column_part),
        preferred_element_type=jnp.float32,
    )
    col_order = [0] + col_bits[2:3] + col_bits[1:2] + col_bits[3:]
    col_part = scatter_by_bits(partial, "col", col_order)[0]
    rows_part = scatter_by_bits(col_part, "row", row_bits)[0]
    keyvalue_grad = gather_by_bits(rows_part, "col", col_bits[::-1])
    keyvalue_grad = keyvalue_grad.transpose(1, 0, 2).reshape(feature_part, -1)
    normed_grad = lax.dot_general(
        query_grad.reshape(-1, inner_width),
        full_query,
        (((1,), (1,)), ((), ())),
        preferred_element_type=jnp.float32,
    )
    normed_grad = normed_grad + lax.dot_general(
        token_grad, full_keyvalue, (((1,), (1,)), ((), ())), preferred_element_type=jnp.float32
    )
    gained = normed_grad.reshape(inputs.shape) * norm_gain
    in_grad = out_grad.astype(jnp.float32) + spread * (
        gained
        - jnp.mean(gained, axis=-1, keepdims=True)
        - standard * jnp.mean(gained * standard, axis=-1, keepdims=True)
    )
    return (layer_out, in_grad.astype(jnp.bfloat16), keyvalue_grad)


def solution(mesh):
    return jax.shard_map(
        local,
        mesh=mesh,
        in_specs=(
            P(None, "row", "col", None),
            P(),
            P("row", None),
            P("row", None),
            P("row", None),
            P(None, "row", "col", None),
        ),
        out_specs=(P(None, "row", "col", None), P(None, "row", "col", None), P("row", None)),
        check_vma=False,
    )
```

```python
import math

import jax
import jax.numpy as jnp
from jax import lax
from jax.sharding import PartitionSpec as P

HEADS = 8
RADIUS = 6


EPS = 1e-05
MASKED = -1e30


def shifted(value, axis, steps):
    count = lax.axis_size(axis)
    first, last = (max(0, -steps), min(count, count - steps))
    return lax.ppermute(value, axis, [(source, source + steps) for source in range(first, last)])


def with_halo(block, sides, width):
    for axis, dim in sides:
        count = lax.axis_size(axis)
        forward = [(i, i + 1) for i in range(count - 1)]
        backward = [(target, source) for source, target in forward]
        low = lax.ppermute(
            lax.slice_in_dim(block, block.shape[dim] - width, None, axis=dim), axis, forward
        )
        high = lax.ppermute(lax.slice_in_dim(block, 0, width, axis=dim), axis, backward)
        block = jnp.concatenate([low, block, high], axis=dim)
    return block


def partner_swap(value, axis, mask):
    count = lax.axis_size(axis)
    return lax.ppermute(value, axis, [(i, i ^ mask) for i in range(count)])


def axis_bit(axis, bit):
    return (lax.axis_index(axis) // (1 << bit)) % 2


def flips(group):
    for code in range(1, 1 << len(group)):
        yield [(code >> k) % 2 for k in range(len(group))]


def gather_by_bits(block, axis, groups):
    levels = lax.axis_size(axis).bit_length() - 1
    mine = [axis_bit(axis, bit) for bit in range(levels)]
    zero = [0] * block.ndim
    held = jnp.zeros((2,) * levels + block.shape, block.dtype)
    held = lax.dynamic_update_slice(
        held, block.reshape((1,) * levels + block.shape), mine[::-1] + zero
    )
    done = set()
    for group in groups:
        start = [0 if b in done else mine[b] for b in range(levels)]
        size = [2 if b in done else 1 for b in range(levels)]
        region = lax.dynamic_slice(held, start[::-1] + zero, size[::-1] + list(block.shape))
        arrived = []
        for flip in flips(group):
            mask = sum(f << b for f, b in zip(flip, group))
            place = list(start)
            for f, b in zip(flip, group):
                place[b] = (mine[b] + f) % 2
            arrived.append((partner_swap(region, axis, mask), place))
        for other, place in arrived:
            held = lax.dynamic_update_slice(held, other, place[::-1] + zero)
        done.update(group)
    return held.reshape((-1,) + block.shape)


def scatter_by_bits(total, axis, groups):
    levels = lax.axis_size(axis).bit_length() - 1
    mine = [axis_bit(axis, bit) for bit in range(levels)]
    held = total.reshape((2,) * levels + (total.shape[0] // 2**levels,) + total.shape[1:])
    rest = [0] * (held.ndim - levels)
    for group in groups:
        size = [1 if b in group else held.shape[levels - 1 - b] for b in range(levels)]
        size = size[::-1] + list(held.shape[levels:])
        own = [mine[b] if b in group else 0 for b in range(levels)]
        summed = lax.dynamic_slice(held, own[::-1] + rest, size)
        for flip in flips(group):
            mask = sum(f << b for f, b in zip(flip, group))
            place = list(own)
            for f, b in zip(flip, group):
                place[b] = (mine[b] + f) % 2
            send = lax.dynamic_slice(held, place[::-1] + rest, size)
            summed = summed + partner_swap(send, axis, mask)
        held = summed
    return held.reshape(held.shape[levels:])


def gather_weight(shard, row_bits):
    half = shard.shape[1] // 2
    own = axis_bit("col", 0)
    piece = lax.dynamic_slice_in_dim(shard, own * half, half, axis=1)
    rows = gather_by_bits(piece, "row", row_bits)
    rows = rows.reshape(-1, half)
    held = jnp.zeros((2,) + rows.shape, rows.dtype)
    held = lax.dynamic_update_slice(held, rows[None], (own, 0, 0))
    held = lax.dynamic_update_slice(held, partner_swap(rows, "col", 1)[None], (1 - own, 0, 0))
    return jnp.concatenate([held[0], held[1]], axis=1)


def normalize(inputs, norm_gain):
    values = inputs.astype(jnp.float32)
    center = values - jnp.mean(values, axis=-1, keepdims=True)
    spread = lax.rsqrt(jnp.mean(center * center, axis=-1, keepdims=True) + EPS)
    standard = center * spread
    return (standard, spread, (standard * norm_gain).astype(jnp.bfloat16))


def window_mask(row_start, col_start, tile_rows, tile_cols, height, map_width):
    ext_rows = tile_rows + 2 * RADIUS
    ext_cols = tile_cols + 2 * RADIUS
    query_pos = jnp.arange(tile_rows * tile_cols, dtype=jnp.int32)
    query_row = query_pos // tile_cols
    query_col = query_pos % tile_cols
    ext_pos = jnp.arange(ext_rows * ext_cols, dtype=jnp.int32)
    ext_row = ext_pos // ext_cols
    ext_col = ext_pos % ext_cols
    nearby = (jnp.abs(ext_row[None, :] - RADIUS - query_row[:, None]) <= RADIUS) & (
        jnp.abs(ext_col[None, :] - RADIUS - query_col[:, None]) <= RADIUS
    )
    global_row = row_start + ext_row - RADIUS
    global_col = col_start + ext_col - RADIUS
    inside = (
        (global_row >= 0) & (global_row < height) & (global_col >= 0) & (global_col < map_width)
    )
    return nearby & inside[None, :]


def tile_forward(queries, keyvalue_ext, allowed):
    batches, query_count, inner_width = queries.shape
    head_size = inner_width // HEADS
    query_heads = queries.reshape(batches, query_count, HEADS, head_size)
    key_heads = keyvalue_ext[:, :, :inner_width].reshape(batches, -1, HEADS, head_size)
    value_heads = keyvalue_ext[:, :, inner_width:].reshape(batches, -1, HEADS, head_size)
    scores = jnp.einsum(
        "bqhd,bkhd->bhqk", query_heads, key_heads, preferred_element_type=jnp.float32
    ) / math.sqrt(head_size)
    scores = jnp.where(allowed, scores, MASKED)
    row_max = jnp.max(scores, axis=-1, keepdims=True)
    exponent = jnp.exp(scores - row_max)
    soft = exponent / jnp.sum(exponent, axis=-1, keepdims=True)
    rounded = soft.astype(jnp.bfloat16)
    attended = jnp.einsum(
        "bhqk,bkhd->bqhd", rounded, value_heads, preferred_element_type=jnp.float32
    )
    return (attended.astype(jnp.bfloat16).reshape(batches, query_count, inner_width), soft, rounded)


def tile_backward(queries, keyvalue_ext, soft, rounded, inner_grad):
    batches, query_count, inner_width = queries.shape
    head_size = inner_width // HEADS
    query_heads = queries.reshape(batches, query_count, HEADS, head_size)
    key_heads = keyvalue_ext[:, :, :inner_width].reshape(batches, -1, HEADS, head_size)
    value_heads = keyvalue_ext[:, :, inner_width:].reshape(batches, -1, HEADS, head_size)
    grad_heads = inner_grad.reshape(batches, query_count, HEADS, head_size)
    prob_grad = jnp.einsum(
        "bqhd,bkhd->bhqk", grad_heads, value_heads, preferred_element_type=jnp.float32
    )
    row_dot = jnp.sum(soft * prob_grad, axis=-1, keepdims=True)
    score_grad = (soft * (prob_grad - row_dot) / math.sqrt(head_size)).astype(jnp.bfloat16)
    query_grad = jnp.einsum(
        "bhqk,bkhd->bqhd", score_grad, key_heads, preferred_element_type=jnp.float32
    )
    key_grad = jnp.einsum(
        "bhqk,bqhd->bkhd", score_grad, query_heads, preferred_element_type=jnp.float32
    )
    value_grad = jnp.einsum(
        "bhqk,bqhd->bkhd", rounded, grad_heads, preferred_element_type=jnp.float32
    )
    ext_count = key_grad.shape[1]
    joined = jnp.concatenate(
        [
            key_grad.reshape(batches, ext_count, inner_width),
            value_grad.reshape(batches, ext_count, inner_width),
        ],
        axis=-1,
    )
    return (query_grad.astype(jnp.bfloat16).reshape(batches, query_count, inner_width), joined)


def fold_cols(extended):
    left_strip = extended[:, :, :RADIUS]
    right_strip = extended[:, :, extended.shape[2] - RADIUS :]
    middle = extended[:, :, RADIUS : extended.shape[2] - RADIUS]
    from_right = shifted(left_strip, "col", -1)
    from_left = shifted(right_strip, "col", 1)
    inner_cols = middle.shape[2]
    return (
        middle
        + jnp.pad(from_left, ((0, 0), (0, 0), (0, inner_cols - RADIUS), (0, 0)))
        + jnp.pad(from_right, ((0, 0), (0, 0), (inner_cols - RADIUS, 0), (0, 0)))
    )


def fold_rows(extended):
    upper_strip = extended[:, :RADIUS]
    lower_strip = extended[:, extended.shape[1] - RADIUS :]
    middle = extended[:, RADIUS : extended.shape[1] - RADIUS]
    from_below = shifted(upper_strip, "row", -1)
    from_above = shifted(lower_strip, "row", 1)
    inner_rows = middle.shape[1]
    return (
        middle
        + jnp.pad(from_above, ((0, 0), (0, inner_rows - RADIUS), (0, 0), (0, 0)))
        + jnp.pad(from_below, ((0, 0), (inner_rows - RADIUS, 0), (0, 0), (0, 0)))
    )


def local(inputs, norm_gain, w_query, w_keyvalue, w_output, out_grad):
    batches, tile_rows, tile_cols, model_width = inputs.shape
    ext_rows = tile_rows + 2 * RADIUS
    ext_cols = tile_cols + 2 * RADIUS
    standard, spread, normed = normalize(inputs, norm_gain)
    flat_norm = normed.reshape(-1, model_width)
    row_levels = lax.axis_size("row").bit_length() - 1
    row_groups = [list(range(b, min(b + 2, row_levels))) for b in range(0, row_levels, 2)]
    full_keyvalue = gather_weight(w_keyvalue, row_groups[::-1])
    full_query = gather_weight(w_query, row_groups[::-1])
    full_output = gather_weight(w_output, row_groups[::-1])
    inner_width = full_query.shape[1]
    queries = jnp.dot(flat_norm, full_query, preferred_element_type=jnp.float32).astype(
        jnp.bfloat16
    )
    queries = queries.reshape(batches, tile_rows * tile_cols, inner_width)
    keyvalue = jnp.dot(flat_norm, full_keyvalue, preferred_element_type=jnp.float32).astype(
        jnp.bfloat16
    )
    keyvalue = keyvalue.reshape(batches, tile_rows, tile_cols, 2 * inner_width)
    keyvalue_ext = with_halo(keyvalue, (("row", 1), ("col", 2)), RADIUS)
    keyvalue_ext = keyvalue_ext.reshape(batches, ext_rows * ext_cols, 2 * inner_width)
    allowed = window_mask(
        lax.axis_index("row") * tile_rows,
        lax.axis_index("col") * tile_cols,
        tile_rows,
        tile_cols,
        tile_rows * lax.axis_size("row"),
        tile_cols * lax.axis_size("col"),
    )
    attended, soft, rounded = tile_forward(queries, keyvalue_ext, allowed)
    projected = jnp.dot(
        attended.reshape(-1, inner_width), full_output, preferred_element_type=jnp.float32
    )
    layer_out = (inputs.astype(jnp.float32) + projected.reshape(inputs.shape)).astype(jnp.bfloat16)
    flat_grad = out_grad.reshape(-1, model_width)
    inner_grad = lax.dot_general(
        flat_grad, full_output, (((1,), (1,)), ((), ())), preferred_element_type=jnp.float32
    ).astype(jnp.bfloat16)
    inner_grad = inner_grad.reshape(batches, tile_rows * tile_cols, inner_width)
    query_grad, keyvalue_part = tile_backward(queries, keyvalue_ext, soft, rounded, inner_grad)
    keyvalue_part = keyvalue_part.reshape(batches, ext_rows, ext_cols, 2 * inner_width)
    owned = fold_rows(fold_cols(keyvalue_part))
    token_grad = owned.astype(jnp.bfloat16).reshape(-1, 2 * inner_width)
    row_count, col_count = lax.axis_size("row"), lax.axis_size("col")
    col_levels = col_count.bit_length() - 1
    col_groups = [[0, 2], [1, 3]] if col_levels == 4 else [[b] for b in range(col_levels)]
    feature_part = model_width // row_count
    column_part = token_grad.shape[1] // col_count
    partial = jnp.einsum(
        "tra,tcb->crab",
        flat_norm.reshape(-1, row_count, feature_part),
        token_grad.reshape(-1, col_count, column_part),
        preferred_element_type=jnp.float32,
    )
    col_part = scatter_by_bits(partial, "col", col_groups)[0]
    rows_part = scatter_by_bits(col_part, "row", row_groups)[0]
    keyvalue_grad = gather_by_bits(rows_part, "col", col_groups[::-1])
    keyvalue_grad = keyvalue_grad.transpose(1, 0, 2).reshape(feature_part, -1)
    normed_grad = lax.dot_general(
        query_grad.reshape(-1, inner_width),
        full_query,
        (((1,), (1,)), ((), ())),
        preferred_element_type=jnp.float32,
    )
    normed_grad = normed_grad + lax.dot_general(
        token_grad, full_keyvalue, (((1,), (1,)), ((), ())), preferred_element_type=jnp.float32
    )
    gained = normed_grad.reshape(inputs.shape) * norm_gain
    in_grad = out_grad.astype(jnp.float32) + spread * (
        gained
        - jnp.mean(gained, axis=-1, keepdims=True)
        - standard * jnp.mean(gained * standard, axis=-1, keepdims=True)
    )
    return (layer_out, in_grad.astype(jnp.bfloat16), keyvalue_grad)


def solution(mesh):
    return jax.shard_map(
        local,
        mesh=mesh,
        in_specs=(
            P(None, "row", "col", None),
            P(),
            P("row", None),
            P("row", None),
            P("row", None),
            P(None, "row", "col", None),
        ),
        out_specs=(P(None, "row", "col", None), P(None, "row", "col", None), P("row", None)),
        check_vma=False,
    )
```

```python
import math

import jax
import jax.numpy as jnp
from jax import lax
from jax.sharding import PartitionSpec as P

HEADS = 8
RADIUS = 6


EPS = 1e-05
MASKED = -1e30


def shifted(value, axis, steps):
    count = lax.axis_size(axis)
    first, last = (max(0, -steps), min(count, count - steps))
    return lax.ppermute(value, axis, [(source, source + steps) for source in range(first, last)])


def with_halo(block, sides, width):
    for axis, dim in sides:
        count = lax.axis_size(axis)
        forward = [(i, i + 1) for i in range(count - 1)]
        backward = [(target, source) for source, target in forward]
        low = lax.ppermute(
            lax.slice_in_dim(block, block.shape[dim] - width, None, axis=dim), axis, forward
        )
        high = lax.ppermute(lax.slice_in_dim(block, 0, width, axis=dim), axis, backward)
        block = jnp.concatenate([low, block, high], axis=dim)
    return block


def partner_swap(value, axis, mask):
    count = lax.axis_size(axis)
    return lax.ppermute(value, axis, [(i, i ^ mask) for i in range(count)])


def axis_bit(axis, bit):
    return (lax.axis_index(axis) // (1 << bit)) % 2


def flips(group):
    for code in range(1, 1 << len(group)):
        yield [(code >> k) % 2 for k in range(len(group))]


def gather_by_bits(block, axis, groups):
    levels = lax.axis_size(axis).bit_length() - 1
    mine = [axis_bit(axis, bit) for bit in range(levels)]
    zero = [0] * block.ndim
    held = jnp.zeros((2,) * levels + block.shape, block.dtype)
    held = lax.dynamic_update_slice(
        held, block.reshape((1,) * levels + block.shape), mine[::-1] + zero
    )
    done = set()
    for group in groups:
        start = [0 if b in done else mine[b] for b in range(levels)]
        size = [2 if b in done else 1 for b in range(levels)]
        region = lax.dynamic_slice(held, start[::-1] + zero, size[::-1] + list(block.shape))
        arrived = []
        for flip in flips(group):
            mask = sum(f << b for f, b in zip(flip, group))
            place = list(start)
            for f, b in zip(flip, group):
                place[b] = (mine[b] + f) % 2
            arrived.append((partner_swap(region, axis, mask), place))
        for other, place in arrived:
            held = lax.dynamic_update_slice(held, other, place[::-1] + zero)
        done.update(group)
    return held.reshape((-1,) + block.shape)


def scatter_by_bits(total, axis, groups):
    levels = lax.axis_size(axis).bit_length() - 1
    mine = [axis_bit(axis, bit) for bit in range(levels)]
    held = total.reshape((2,) * levels + (total.shape[0] // 2**levels,) + total.shape[1:])
    rest = [0] * (held.ndim - levels)
    for group in groups:
        size = [1 if b in group else held.shape[levels - 1 - b] for b in range(levels)]
        size = size[::-1] + list(held.shape[levels:])
        own = [mine[b] if b in group else 0 for b in range(levels)]
        summed = lax.dynamic_slice(held, own[::-1] + rest, size)
        for flip in flips(group):
            mask = sum(f << b for f, b in zip(flip, group))
            place = list(own)
            for f, b in zip(flip, group):
                place[b] = (mine[b] + f) % 2
            send = lax.dynamic_slice(held, place[::-1] + rest, size)
            summed = summed + partner_swap(send, axis, mask)
        held = summed
    return held.reshape(held.shape[levels:])


def gather_weights(w_query, w_keyvalue, w_output, row_groups):
    rows, width = w_query.shape
    kv_pack = w_keyvalue.reshape(rows, 2, width).transpose(1, 0, 2).reshape(2 * rows, width)
    out_rows = w_output.shape[0]
    out_pack = w_output.reshape(out_rows, 2, width).transpose(1, 0, 2).reshape(2 * out_rows, width)
    qo_pack = jnp.concatenate([w_query, out_pack], axis=0)
    own = axis_bit("col", 0)
    packed = jnp.where(own == 0, kv_pack, qo_pack)
    fetched = gather_by_bits(packed, "row", row_groups)
    held = jnp.zeros((2,) + fetched.shape, fetched.dtype)
    held = lax.dynamic_update_slice(held, fetched[None], (own, 0, 0, 0))
    held = lax.dynamic_update_slice(held, partner_swap(fetched, "col", 1)[None], (1 - own, 0, 0, 0))
    count = fetched.shape[0]
    kv = held[0].reshape(count, 2, rows, width).transpose(0, 2, 1, 3).reshape(count * rows, 2 * width)
    query = held[1, :, :rows].reshape(count * rows, width)
    output = held[1, :, rows:].reshape(count, 2, out_rows, width).transpose(0, 2, 1, 3)
    return query, kv, output.reshape(count * out_rows, 2 * width)


def normalize(inputs, norm_gain):
    values = inputs.astype(jnp.float32)
    center = values - jnp.mean(values, axis=-1, keepdims=True)
    spread = lax.rsqrt(jnp.mean(center * center, axis=-1, keepdims=True) + EPS)
    standard = center * spread
    return (standard, spread, (standard * norm_gain).astype(jnp.bfloat16))


def window_mask(row_start, col_start, tile_rows, tile_cols, height, map_width):
    ext_rows = tile_rows + 2 * RADIUS
    ext_cols = tile_cols + 2 * RADIUS
    query_pos = jnp.arange(tile_rows * tile_cols, dtype=jnp.int32)
    query_row = query_pos // tile_cols
    query_col = query_pos % tile_cols
    ext_pos = jnp.arange(ext_rows * ext_cols, dtype=jnp.int32)
    ext_row = ext_pos // ext_cols
    ext_col = ext_pos % ext_cols
    nearby = (jnp.abs(ext_row[None, :] - RADIUS - query_row[:, None]) <= RADIUS) & (
        jnp.abs(ext_col[None, :] - RADIUS - query_col[:, None]) <= RADIUS
    )
    global_row = row_start + ext_row - RADIUS
    global_col = col_start + ext_col - RADIUS
    inside = (
        (global_row >= 0) & (global_row < height) & (global_col >= 0) & (global_col < map_width)
    )
    return nearby & inside[None, :]


def tile_forward(queries, keyvalue_ext, allowed):
    batches, query_count, inner_width = queries.shape
    head_size = inner_width // HEADS
    query_heads = queries.reshape(batches, query_count, HEADS, head_size)
    key_heads = keyvalue_ext[:, :, :inner_width].reshape(batches, -1, HEADS, head_size)
    value_heads = keyvalue_ext[:, :, inner_width:].reshape(batches, -1, HEADS, head_size)
    scores = jnp.einsum(
        "bqhd,bkhd->bhqk", query_heads, key_heads, preferred_element_type=jnp.float32
    ) / math.sqrt(head_size)
    scores = jnp.where(allowed, scores, MASKED)
    row_max = jnp.max(scores, axis=-1, keepdims=True)
    exponent = jnp.exp(scores - row_max)
    soft = exponent / jnp.sum(exponent, axis=-1, keepdims=True)
    rounded = soft.astype(jnp.bfloat16)
    attended = jnp.einsum(
        "bhqk,bkhd->bqhd", rounded, value_heads, preferred_element_type=jnp.float32
    )
    return (attended.astype(jnp.bfloat16).reshape(batches, query_count, inner_width), soft, rounded)


def tile_backward(queries, keyvalue_ext, soft, rounded, inner_grad):
    batches, query_count, inner_width = queries.shape
    head_size = inner_width // HEADS
    query_heads = queries.reshape(batches, query_count, HEADS, head_size)
    key_heads = keyvalue_ext[:, :, :inner_width].reshape(batches, -1, HEADS, head_size)
    value_heads = keyvalue_ext[:, :, inner_width:].reshape(batches, -1, HEADS, head_size)
    grad_heads = inner_grad.reshape(batches, query_count, HEADS, head_size)
    prob_grad = jnp.einsum(
        "bqhd,bkhd->bhqk", grad_heads, value_heads, preferred_element_type=jnp.float32
    )
    row_dot = jnp.sum(soft * prob_grad, axis=-1, keepdims=True)
    score_grad = (soft * (prob_grad - row_dot) / math.sqrt(head_size)).astype(jnp.bfloat16)
    query_grad = jnp.einsum(
        "bhqk,bkhd->bqhd", score_grad, key_heads, preferred_element_type=jnp.float32
    )
    key_grad = jnp.einsum(
        "bhqk,bqhd->bkhd", score_grad, query_heads, preferred_element_type=jnp.float32
    )
    value_grad = jnp.einsum(
        "bhqk,bqhd->bkhd", rounded, grad_heads, preferred_element_type=jnp.float32
    )
    ext_count = key_grad.shape[1]
    joined = jnp.concatenate(
        [
            key_grad.reshape(batches, ext_count, inner_width),
            value_grad.reshape(batches, ext_count, inner_width),
        ],
        axis=-1,
    )
    return (query_grad.astype(jnp.bfloat16).reshape(batches, query_count, inner_width), joined)


def fold_cols(extended):
    left_strip = extended[:, :, :RADIUS]
    right_strip = extended[:, :, extended.shape[2] - RADIUS :]
    middle = extended[:, :, RADIUS : extended.shape[2] - RADIUS]
    from_right = shifted(left_strip, "col", -1)
    from_left = shifted(right_strip, "col", 1)
    inner_cols = middle.shape[2]
    return (
        middle
        + jnp.pad(from_left, ((0, 0), (0, 0), (0, inner_cols - RADIUS), (0, 0)))
        + jnp.pad(from_right, ((0, 0), (0, 0), (inner_cols - RADIUS, 0), (0, 0)))
    )


def fold_rows(extended):
    upper_strip = extended[:, :RADIUS]
    lower_strip = extended[:, extended.shape[1] - RADIUS :]
    middle = extended[:, RADIUS : extended.shape[1] - RADIUS]
    from_below = shifted(upper_strip, "row", -1)
    from_above = shifted(lower_strip, "row", 1)
    inner_rows = middle.shape[1]
    return (
        middle
        + jnp.pad(from_above, ((0, 0), (0, inner_rows - RADIUS), (0, 0), (0, 0)))
        + jnp.pad(from_below, ((0, 0), (inner_rows - RADIUS, 0), (0, 0), (0, 0)))
    )


def local(inputs, norm_gain, w_query, w_keyvalue, w_output, out_grad):
    batches, tile_rows, tile_cols, model_width = inputs.shape
    ext_rows = tile_rows + 2 * RADIUS
    ext_cols = tile_cols + 2 * RADIUS
    standard, spread, normed = normalize(inputs, norm_gain)
    flat_norm = normed.reshape(-1, model_width)
    row_levels = lax.axis_size("row").bit_length() - 1
    row_groups = [[b] for b in range(row_levels)]
    full_query, full_keyvalue, full_output = gather_weights(
        w_query, w_keyvalue, w_output, row_groups[::-1]
    )
    inner_width = full_query.shape[1]
    queries = jnp.dot(flat_norm, full_query, preferred_element_type=jnp.float32).astype(
        jnp.bfloat16
    )
    queries = queries.reshape(batches, tile_rows * tile_cols, inner_width)
    keyvalue = jnp.dot(flat_norm, full_keyvalue, preferred_element_type=jnp.float32).astype(
        jnp.bfloat16
    )
    keyvalue = keyvalue.reshape(batches, tile_rows, tile_cols, 2 * inner_width)
    keyvalue_ext = with_halo(keyvalue, (("row", 1), ("col", 2)), RADIUS)
    keyvalue_ext = keyvalue_ext.reshape(batches, ext_rows * ext_cols, 2 * inner_width)
    allowed = window_mask(
        lax.axis_index("row") * tile_rows,
        lax.axis_index("col") * tile_cols,
        tile_rows,
        tile_cols,
        tile_rows * lax.axis_size("row"),
        tile_cols * lax.axis_size("col"),
    )
    attended, soft, rounded = tile_forward(queries, keyvalue_ext, allowed)
    projected = jnp.dot(
        attended.reshape(-1, inner_width), full_output, preferred_element_type=jnp.float32
    )
    layer_out = (inputs.astype(jnp.float32) + projected.reshape(inputs.shape)).astype(jnp.bfloat16)
    flat_grad = out_grad.reshape(-1, model_width)
    inner_grad = lax.dot_general(
        flat_grad, full_output, (((1,), (1,)), ((), ())), preferred_element_type=jnp.float32
    ).astype(jnp.bfloat16)
    inner_grad = inner_grad.reshape(batches, tile_rows * tile_cols, inner_width)
    query_grad, keyvalue_part = tile_backward(queries, keyvalue_ext, soft, rounded, inner_grad)
    keyvalue_part = keyvalue_part.reshape(batches, ext_rows, ext_cols, 2 * inner_width)
    owned = fold_rows(fold_cols(keyvalue_part))
    token_grad = owned.astype(jnp.bfloat16).reshape(-1, 2 * inner_width)
    row_count, col_count = lax.axis_size("row"), lax.axis_size("col")
    col_levels = col_count.bit_length() - 1
    col_groups = [[0], [2], [1], [3]] if col_levels == 4 else [[b] for b in range(col_levels)]
    feature_part = model_width // row_count
    column_part = token_grad.shape[1] // col_count
    partial = lax.dot_general(
        token_grad, flat_norm, (((0,), (0,)), ((), ())), preferred_element_type=jnp.float32
    )
    partial = partial.reshape(col_count, column_part, model_width)
    col_part = scatter_by_bits(partial, "col", col_groups)[0]
    lanes = 256
    by_rows = col_part.reshape(column_part, row_count, feature_part).transpose(1, 2, 0)
    by_rows = by_rows.reshape(row_count, feature_part * column_part // lanes, lanes)
    rows_part = scatter_by_bits(by_rows, "row", row_groups)[0]
    keyvalue_grad = gather_by_bits(rows_part, "col", col_groups[::-1])
    keyvalue_grad = keyvalue_grad.reshape(col_count, feature_part, column_part)
    keyvalue_grad = keyvalue_grad.transpose(1, 0, 2).reshape(feature_part, -1)
    normed_grad = lax.dot_general(
        query_grad.reshape(-1, inner_width),
        full_query,
        (((1,), (1,)), ((), ())),
        preferred_element_type=jnp.float32,
    )
    normed_grad = normed_grad + lax.dot_general(
        token_grad, full_keyvalue, (((1,), (1,)), ((), ())), preferred_element_type=jnp.float32
    )
    gained = normed_grad.reshape(inputs.shape) * norm_gain
    in_grad = out_grad.astype(jnp.float32) + spread * (
        gained
        - jnp.mean(gained, axis=-1, keepdims=True)
        - standard * jnp.mean(gained * standard, axis=-1, keepdims=True)
    )
    return (layer_out, in_grad.astype(jnp.bfloat16), keyvalue_grad)


def solution(mesh):
    return jax.shard_map(
        local,
        mesh=mesh,
        in_specs=(
            P(None, "row", "col", None),
            P(),
            P("row", None),
            P("row", None),
            P("row", None),
            P(None, "row", "col", None),
        ),
        out_specs=(P(None, "row", "col", None), P(None, "row", "col", None), P("row", None)),
        check_vma=False,
    )
```

```python
import math

import jax
import jax.numpy as jnp
from jax import lax
from jax.sharding import PartitionSpec as P

HEADS = 8
RADIUS = 6


EPS = 1e-05
MASKED = -1e30


def shifted(value, axis, steps):
    count = lax.axis_size(axis)
    first, last = (max(0, -steps), min(count, count - steps))
    return lax.ppermute(value, axis, [(source, source + steps) for source in range(first, last)])


def with_halo(block, sides, width):
    for axis, dim in sides:
        count = lax.axis_size(axis)
        forward = [(i, i + 1) for i in range(count - 1)]
        backward = [(target, source) for source, target in forward]
        low = lax.ppermute(
            lax.slice_in_dim(block, block.shape[dim] - width, None, axis=dim), axis, forward
        )
        high = lax.ppermute(lax.slice_in_dim(block, 0, width, axis=dim), axis, backward)
        block = jnp.concatenate([low, block, high], axis=dim)
    return block


def partner_swap(value, axis, mask):
    count = lax.axis_size(axis)
    return lax.ppermute(value, axis, [(i, i ^ mask) for i in range(count)])


def axis_bit(axis, bit):
    return (lax.axis_index(axis) // (1 << bit)) % 2


def flips(group):
    for code in range(1, 1 << len(group)):
        yield [(code >> k) % 2 for k in range(len(group))]


def gather_by_bits(block, axis, groups):
    levels = lax.axis_size(axis).bit_length() - 1
    mine = [axis_bit(axis, bit) for bit in range(levels)]
    zero = [0] * block.ndim
    held = jnp.zeros((2,) * levels + block.shape, block.dtype)
    held = lax.dynamic_update_slice(
        held, block.reshape((1,) * levels + block.shape), mine[::-1] + zero
    )
    done = set()
    for group in groups:
        start = [0 if b in done else mine[b] for b in range(levels)]
        size = [2 if b in done else 1 for b in range(levels)]
        region = lax.dynamic_slice(held, start[::-1] + zero, size[::-1] + list(block.shape))
        arrived = []
        for flip in flips(group):
            mask = sum(f << b for f, b in zip(flip, group))
            place = list(start)
            for f, b in zip(flip, group):
                place[b] = (mine[b] + f) % 2
            arrived.append((partner_swap(region, axis, mask), place))
        for other, place in arrived:
            held = lax.dynamic_update_slice(held, other, place[::-1] + zero)
        done.update(group)
    return held.reshape((-1,) + block.shape)


def scatter_by_bits(total, axis, groups):
    levels = lax.axis_size(axis).bit_length() - 1
    mine = [axis_bit(axis, bit) for bit in range(levels)]
    held = total.reshape((2,) * levels + (total.shape[0] // 2**levels,) + total.shape[1:])
    rest = [0] * (held.ndim - levels)
    for group in groups:
        size = [1 if b in group else held.shape[levels - 1 - b] for b in range(levels)]
        size = size[::-1] + list(held.shape[levels:])
        own = [mine[b] if b in group else 0 for b in range(levels)]
        summed = lax.dynamic_slice(held, own[::-1] + rest, size)
        for flip in flips(group):
            mask = sum(f << b for f, b in zip(flip, group))
            place = list(own)
            for f, b in zip(flip, group):
                place[b] = (mine[b] + f) % 2
            send = lax.dynamic_slice(held, place[::-1] + rest, size)
            summed = summed + partner_swap(send, axis, mask)
        held = summed
    return held.reshape(held.shape[levels:])


def gather_weights(w_query, w_keyvalue, w_output, row_groups):
    rows, width = w_query.shape
    kv_pack = w_keyvalue.reshape(rows, 2, width).transpose(1, 0, 2).reshape(2 * rows, width)
    out_rows = w_output.shape[0]
    out_pack = w_output.reshape(out_rows, 2, width).transpose(1, 0, 2).reshape(2 * out_rows, width)
    qo_pack = jnp.concatenate([w_query, out_pack], axis=0)
    own = axis_bit("col", 0)
    packed = jnp.where(own == 0, kv_pack, qo_pack)
    fetched = gather_by_bits(packed, "row", row_groups)
    held = jnp.zeros((2,) + fetched.shape, fetched.dtype)
    held = lax.dynamic_update_slice(held, fetched[None], (own, 0, 0, 0))
    held = lax.dynamic_update_slice(held, partner_swap(fetched, "col", 1)[None], (1 - own, 0, 0, 0))
    count = fetched.shape[0]
    kv = held[0].reshape(count, 2, rows, width).transpose(0, 2, 1, 3).reshape(count * rows, 2 * width)
    query = held[1, :, :rows].reshape(count * rows, width)
    output = held[1, :, rows:].reshape(count, 2, out_rows, width).transpose(0, 2, 1, 3)
    return query, kv, output.reshape(count * out_rows, 2 * width)


def normalize(inputs, norm_gain):
    values = inputs.astype(jnp.float32)
    center = values - jnp.mean(values, axis=-1, keepdims=True)
    spread = lax.rsqrt(jnp.mean(center * center, axis=-1, keepdims=True) + EPS)
    standard = center * spread
    return (standard, spread, (standard * norm_gain).astype(jnp.bfloat16))


def window_mask(row_start, col_start, tile_rows, tile_cols, height, map_width):
    ext_rows = tile_rows + 2 * RADIUS
    ext_cols = tile_cols + 2 * RADIUS
    query_pos = jnp.arange(tile_rows * tile_cols, dtype=jnp.int32)
    query_row = query_pos // tile_cols
    query_col = query_pos % tile_cols
    ext_pos = jnp.arange(ext_rows * ext_cols, dtype=jnp.int32)
    ext_row = ext_pos // ext_cols
    ext_col = ext_pos % ext_cols
    nearby = (jnp.abs(ext_row[None, :] - RADIUS - query_row[:, None]) <= RADIUS) & (
        jnp.abs(ext_col[None, :] - RADIUS - query_col[:, None]) <= RADIUS
    )
    global_row = row_start + ext_row - RADIUS
    global_col = col_start + ext_col - RADIUS
    inside = (
        (global_row >= 0) & (global_row < height) & (global_col >= 0) & (global_col < map_width)
    )
    return nearby & inside[None, :]


def tile_forward(queries, keyvalue_ext, allowed):
    batches, query_count, inner_width = queries.shape
    head_size = inner_width // HEADS
    query_heads = queries.reshape(batches, query_count, HEADS, head_size)
    key_heads = keyvalue_ext[:, :, :inner_width].reshape(batches, -1, HEADS, head_size)
    value_heads = keyvalue_ext[:, :, inner_width:].reshape(batches, -1, HEADS, head_size)
    scores = jnp.einsum(
        "bqhd,bkhd->bhqk", query_heads, key_heads, preferred_element_type=jnp.float32
    ) / math.sqrt(head_size)
    scores = jnp.where(allowed, scores, MASKED)
    row_max = jnp.max(scores, axis=-1, keepdims=True)
    exponent = jnp.exp(scores - row_max)
    soft = exponent / jnp.sum(exponent, axis=-1, keepdims=True)
    rounded = soft.astype(jnp.bfloat16)
    attended = jnp.einsum(
        "bhqk,bkhd->bqhd", rounded, value_heads, preferred_element_type=jnp.float32
    )
    return (attended.astype(jnp.bfloat16).reshape(batches, query_count, inner_width), soft, rounded)


def tile_backward(queries, keyvalue_ext, soft, rounded, inner_grad):
    batches, query_count, inner_width = queries.shape
    head_size = inner_width // HEADS
    query_heads = queries.reshape(batches, query_count, HEADS, head_size)
    key_heads = keyvalue_ext[:, :, :inner_width].reshape(batches, -1, HEADS, head_size)
    value_heads = keyvalue_ext[:, :, inner_width:].reshape(batches, -1, HEADS, head_size)
    grad_heads = inner_grad.reshape(batches, query_count, HEADS, head_size)
    prob_grad = jnp.einsum(
        "bqhd,bkhd->bhqk", grad_heads, value_heads, preferred_element_type=jnp.float32
    )
    row_dot = jnp.sum(soft * prob_grad, axis=-1, keepdims=True)
    score_grad = (soft * (prob_grad - row_dot) / math.sqrt(head_size)).astype(jnp.bfloat16)
    query_grad = jnp.einsum(
        "bhqk,bkhd->bqhd", score_grad, key_heads, preferred_element_type=jnp.float32
    )
    key_grad = jnp.einsum(
        "bhqk,bqhd->bkhd", score_grad, query_heads, preferred_element_type=jnp.float32
    )
    value_grad = jnp.einsum(
        "bhqk,bqhd->bkhd", rounded, grad_heads, preferred_element_type=jnp.float32
    )
    ext_count = key_grad.shape[1]
    joined = jnp.concatenate(
        [
            key_grad.reshape(batches, ext_count, inner_width),
            value_grad.reshape(batches, ext_count, inner_width),
        ],
        axis=-1,
    )
    return (query_grad.astype(jnp.bfloat16).reshape(batches, query_count, inner_width), joined)


def fold_cols(extended):
    left_strip = extended[:, :, :RADIUS]
    right_strip = extended[:, :, extended.shape[2] - RADIUS :]
    middle = extended[:, :, RADIUS : extended.shape[2] - RADIUS]
    from_right = shifted(left_strip, "col", -1)
    from_left = shifted(right_strip, "col", 1)
    inner_cols = middle.shape[2]
    return (
        middle
        + jnp.pad(from_left, ((0, 0), (0, 0), (0, inner_cols - RADIUS), (0, 0)))
        + jnp.pad(from_right, ((0, 0), (0, 0), (inner_cols - RADIUS, 0), (0, 0)))
    )


def fold_rows(extended):
    upper_strip = extended[:, :RADIUS]
    lower_strip = extended[:, extended.shape[1] - RADIUS :]
    middle = extended[:, RADIUS : extended.shape[1] - RADIUS]
    from_below = shifted(upper_strip, "row", -1)
    from_above = shifted(lower_strip, "row", 1)
    inner_rows = middle.shape[1]
    return (
        middle
        + jnp.pad(from_above, ((0, 0), (0, inner_rows - RADIUS), (0, 0), (0, 0)))
        + jnp.pad(from_below, ((0, 0), (inner_rows - RADIUS, 0), (0, 0), (0, 0)))
    )


def local(inputs, norm_gain, w_query, w_keyvalue, w_output, out_grad):
    batches, tile_rows, tile_cols, model_width = inputs.shape
    ext_rows = tile_rows + 2 * RADIUS
    ext_cols = tile_cols + 2 * RADIUS
    standard, spread, normed = normalize(inputs, norm_gain)
    flat_norm = normed.reshape(-1, model_width)
    row_levels = lax.axis_size("row").bit_length() - 1
    row_groups = [[b] for b in range(row_levels)]
    full_query, full_keyvalue, full_output = gather_weights(
        w_query, w_keyvalue, w_output, row_groups[::-1]
    )
    inner_width = full_query.shape[1]
    queries = jnp.dot(flat_norm, full_query, preferred_element_type=jnp.float32).astype(
        jnp.bfloat16
    )
    queries = queries.reshape(batches, tile_rows * tile_cols, inner_width)
    keyvalue = jnp.dot(flat_norm, full_keyvalue, preferred_element_type=jnp.float32).astype(
        jnp.bfloat16
    )
    keyvalue = keyvalue.reshape(batches, tile_rows, tile_cols, 2 * inner_width)
    keyvalue_ext = with_halo(keyvalue, (("row", 1), ("col", 2)), RADIUS)
    keyvalue_ext = keyvalue_ext.reshape(batches, ext_rows * ext_cols, 2 * inner_width)
    allowed = window_mask(
        lax.axis_index("row") * tile_rows,
        lax.axis_index("col") * tile_cols,
        tile_rows,
        tile_cols,
        tile_rows * lax.axis_size("row"),
        tile_cols * lax.axis_size("col"),
    )
    attended, soft, rounded = tile_forward(queries, keyvalue_ext, allowed)
    projected = jnp.dot(
        attended.reshape(-1, inner_width), full_output, preferred_element_type=jnp.float32
    )
    layer_out = (inputs.astype(jnp.float32) + projected.reshape(inputs.shape)).astype(jnp.bfloat16)
    flat_grad = out_grad.reshape(-1, model_width)
    inner_grad = lax.dot_general(
        flat_grad, full_output, (((1,), (1,)), ((), ())), preferred_element_type=jnp.float32
    ).astype(jnp.bfloat16)
    inner_grad = inner_grad.reshape(batches, tile_rows * tile_cols, inner_width)
    query_grad, keyvalue_part = tile_backward(queries, keyvalue_ext, soft, rounded, inner_grad)
    keyvalue_part = keyvalue_part.reshape(batches, ext_rows, ext_cols, 2 * inner_width)
    owned = fold_rows(fold_cols(keyvalue_part))
    token_grad = owned.astype(jnp.bfloat16).reshape(-1, 2 * inner_width)
    row_count, col_count = lax.axis_size("row"), lax.axis_size("col")
    col_levels = col_count.bit_length() - 1
    feature_part = model_width // row_count
    partial = lax.dot_general(
        flat_norm, token_grad, (((0,), (0,)), ((), ())), preferred_element_type=jnp.float32
    )
    half = partial.shape[1] // 2
    own = axis_bit("col", 0)
    halves = partial.reshape(model_width, 2, half)
    pair_part = lax.dynamic_index_in_dim(halves, own, 1, keepdims=False) + partner_swap(
        lax.dynamic_index_in_dim(halves, 1 - own, 1, keepdims=False), "col", 1
    )
    rows_part = scatter_by_bits(
        pair_part.reshape(row_count, feature_part, half), "row", row_groups
    )[0]
    for bit in range(1, col_levels):
        rows_part = rows_part + partner_swap(rows_part, "col", 1 << bit)
    held = jnp.zeros((2,) + rows_part.shape, rows_part.dtype)
    held = lax.dynamic_update_slice(held, rows_part[None], (own, 0, 0))
    held = lax.dynamic_update_slice(held, partner_swap(rows_part, "col", 1)[None], (1 - own, 0, 0))
    keyvalue_grad = held.transpose(1, 0, 2).reshape(feature_part, -1)
    normed_grad = lax.dot_general(
        query_grad.reshape(-1, inner_width),
        full_query,
        (((1,), (1,)), ((), ())),
        preferred_element_type=jnp.float32,
    )
    normed_grad = normed_grad + lax.dot_general(
        token_grad, full_keyvalue, (((1,), (1,)), ((), ())), preferred_element_type=jnp.float32
    )
    gained = normed_grad.reshape(inputs.shape) * norm_gain
    in_grad = out_grad.astype(jnp.float32) + spread * (
        gained
        - jnp.mean(gained, axis=-1, keepdims=True)
        - standard * jnp.mean(gained * standard, axis=-1, keepdims=True)
    )
    return (layer_out, in_grad.astype(jnp.bfloat16), keyvalue_grad)


def solution(mesh):
    return jax.shard_map(
        local,
        mesh=mesh,
        in_specs=(
            P(None, "row", "col", None),
            P(),
            P("row", None),
            P("row", None),
            P("row", None),
            P(None, "row", "col", None),
        ),
        out_specs=(P(None, "row", "col", None), P(None, "row", "col", None), P("row", None)),
        check_vma=False,
    )
```

```python
import math

import jax
import jax.numpy as jnp
from jax import lax
from jax.sharding import PartitionSpec as P

HEADS = 8
RADIUS = 6


EPS = 1e-05
MASKED = -1e30


def shifted(value, axis, steps):
    count = lax.axis_size(axis)
    first, last = (max(0, -steps), min(count, count - steps))
    return lax.ppermute(value, axis, [(source, source + steps) for source in range(first, last)])


def with_halo(block, sides, width):
    for axis, dim in sides:
        count = lax.axis_size(axis)
        forward = [(i, i + 1) for i in range(count - 1)]
        backward = [(target, source) for source, target in forward]
        low = lax.ppermute(
            lax.slice_in_dim(block, block.shape[dim] - width, None, axis=dim), axis, forward
        )
        high = lax.ppermute(lax.slice_in_dim(block, 0, width, axis=dim), axis, backward)
        block = jnp.concatenate([low, block, high], axis=dim)
    return block


def partner_swap(value, axis, mask):
    count = lax.axis_size(axis)
    return lax.ppermute(value, axis, [(i, i ^ mask) for i in range(count)])


def axis_bit(axis, bit):
    return (lax.axis_index(axis) // (1 << bit)) % 2


def flips(group):
    for code in range(1, 1 << len(group)):
        yield [(code >> k) % 2 for k in range(len(group))]


def gather_by_bits(block, axis, groups):
    levels = lax.axis_size(axis).bit_length() - 1
    mine = [axis_bit(axis, bit) for bit in range(levels)]
    zero = [0] * block.ndim
    held = jnp.zeros((2,) * levels + block.shape, block.dtype)
    held = lax.dynamic_update_slice(
        held, block.reshape((1,) * levels + block.shape), mine[::-1] + zero
    )
    done = set()
    for group in groups:
        start = [0 if b in done else mine[b] for b in range(levels)]
        size = [2 if b in done else 1 for b in range(levels)]
        region = lax.dynamic_slice(held, start[::-1] + zero, size[::-1] + list(block.shape))
        arrived = []
        for flip in flips(group):
            mask = sum(f << b for f, b in zip(flip, group))
            place = list(start)
            for f, b in zip(flip, group):
                place[b] = (mine[b] + f) % 2
            arrived.append((partner_swap(region, axis, mask), place))
        for other, place in arrived:
            held = lax.dynamic_update_slice(held, other, place[::-1] + zero)
        done.update(group)
    return held.reshape((-1,) + block.shape)


def scatter_by_bits(total, axis, groups):
    levels = lax.axis_size(axis).bit_length() - 1
    mine = [axis_bit(axis, bit) for bit in range(levels)]
    held = total.reshape((2,) * levels + (total.shape[0] // 2**levels,) + total.shape[1:])
    rest = [0] * (held.ndim - levels)
    for group in groups:
        size = [1 if b in group else held.shape[levels - 1 - b] for b in range(levels)]
        size = size[::-1] + list(held.shape[levels:])
        own = [mine[b] if b in group else 0 for b in range(levels)]
        summed = lax.dynamic_slice(held, own[::-1] + rest, size)
        for flip in flips(group):
            mask = sum(f << b for f, b in zip(flip, group))
            place = list(own)
            for f, b in zip(flip, group):
                place[b] = (mine[b] + f) % 2
            send = lax.dynamic_slice(held, place[::-1] + rest, size)
            summed = summed + partner_swap(send, axis, mask)
        held = summed
    return held.reshape(held.shape[levels:])


def gather_weights(w_query, w_keyvalue, w_output, row_groups):
    rows, width = w_query.shape
    kv_pack = w_keyvalue.reshape(rows, 2, width).transpose(1, 0, 2).reshape(2 * rows, width)
    out_rows = w_output.shape[0]
    out_pack = w_output.reshape(out_rows, 2, width).transpose(1, 0, 2).reshape(2 * out_rows, width)
    qo_pack = jnp.concatenate([w_query, out_pack], axis=0)
    own = axis_bit("col", 0)
    packed = jnp.where(own == 0, kv_pack, qo_pack)
    fetched = gather_by_bits(packed, "row", row_groups)
    held = jnp.zeros((2,) + fetched.shape, fetched.dtype)
    held = lax.dynamic_update_slice(held, fetched[None], (own, 0, 0, 0))
    held = lax.dynamic_update_slice(held, partner_swap(fetched, "col", 1)[None], (1 - own, 0, 0, 0))
    count = fetched.shape[0]
    kv = held[0].reshape(count, 2, rows, width).transpose(0, 2, 1, 3).reshape(count * rows, 2 * width)
    query = held[1, :, :rows].reshape(count * rows, width)
    output = held[1, :, rows:].reshape(count, 2, out_rows, width).transpose(0, 2, 1, 3)
    return query, kv, output.reshape(count * out_rows, 2 * width)


def normalize(inputs, norm_gain):
    values = inputs.astype(jnp.float32)
    center = values - jnp.mean(values, axis=-1, keepdims=True)
    spread = lax.rsqrt(jnp.mean(center * center, axis=-1, keepdims=True) + EPS)
    standard = center * spread
    return (standard, spread, (standard * norm_gain).astype(jnp.bfloat16))


def window_mask(row_start, col_start, tile_rows, tile_cols, height, map_width):
    ext_rows = tile_rows + 2 * RADIUS
    ext_cols = tile_cols + 2 * RADIUS
    query_pos = jnp.arange(tile_rows * tile_cols, dtype=jnp.int32)
    query_row = query_pos // tile_cols
    query_col = query_pos % tile_cols
    ext_pos = jnp.arange(ext_rows * ext_cols, dtype=jnp.int32)
    ext_row = ext_pos // ext_cols
    ext_col = ext_pos % ext_cols
    nearby = (jnp.abs(ext_row[None, :] - RADIUS - query_row[:, None]) <= RADIUS) & (
        jnp.abs(ext_col[None, :] - RADIUS - query_col[:, None]) <= RADIUS
    )
    global_row = row_start + ext_row - RADIUS
    global_col = col_start + ext_col - RADIUS
    inside = (
        (global_row >= 0) & (global_row < height) & (global_col >= 0) & (global_col < map_width)
    )
    return nearby & inside[None, :]


def tile_forward(queries, keyvalue_ext, allowed):
    batches, query_count, inner_width = queries.shape
    head_size = inner_width // HEADS
    query_heads = queries.reshape(batches, query_count, HEADS, head_size)
    key_heads = keyvalue_ext[:, :, :inner_width].reshape(batches, -1, HEADS, head_size)
    value_heads = keyvalue_ext[:, :, inner_width:].reshape(batches, -1, HEADS, head_size)
    scores = jnp.einsum(
        "bqhd,bkhd->bhqk", query_heads, key_heads, preferred_element_type=jnp.float32
    ) / math.sqrt(head_size)
    scores = jnp.where(allowed, scores, MASKED)
    row_max = jnp.max(scores, axis=-1, keepdims=True)
    exponent = jnp.exp(scores - row_max)
    soft = exponent / jnp.sum(exponent, axis=-1, keepdims=True)
    rounded = soft.astype(jnp.bfloat16)
    attended = jnp.einsum(
        "bhqk,bkhd->bqhd", rounded, value_heads, preferred_element_type=jnp.float32
    )
    return (attended.astype(jnp.bfloat16).reshape(batches, query_count, inner_width), soft, rounded)


def tile_backward(queries, keyvalue_ext, soft, rounded, inner_grad):
    batches, query_count, inner_width = queries.shape
    head_size = inner_width // HEADS
    query_heads = queries.reshape(batches, query_count, HEADS, head_size)
    key_heads = keyvalue_ext[:, :, :inner_width].reshape(batches, -1, HEADS, head_size)
    value_heads = keyvalue_ext[:, :, inner_width:].reshape(batches, -1, HEADS, head_size)
    grad_heads = inner_grad.reshape(batches, query_count, HEADS, head_size)
    prob_grad = jnp.einsum(
        "bqhd,bkhd->bhqk", grad_heads, value_heads, preferred_element_type=jnp.float32
    )
    row_dot = jnp.sum(soft * prob_grad, axis=-1, keepdims=True)
    score_grad = (soft * (prob_grad - row_dot) / math.sqrt(head_size)).astype(jnp.bfloat16)
    query_grad = jnp.einsum(
        "bhqk,bkhd->bqhd", score_grad, key_heads, preferred_element_type=jnp.float32
    )
    key_grad = jnp.einsum(
        "bhqk,bqhd->bkhd", score_grad, query_heads, preferred_element_type=jnp.float32
    )
    value_grad = jnp.einsum(
        "bhqk,bqhd->bkhd", rounded, grad_heads, preferred_element_type=jnp.float32
    )
    ext_count = key_grad.shape[1]
    joined = jnp.concatenate(
        [
            key_grad.reshape(batches, ext_count, inner_width),
            value_grad.reshape(batches, ext_count, inner_width),
        ],
        axis=-1,
    )
    return (query_grad.astype(jnp.bfloat16).reshape(batches, query_count, inner_width), joined)


def fold_cols(extended):
    left_strip = extended[:, :, :RADIUS]
    right_strip = extended[:, :, extended.shape[2] - RADIUS :]
    middle = extended[:, :, RADIUS : extended.shape[2] - RADIUS]
    from_right = shifted(left_strip, "col", -1)
    from_left = shifted(right_strip, "col", 1)
    inner_cols = middle.shape[2]
    return (
        middle
        + jnp.pad(from_left, ((0, 0), (0, 0), (0, inner_cols - RADIUS), (0, 0)))
        + jnp.pad(from_right, ((0, 0), (0, 0), (inner_cols - RADIUS, 0), (0, 0)))
    )


def fold_rows(extended):
    upper_strip = extended[:, :RADIUS]
    lower_strip = extended[:, extended.shape[1] - RADIUS :]
    middle = extended[:, RADIUS : extended.shape[1] - RADIUS]
    from_below = shifted(upper_strip, "row", -1)
    from_above = shifted(lower_strip, "row", 1)
    inner_rows = middle.shape[1]
    return (
        middle
        + jnp.pad(from_above, ((0, 0), (0, inner_rows - RADIUS), (0, 0), (0, 0)))
        + jnp.pad(from_below, ((0, 0), (inner_rows - RADIUS, 0), (0, 0), (0, 0)))
    )


def local(inputs, norm_gain, w_query, w_keyvalue, w_output, out_grad):
    batches, tile_rows, tile_cols, model_width = inputs.shape
    ext_rows = tile_rows + 2 * RADIUS
    ext_cols = tile_cols + 2 * RADIUS
    standard, spread, normed = normalize(inputs, norm_gain)
    flat_norm = normed.reshape(-1, model_width)
    row_levels = lax.axis_size("row").bit_length() - 1
    row_groups = [[b] for b in range(row_levels)]
    full_query, full_keyvalue, full_output = gather_weights(
        w_query, w_keyvalue, w_output, row_groups[::-1]
    )
    inner_width = full_query.shape[1]
    queries = jnp.dot(flat_norm, full_query, preferred_element_type=jnp.float32).astype(
        jnp.bfloat16
    )
    queries = queries.reshape(batches, tile_rows * tile_cols, inner_width)
    keyvalue = jnp.dot(flat_norm, full_keyvalue, preferred_element_type=jnp.float32).astype(
        jnp.bfloat16
    )
    keyvalue = keyvalue.reshape(batches, tile_rows, tile_cols, 2 * inner_width)
    joined_ext = with_halo(
        jnp.concatenate([keyvalue, normed], axis=-1), (("row", 1), ("col", 2)), RADIUS
    )
    keyvalue_ext = joined_ext[..., : 2 * inner_width].reshape(
        batches, ext_rows * ext_cols, 2 * inner_width
    )
    normed_ext = joined_ext[..., 2 * inner_width :].reshape(-1, model_width)
    allowed = window_mask(
        lax.axis_index("row") * tile_rows,
        lax.axis_index("col") * tile_cols,
        tile_rows,
        tile_cols,
        tile_rows * lax.axis_size("row"),
        tile_cols * lax.axis_size("col"),
    )
    attended, soft, rounded = tile_forward(queries, keyvalue_ext, allowed)
    projected = jnp.dot(
        attended.reshape(-1, inner_width), full_output, preferred_element_type=jnp.float32
    )
    layer_out = (inputs.astype(jnp.float32) + projected.reshape(inputs.shape)).astype(jnp.bfloat16)
    flat_grad = out_grad.reshape(-1, model_width)
    inner_grad = lax.dot_general(
        flat_grad, full_output, (((1,), (1,)), ((), ())), preferred_element_type=jnp.float32
    ).astype(jnp.bfloat16)
    inner_grad = inner_grad.reshape(batches, tile_rows * tile_cols, inner_width)
    query_grad, keyvalue_part = tile_backward(queries, keyvalue_ext, soft, rounded, inner_grad)
    keyvalue_part = keyvalue_part.reshape(batches, ext_rows, ext_cols, 2 * inner_width)
    owned = fold_rows(fold_cols(keyvalue_part))
    token_grad = owned.astype(jnp.bfloat16).reshape(-1, 2 * inner_width)
    row_count, col_count = lax.axis_size("row"), lax.axis_size("col")
    col_levels = col_count.bit_length() - 1
    feature_part = model_width // row_count
    partial = lax.dot_general(
        normed_ext,
        keyvalue_part.reshape(-1, 2 * inner_width).astype(jnp.bfloat16),
        (((0,), (0,)), ((), ())),
        preferred_element_type=jnp.float32,
    )
    half = partial.shape[1] // 2
    own = axis_bit("col", 0)
    halves = partial.reshape(model_width, 2, half)
    pair_part = lax.dynamic_index_in_dim(halves, own, 1, keepdims=False) + partner_swap(
        lax.dynamic_index_in_dim(halves, 1 - own, 1, keepdims=False), "col", 1
    )
    rows_part = scatter_by_bits(
        pair_part.reshape(row_count, feature_part, half), "row", row_groups
    )[0]
    for bit in range(1, col_levels):
        rows_part = rows_part + partner_swap(rows_part, "col", 1 << bit)
    held = jnp.zeros((2,) + rows_part.shape, rows_part.dtype)
    held = lax.dynamic_update_slice(held, rows_part[None], (own, 0, 0))
    held = lax.dynamic_update_slice(held, partner_swap(rows_part, "col", 1)[None], (1 - own, 0, 0))
    keyvalue_grad = held.transpose(1, 0, 2).reshape(feature_part, -1)
    normed_grad = lax.dot_general(
        query_grad.reshape(-1, inner_width),
        full_query,
        (((1,), (1,)), ((), ())),
        preferred_element_type=jnp.float32,
    )
    normed_grad = normed_grad + lax.dot_general(
        token_grad, full_keyvalue, (((1,), (1,)), ((), ())), preferred_element_type=jnp.float32
    )
    gained = normed_grad.reshape(inputs.shape) * norm_gain
    in_grad = out_grad.astype(jnp.float32) + spread * (
        gained
        - jnp.mean(gained, axis=-1, keepdims=True)
        - standard * jnp.mean(gained * standard, axis=-1, keepdims=True)
    )
    return (layer_out, in_grad.astype(jnp.bfloat16), keyvalue_grad)


def solution(mesh):
    return jax.shard_map(
        local,
        mesh=mesh,
        in_specs=(
            P(None, "row", "col", None),
            P(),
            P("row", None),
            P("row", None),
            P("row", None),
            P(None, "row", "col", None),
        ),
        out_specs=(P(None, "row", "col", None), P(None, "row", "col", None), P("row", None)),
        check_vma=False,
    )
```

```python
import math

import jax
import jax.numpy as jnp
from jax import lax
from jax.sharding import PartitionSpec as P

HEADS = 8
RADIUS = 6


EPS = 1e-05
MASKED = -1e30


def shifted(value, axis, steps):
    count = lax.axis_size(axis)
    first, last = (max(0, -steps), min(count, count - steps))
    return lax.ppermute(value, axis, [(source, source + steps) for source in range(first, last)])


def with_halo(block, sides, width):
    for axis, dim in sides:
        count = lax.axis_size(axis)
        forward = [(i, i + 1) for i in range(count - 1)]
        backward = [(target, source) for source, target in forward]
        low = lax.ppermute(
            lax.slice_in_dim(block, block.shape[dim] - width, None, axis=dim), axis, forward
        )
        high = lax.ppermute(lax.slice_in_dim(block, 0, width, axis=dim), axis, backward)
        block = jnp.concatenate([low, block, high], axis=dim)
    return block


def partner_swap(value, axis, mask):
    count = lax.axis_size(axis)
    return lax.ppermute(value, axis, [(i, i ^ mask) for i in range(count)])


def axis_bit(axis, bit):
    return (lax.axis_index(axis) // (1 << bit)) % 2


def flips(group):
    for code in range(1, 1 << len(group)):
        yield [(code >> k) % 2 for k in range(len(group))]


def gather_by_bits(block, axis, groups):
    levels = lax.axis_size(axis).bit_length() - 1
    mine = [axis_bit(axis, bit) for bit in range(levels)]
    zero = [0] * block.ndim
    held = jnp.zeros((2,) * levels + block.shape, block.dtype)
    held = lax.dynamic_update_slice(
        held, block.reshape((1,) * levels + block.shape), mine[::-1] + zero
    )
    done = set()
    for group in groups:
        start = [0 if b in done else mine[b] for b in range(levels)]
        size = [2 if b in done else 1 for b in range(levels)]
        region = lax.dynamic_slice(held, start[::-1] + zero, size[::-1] + list(block.shape))
        arrived = []
        for flip in flips(group):
            mask = sum(f << b for f, b in zip(flip, group))
            place = list(start)
            for f, b in zip(flip, group):
                place[b] = (mine[b] + f) % 2
            arrived.append((partner_swap(region, axis, mask), place))
        for other, place in arrived:
            held = lax.dynamic_update_slice(held, other, place[::-1] + zero)
        done.update(group)
    return held.reshape((-1,) + block.shape)


def scatter_by_bits(total, axis, groups):
    levels = lax.axis_size(axis).bit_length() - 1
    mine = [axis_bit(axis, bit) for bit in range(levels)]
    held = total.reshape((2,) * levels + (total.shape[0] // 2**levels,) + total.shape[1:])
    rest = [0] * (held.ndim - levels)
    for group in groups:
        size = [1 if b in group else held.shape[levels - 1 - b] for b in range(levels)]
        size = size[::-1] + list(held.shape[levels:])
        own = [mine[b] if b in group else 0 for b in range(levels)]
        summed = lax.dynamic_slice(held, own[::-1] + rest, size)
        for flip in flips(group):
            mask = sum(f << b for f, b in zip(flip, group))
            place = list(own)
            for f, b in zip(flip, group):
                place[b] = (mine[b] + f) % 2
            send = lax.dynamic_slice(held, place[::-1] + rest, size)
            summed = summed + partner_swap(send, axis, mask)
        held = summed
    return held.reshape(held.shape[levels:])


def reduce_over_bits(block, axis, bits):
    mine = [axis_bit(axis, bit) for bit in bits]
    code = sum(m * (1 << k) for k, m in enumerate(mine))
    zero = [0] * block.ndim
    held = jnp.zeros((1 << len(bits),) + block.shape, block.dtype)
    held = lax.dynamic_update_slice(held, block[None], [code] + zero)
    for flip in flips(bits):
        mask = sum(f << b for f, b in zip(flip, bits))
        other = sum(((m + f) % 2) * (1 << k) for k, (m, f) in enumerate(zip(mine, flip)))
        held = lax.dynamic_update_slice(held, partner_swap(block, axis, mask)[None], [other] + zero)
    return jnp.sum(held, axis=0)


def gather_weights(w_query, w_keyvalue, w_output, row_groups):
    rows, width = w_query.shape
    kv_pack = w_keyvalue.reshape(rows, 2, width).transpose(1, 0, 2).reshape(2 * rows, width)
    out_rows = w_output.shape[0]
    out_pack = w_output.reshape(out_rows, 2, width).transpose(1, 0, 2).reshape(2 * out_rows, width)
    qo_pack = jnp.concatenate([w_query, out_pack], axis=0)
    own = axis_bit("col", 0)
    packed = jnp.where(own == 0, kv_pack, qo_pack)
    fetched = gather_by_bits(packed, "row", row_groups)
    held = jnp.zeros((2,) + fetched.shape, fetched.dtype)
    held = lax.dynamic_update_slice(held, fetched[None], (own, 0, 0, 0))
    held = lax.dynamic_update_slice(held, partner_swap(fetched, "col", 1)[None], (1 - own, 0, 0, 0))
    count = fetched.shape[0]
    kv = held[0].reshape(count, 2, rows, width).transpose(0, 2, 1, 3).reshape(count * rows, 2 * width)
    query = held[1, :, :rows].reshape(count * rows, width)
    output = held[1, :, rows:].reshape(count, 2, out_rows, width).transpose(0, 2, 1, 3)
    return query, kv, output.reshape(count * out_rows, 2 * width)


def normalize(inputs, norm_gain):
    values = inputs.astype(jnp.float32)
    center = values - jnp.mean(values, axis=-1, keepdims=True)
    spread = lax.rsqrt(jnp.mean(center * center, axis=-1, keepdims=True) + EPS)
    standard = center * spread
    return (standard, spread, (standard * norm_gain).astype(jnp.bfloat16))


def window_mask(row_start, col_start, tile_rows, tile_cols, height, map_width):
    ext_rows = tile_rows + 2 * RADIUS
    ext_cols = tile_cols + 2 * RADIUS
    query_pos = jnp.arange(tile_rows * tile_cols, dtype=jnp.int32)
    query_row = query_pos // tile_cols
    query_col = query_pos % tile_cols
    ext_pos = jnp.arange(ext_rows * ext_cols, dtype=jnp.int32)
    ext_row = ext_pos // ext_cols
    ext_col = ext_pos % ext_cols
    nearby = (jnp.abs(ext_row[None, :] - RADIUS - query_row[:, None]) <= RADIUS) & (
        jnp.abs(ext_col[None, :] - RADIUS - query_col[:, None]) <= RADIUS
    )
    global_row = row_start + ext_row - RADIUS
    global_col = col_start + ext_col - RADIUS
    inside = (
        (global_row >= 0) & (global_row < height) & (global_col >= 0) & (global_col < map_width)
    )
    return nearby & inside[None, :]


def tile_forward(queries, keyvalue_ext, allowed):
    batches, query_count, inner_width = queries.shape
    head_size = inner_width // HEADS
    query_heads = queries.reshape(batches, query_count, HEADS, head_size)
    key_heads = keyvalue_ext[:, :, :inner_width].reshape(batches, -1, HEADS, head_size)
    value_heads = keyvalue_ext[:, :, inner_width:].reshape(batches, -1, HEADS, head_size)
    scores = jnp.einsum(
        "bqhd,bkhd->bhqk", query_heads, key_heads, preferred_element_type=jnp.float32
    ) / math.sqrt(head_size)
    scores = jnp.where(allowed, scores, MASKED)
    row_max = jnp.max(scores, axis=-1, keepdims=True)
    exponent = jnp.exp(scores - row_max)
    soft = exponent / jnp.sum(exponent, axis=-1, keepdims=True)
    rounded = soft.astype(jnp.bfloat16)
    attended = jnp.einsum(
        "bhqk,bkhd->bqhd", rounded, value_heads, preferred_element_type=jnp.float32
    )
    return (attended.astype(jnp.bfloat16).reshape(batches, query_count, inner_width), soft, rounded)


def tile_backward(queries, keyvalue_ext, soft, rounded, inner_grad):
    batches, query_count, inner_width = queries.shape
    head_size = inner_width // HEADS
    query_heads = queries.reshape(batches, query_count, HEADS, head_size)
    key_heads = keyvalue_ext[:, :, :inner_width].reshape(batches, -1, HEADS, head_size)
    value_heads = keyvalue_ext[:, :, inner_width:].reshape(batches, -1, HEADS, head_size)
    grad_heads = inner_grad.reshape(batches, query_count, HEADS, head_size)
    prob_grad = jnp.einsum(
        "bqhd,bkhd->bhqk", grad_heads, value_heads, preferred_element_type=jnp.float32
    )
    row_dot = jnp.sum(soft * prob_grad, axis=-1, keepdims=True)
    score_grad = (soft * (prob_grad - row_dot) / math.sqrt(head_size)).astype(jnp.bfloat16)
    query_grad = jnp.einsum(
        "bhqk,bkhd->bqhd", score_grad, key_heads, preferred_element_type=jnp.float32
    )
    key_grad = jnp.einsum(
        "bhqk,bqhd->bkhd", score_grad, query_heads, preferred_element_type=jnp.float32
    )
    value_grad = jnp.einsum(
        "bhqk,bqhd->bkhd", rounded, grad_heads, preferred_element_type=jnp.float32
    )
    ext_count = key_grad.shape[1]
    joined = jnp.concatenate(
        [
            key_grad.reshape(batches, ext_count, inner_width),
            value_grad.reshape(batches, ext_count, inner_width),
        ],
        axis=-1,
    )
    return (query_grad.astype(jnp.bfloat16).reshape(batches, query_count, inner_width), joined)


def fold_cols(extended):
    left_strip = extended[:, :, :RADIUS]
    right_strip = extended[:, :, extended.shape[2] - RADIUS :]
    middle = extended[:, :, RADIUS : extended.shape[2] - RADIUS]
    from_right = shifted(left_strip, "col", -1)
    from_left = shifted(right_strip, "col", 1)
    inner_cols = middle.shape[2]
    return (
        middle
        + jnp.pad(from_left, ((0, 0), (0, 0), (0, inner_cols - RADIUS), (0, 0)))
        + jnp.pad(from_right, ((0, 0), (0, 0), (inner_cols - RADIUS, 0), (0, 0)))
    )


def fold_rows(extended):
    upper_strip = extended[:, :RADIUS]
    lower_strip = extended[:, extended.shape[1] - RADIUS :]
    middle = extended[:, RADIUS : extended.shape[1] - RADIUS]
    from_below = shifted(upper_strip, "row", -1)
    from_above = shifted(lower_strip, "row", 1)
    inner_rows = middle.shape[1]
    return (
        middle
        + jnp.pad(from_above, ((0, 0), (0, inner_rows - RADIUS), (0, 0), (0, 0)))
        + jnp.pad(from_below, ((0, 0), (inner_rows - RADIUS, 0), (0, 0), (0, 0)))
    )


def local(inputs, norm_gain, w_query, w_keyvalue, w_output, out_grad):
    batches, tile_rows, tile_cols, model_width = inputs.shape
    ext_rows = tile_rows + 2 * RADIUS
    ext_cols = tile_cols + 2 * RADIUS
    standard, spread, normed = normalize(inputs, norm_gain)
    flat_norm = normed.reshape(-1, model_width)
    row_levels = lax.axis_size("row").bit_length() - 1
    row_groups = [[b] for b in range(row_levels)]
    far_groups = [list(range(2, row_levels))] + [[1], [0]] if row_levels > 2 else row_groups[::-1]
    full_query, full_keyvalue, full_output = gather_weights(
        w_query, w_keyvalue, w_output, far_groups
    )
    inner_width = full_query.shape[1]
    queries = jnp.dot(flat_norm, full_query, preferred_element_type=jnp.float32).astype(
        jnp.bfloat16
    )
    queries = queries.reshape(batches, tile_rows * tile_cols, inner_width)
    keyvalue = jnp.dot(flat_norm, full_keyvalue, preferred_element_type=jnp.float32).astype(
        jnp.bfloat16
    )
    keyvalue = keyvalue.reshape(batches, tile_rows, tile_cols, 2 * inner_width)
    joined_ext = with_halo(
        jnp.concatenate([keyvalue, normed], axis=-1), (("row", 1), ("col", 2)), RADIUS
    )
    keyvalue_ext = joined_ext[..., : 2 * inner_width].reshape(
        batches, ext_rows * ext_cols, 2 * inner_width
    )
    normed_ext = joined_ext[..., 2 * inner_width :].reshape(-1, model_width)
    allowed = window_mask(
        lax.axis_index("row") * tile_rows,
        lax.axis_index("col") * tile_cols,
        tile_rows,
        tile_cols,
        tile_rows * lax.axis_size("row"),
        tile_cols * lax.axis_size("col"),
    )
    attended, soft, rounded = tile_forward(queries, keyvalue_ext, allowed)
    projected = jnp.dot(
        attended.reshape(-1, inner_width), full_output, preferred_element_type=jnp.float32
    )
    layer_out = (inputs.astype(jnp.float32) + projected.reshape(inputs.shape)).astype(jnp.bfloat16)
    flat_grad = out_grad.reshape(-1, model_width)
    inner_grad = lax.dot_general(
        flat_grad, full_output, (((1,), (1,)), ((), ())), preferred_element_type=jnp.float32
    ).astype(jnp.bfloat16)
    inner_grad = inner_grad.reshape(batches, tile_rows * tile_cols, inner_width)
    query_grad, keyvalue_part = tile_backward(queries, keyvalue_ext, soft, rounded, inner_grad)
    keyvalue_part = keyvalue_part.reshape(batches, ext_rows, ext_cols, 2 * inner_width)
    owned = fold_rows(fold_cols(keyvalue_part))
    token_grad = owned.astype(jnp.bfloat16).reshape(-1, 2 * inner_width)
    row_count, col_count = lax.axis_size("row"), lax.axis_size("col")
    col_levels = col_count.bit_length() - 1
    feature_part = model_width // row_count
    partial = lax.dot_general(
        normed_ext,
        keyvalue_part.reshape(-1, 2 * inner_width).astype(jnp.bfloat16),
        (((0,), (0,)), ((), ())),
        preferred_element_type=jnp.float32,
    )
    half = partial.shape[1] // 2
    own = axis_bit("col", 0)
    halves = partial.reshape(model_width, 2, half)
    pair_part = lax.dynamic_index_in_dim(halves, own, 1, keepdims=False) + partner_swap(
        lax.dynamic_index_in_dim(halves, 1 - own, 1, keepdims=False), "col", 1
    )
    rows_part = scatter_by_bits(
        pair_part.reshape(row_count, feature_part, half), "row", row_groups
    )[0]
    rows_part = reduce_over_bits(rows_part, "col", list(range(1, col_levels)))
    held = jnp.zeros((2,) + rows_part.shape, rows_part.dtype)
    held = lax.dynamic_update_slice(held, rows_part[None], (own, 0, 0))
    held = lax.dynamic_update_slice(held, partner_swap(rows_part, "col", 1)[None], (1 - own, 0, 0))
    keyvalue_grad = held.transpose(1, 0, 2).reshape(feature_part, -1)
    normed_grad = lax.dot_general(
        query_grad.reshape(-1, inner_width),
        full_query,
        (((1,), (1,)), ((), ())),
        preferred_element_type=jnp.float32,
    )
    normed_grad = normed_grad + lax.dot_general(
        token_grad, full_keyvalue, (((1,), (1,)), ((), ())), preferred_element_type=jnp.float32
    )
    gained = normed_grad.reshape(inputs.shape) * norm_gain
    in_grad = out_grad.astype(jnp.float32) + spread * (
        gained
        - jnp.mean(gained, axis=-1, keepdims=True)
        - standard * jnp.mean(gained * standard, axis=-1, keepdims=True)
    )
    return (layer_out, in_grad.astype(jnp.bfloat16), keyvalue_grad)


def solution(mesh):
    return jax.shard_map(
        local,
        mesh=mesh,
        in_specs=(
            P(None, "row", "col", None),
            P(),
            P("row", None),
            P("row", None),
            P("row", None),
            P(None, "row", "col", None),
        ),
        out_specs=(P(None, "row", "col", None), P(None, "row", "col", None), P("row", None)),
        check_vma=False,
    )
```

```python
import math

import jax
import jax.numpy as jnp
from jax import lax
from jax.sharding import PartitionSpec as P

HEADS = 8
RADIUS = 6


EPS = 1e-05
MASKED = -1e30


def shifted(value, axis, steps):
    count = lax.axis_size(axis)
    first, last = (max(0, -steps), min(count, count - steps))
    return lax.ppermute(value, axis, [(source, source + steps) for source in range(first, last)])


def with_halo(block, sides, width):
    for axis, dim in sides:
        count = lax.axis_size(axis)
        forward = [(i, i + 1) for i in range(count - 1)]
        backward = [(target, source) for source, target in forward]
        low = lax.ppermute(
            lax.slice_in_dim(block, block.shape[dim] - width, None, axis=dim), axis, forward
        )
        high = lax.ppermute(lax.slice_in_dim(block, 0, width, axis=dim), axis, backward)
        block = jnp.concatenate([low, block, high], axis=dim)
    return block


def partner_swap(value, axis, mask):
    count = lax.axis_size(axis)
    return lax.ppermute(value, axis, [(i, i ^ mask) for i in range(count)])


def axis_bit(axis, bit):
    return (lax.axis_index(axis) // (1 << bit)) % 2


def flips(group):
    for code in range(1, 1 << len(group)):
        yield [(code >> k) % 2 for k in range(len(group))]


def gather_by_bits(block, axis, groups):
    levels = lax.axis_size(axis).bit_length() - 1
    mine = [axis_bit(axis, bit) for bit in range(levels)]
    zero = [0] * block.ndim
    held = jnp.zeros((2,) * levels + block.shape, block.dtype)
    held = lax.dynamic_update_slice(
        held, block.reshape((1,) * levels + block.shape), mine[::-1] + zero
    )
    done = set()
    for group in groups:
        start = [0 if b in done else mine[b] for b in range(levels)]
        size = [2 if b in done else 1 for b in range(levels)]
        region = lax.dynamic_slice(held, start[::-1] + zero, size[::-1] + list(block.shape))
        arrived = []
        for flip in flips(group):
            mask = sum(f << b for f, b in zip(flip, group))
            place = list(start)
            for f, b in zip(flip, group):
                place[b] = (mine[b] + f) % 2
            arrived.append((partner_swap(region, axis, mask), place))
        for other, place in arrived:
            held = lax.dynamic_update_slice(held, other, place[::-1] + zero)
        done.update(group)
    return held.reshape((-1,) + block.shape)


def scatter_by_bits(total, axis, groups, narrow=0):
    levels = lax.axis_size(axis).bit_length() - 1
    mine = [axis_bit(axis, bit) for bit in range(levels)]
    held = total.reshape((2,) * levels + (total.shape[0] // 2**levels,) + total.shape[1:])
    rest = [0] * (held.ndim - levels)
    for step, group in enumerate(groups):
        size = [1 if b in group else held.shape[levels - 1 - b] for b in range(levels)]
        size = size[::-1] + list(held.shape[levels:])
        own = [mine[b] if b in group else 0 for b in range(levels)]
        summed = lax.dynamic_slice(held, own[::-1] + rest, size)
        for flip in flips(group):
            mask = sum(f << b for f, b in zip(flip, group))
            place = list(own)
            for f, b in zip(flip, group):
                place[b] = (mine[b] + f) % 2
            send = lax.dynamic_slice(held, place[::-1] + rest, size)
            if step < narrow:
                send = send.astype(jnp.bfloat16)
            summed = summed + partner_swap(send, axis, mask).astype(summed.dtype)
        held = summed
    return held.reshape(held.shape[levels:])


def gather_weights(w_query, w_keyvalue, w_output, row_groups):
    rows, width = w_query.shape
    kv_pack = w_keyvalue.reshape(rows, 2, width).transpose(1, 0, 2).reshape(2 * rows, width)
    out_rows = w_output.shape[0]
    out_pack = w_output.reshape(out_rows, 2, width).transpose(1, 0, 2).reshape(2 * out_rows, width)
    qo_pack = jnp.concatenate([w_query, out_pack], axis=0)
    own = axis_bit("col", 0)
    packed = jnp.where(own == 0, kv_pack, qo_pack)
    fetched = gather_by_bits(packed, "row", row_groups)
    held = jnp.zeros((2,) + fetched.shape, fetched.dtype)
    held = lax.dynamic_update_slice(held, fetched[None], (own, 0, 0, 0))
    held = lax.dynamic_update_slice(held, partner_swap(fetched, "col", 1)[None], (1 - own, 0, 0, 0))
    count = fetched.shape[0]
    kv = held[0].reshape(count, 2, rows, width).transpose(0, 2, 1, 3).reshape(count * rows, 2 * width)
    query = held[1, :, :rows].reshape(count * rows, width)
    output = held[1, :, rows:].reshape(count, 2, out_rows, width).transpose(0, 2, 1, 3)
    return query, kv, output.reshape(count * out_rows, 2 * width)


def normalize(inputs, norm_gain):
    values = inputs.astype(jnp.float32)
    center = values - jnp.mean(values, axis=-1, keepdims=True)
    spread = lax.rsqrt(jnp.mean(center * center, axis=-1, keepdims=True) + EPS)
    standard = center * spread
    return (standard, spread, (standard * norm_gain).astype(jnp.bfloat16))


def window_mask(row_start, col_start, tile_rows, tile_cols, height, map_width):
    ext_rows = tile_rows + 2 * RADIUS
    ext_cols = tile_cols + 2 * RADIUS
    query_pos = jnp.arange(tile_rows * tile_cols, dtype=jnp.int32)
    query_row = query_pos // tile_cols
    query_col = query_pos % tile_cols
    ext_pos = jnp.arange(ext_rows * ext_cols, dtype=jnp.int32)
    ext_row = ext_pos // ext_cols
    ext_col = ext_pos % ext_cols
    nearby = (jnp.abs(ext_row[None, :] - RADIUS - query_row[:, None]) <= RADIUS) & (
        jnp.abs(ext_col[None, :] - RADIUS - query_col[:, None]) <= RADIUS
    )
    global_row = row_start + ext_row - RADIUS
    global_col = col_start + ext_col - RADIUS
    inside = (
        (global_row >= 0) & (global_row < height) & (global_col >= 0) & (global_col < map_width)
    )
    return nearby & inside[None, :]


def tile_forward(queries, keyvalue_ext, allowed):
    batches, query_count, inner_width = queries.shape
    head_size = inner_width // HEADS
    query_heads = queries.reshape(batches, query_count, HEADS, head_size)
    key_heads = keyvalue_ext[:, :, :inner_width].reshape(batches, -1, HEADS, head_size)
    value_heads = keyvalue_ext[:, :, inner_width:].reshape(batches, -1, HEADS, head_size)
    scores = jnp.einsum(
        "bqhd,bkhd->bhqk", query_heads, key_heads, preferred_element_type=jnp.float32
    ) / math.sqrt(head_size)
    scores = jnp.where(allowed, scores, MASKED)
    row_max = jnp.max(scores, axis=-1, keepdims=True)
    exponent = jnp.exp(scores - row_max)
    soft = exponent / jnp.sum(exponent, axis=-1, keepdims=True)
    rounded = soft.astype(jnp.bfloat16)
    attended = jnp.einsum(
        "bhqk,bkhd->bqhd", rounded, value_heads, preferred_element_type=jnp.float32
    )
    return (attended.astype(jnp.bfloat16).reshape(batches, query_count, inner_width), soft, rounded)


def tile_backward(queries, keyvalue_ext, soft, rounded, inner_grad):
    batches, query_count, inner_width = queries.shape
    head_size = inner_width // HEADS
    query_heads = queries.reshape(batches, query_count, HEADS, head_size)
    key_heads = keyvalue_ext[:, :, :inner_width].reshape(batches, -1, HEADS, head_size)
    value_heads = keyvalue_ext[:, :, inner_width:].reshape(batches, -1, HEADS, head_size)
    grad_heads = inner_grad.reshape(batches, query_count, HEADS, head_size)
    prob_grad = jnp.einsum(
        "bqhd,bkhd->bhqk", grad_heads, value_heads, preferred_element_type=jnp.float32
    )
    row_dot = jnp.sum(soft * prob_grad, axis=-1, keepdims=True)
    score_grad = (soft * (prob_grad - row_dot) / math.sqrt(head_size)).astype(jnp.bfloat16)
    query_grad = jnp.einsum(
        "bhqk,bkhd->bqhd", score_grad, key_heads, preferred_element_type=jnp.float32
    )
    key_grad = jnp.einsum(
        "bhqk,bqhd->bkhd", score_grad, query_heads, preferred_element_type=jnp.float32
    )
    value_grad = jnp.einsum(
        "bhqk,bqhd->bkhd", rounded, grad_heads, preferred_element_type=jnp.float32
    )
    ext_count = key_grad.shape[1]
    joined = jnp.concatenate(
        [
            key_grad.reshape(batches, ext_count, inner_width),
            value_grad.reshape(batches, ext_count, inner_width),
        ],
        axis=-1,
    )
    return (query_grad.astype(jnp.bfloat16).reshape(batches, query_count, inner_width), joined)


def fold_cols(extended):
    left_strip = extended[:, :, :RADIUS]
    right_strip = extended[:, :, extended.shape[2] - RADIUS :]
    middle = extended[:, :, RADIUS : extended.shape[2] - RADIUS]
    from_right = shifted(left_strip, "col", -1)
    from_left = shifted(right_strip, "col", 1)
    inner_cols = middle.shape[2]
    return (
        middle
        + jnp.pad(from_left, ((0, 0), (0, 0), (0, inner_cols - RADIUS), (0, 0)))
        + jnp.pad(from_right, ((0, 0), (0, 0), (inner_cols - RADIUS, 0), (0, 0)))
    )


def fold_rows(extended):
    upper_strip = extended[:, :RADIUS]
    lower_strip = extended[:, extended.shape[1] - RADIUS :]
    middle = extended[:, RADIUS : extended.shape[1] - RADIUS]
    from_below = shifted(upper_strip, "row", -1)
    from_above = shifted(lower_strip, "row", 1)
    inner_rows = middle.shape[1]
    return (
        middle
        + jnp.pad(from_above, ((0, 0), (0, inner_rows - RADIUS), (0, 0), (0, 0)))
        + jnp.pad(from_below, ((0, 0), (inner_rows - RADIUS, 0), (0, 0), (0, 0)))
    )


def local(inputs, norm_gain, w_query, w_keyvalue, w_output, out_grad):
    batches, tile_rows, tile_cols, model_width = inputs.shape
    ext_rows = tile_rows + 2 * RADIUS
    ext_cols = tile_cols + 2 * RADIUS
    standard, spread, normed = normalize(inputs, norm_gain)
    flat_norm = normed.reshape(-1, model_width)
    row_levels = lax.axis_size("row").bit_length() - 1
    row_groups = [[b] for b in range(row_levels)]
    full_query, full_keyvalue, full_output = gather_weights(
        w_query, w_keyvalue, w_output, row_groups[::-1]
    )
    inner_width = full_query.shape[1]
    queries = jnp.dot(flat_norm, full_query, preferred_element_type=jnp.float32).astype(
        jnp.bfloat16
    )
    queries = queries.reshape(batches, tile_rows * tile_cols, inner_width)
    keyvalue = jnp.dot(flat_norm, full_keyvalue, preferred_element_type=jnp.float32).astype(
        jnp.bfloat16
    )
    keyvalue = keyvalue.reshape(batches, tile_rows, tile_cols, 2 * inner_width)
    joined_ext = with_halo(
        jnp.concatenate([keyvalue, normed], axis=-1), (("row", 1), ("col", 2)), RADIUS
    )
    keyvalue_ext = joined_ext[..., : 2 * inner_width].reshape(
        batches, ext_rows * ext_cols, 2 * inner_width
    )
    normed_ext = joined_ext[..., 2 * inner_width :].reshape(-1, model_width)
    allowed = window_mask(
        lax.axis_index("row") * tile_rows,
        lax.axis_index("col") * tile_cols,
        tile_rows,
        tile_cols,
        tile_rows * lax.axis_size("row"),
        tile_cols * lax.axis_size("col"),
    )
    attended, soft, rounded = tile_forward(queries, keyvalue_ext, allowed)
    projected = jnp.dot(
        attended.reshape(-1, inner_width), full_output, preferred_element_type=jnp.float32
    )
    layer_out = (inputs.astype(jnp.float32) + projected.reshape(inputs.shape)).astype(jnp.bfloat16)
    flat_grad = out_grad.reshape(-1, model_width)
    inner_grad = lax.dot_general(
        flat_grad, full_output, (((1,), (1,)), ((), ())), preferred_element_type=jnp.float32
    ).astype(jnp.bfloat16)
    inner_grad = inner_grad.reshape(batches, tile_rows * tile_cols, inner_width)
    query_grad, keyvalue_part = tile_backward(queries, keyvalue_ext, soft, rounded, inner_grad)
    keyvalue_part = keyvalue_part.reshape(batches, ext_rows, ext_cols, 2 * inner_width)
    owned = fold_rows(fold_cols(keyvalue_part))
    token_grad = owned.astype(jnp.bfloat16).reshape(-1, 2 * inner_width)
    row_count, col_count = lax.axis_size("row"), lax.axis_size("col")
    col_levels = col_count.bit_length() - 1
    feature_part = model_width // row_count
    partial = lax.dot_general(
        normed_ext,
        keyvalue_part.reshape(-1, 2 * inner_width).astype(jnp.bfloat16),
        (((0,), (0,)), ((), ())),
        preferred_element_type=jnp.float32,
    )
    half = partial.shape[1] // 2
    own = axis_bit("col", 0)
    halves = partial.reshape(model_width, 2, half)
    pair_part = lax.dynamic_index_in_dim(halves, own, 1, keepdims=False) + partner_swap(
        lax.dynamic_index_in_dim(halves, 1 - own, 1, keepdims=False).astype(jnp.bfloat16),
        "col",
        1,
    ).astype(jnp.float32)
    rows_part = scatter_by_bits(
        pair_part.reshape(row_count, feature_part, half), "row", row_groups, narrow=1
    )[0]
    for bit in range(1, col_levels):
        rows_part = rows_part + partner_swap(rows_part, "col", 1 << bit)
    held = jnp.zeros((2,) + rows_part.shape, rows_part.dtype)
    held = lax.dynamic_update_slice(held, rows_part[None], (own, 0, 0))
    held = lax.dynamic_update_slice(held, partner_swap(rows_part, "col", 1)[None], (1 - own, 0, 0))
    keyvalue_grad = held.transpose(1, 0, 2).reshape(feature_part, -1)
    normed_grad = lax.dot_general(
        query_grad.reshape(-1, inner_width),
        full_query,
        (((1,), (1,)), ((), ())),
        preferred_element_type=jnp.float32,
    )
    normed_grad = normed_grad + lax.dot_general(
        token_grad, full_keyvalue, (((1,), (1,)), ((), ())), preferred_element_type=jnp.float32
    )
    gained = normed_grad.reshape(inputs.shape) * norm_gain
    in_grad = out_grad.astype(jnp.float32) + spread * (
        gained
        - jnp.mean(gained, axis=-1, keepdims=True)
        - standard * jnp.mean(gained * standard, axis=-1, keepdims=True)
    )
    return (layer_out, in_grad.astype(jnp.bfloat16), keyvalue_grad)


def solution(mesh):
    return jax.shard_map(
        local,
        mesh=mesh,
        in_specs=(
            P(None, "row", "col", None),
            P(),
            P("row", None),
            P("row", None),
            P("row", None),
            P(None, "row", "col", None),
        ),
        out_specs=(P(None, "row", "col", None), P(None, "row", "col", None), P("row", None)),
        check_vma=False,
    )
```

```python
import math

import jax
import jax.numpy as jnp
from jax import lax
from jax.sharding import PartitionSpec as P

HEADS = 8
RADIUS = 6


EPS = 1e-05
MASKED = -1e30


def shifted(value, axis, steps):
    count = lax.axis_size(axis)
    first, last = (max(0, -steps), min(count, count - steps))
    return lax.ppermute(value, axis, [(source, source + steps) for source in range(first, last)])


def with_halo(block, sides, width):
    for axis, dim in sides:
        count = lax.axis_size(axis)
        forward = [(i, i + 1) for i in range(count - 1)]
        backward = [(target, source) for source, target in forward]
        low = lax.ppermute(
            lax.slice_in_dim(block, block.shape[dim] - width, None, axis=dim), axis, forward
        )
        high = lax.ppermute(lax.slice_in_dim(block, 0, width, axis=dim), axis, backward)
        block = jnp.concatenate([low, block, high], axis=dim)
    return block


def partner_swap(value, axis, mask):
    count = lax.axis_size(axis)
    return lax.ppermute(value, axis, [(i, i ^ mask) for i in range(count)])


def axis_bit(axis, bit):
    return (lax.axis_index(axis) // (1 << bit)) % 2


def flips(group):
    for code in range(1, 1 << len(group)):
        yield [(code >> k) % 2 for k in range(len(group))]


def gather_by_bits(block, axis, groups, tie=None, tie_at=2):
    levels = lax.axis_size(axis).bit_length() - 1
    mine = [axis_bit(axis, bit) for bit in range(levels)]
    zero = [0] * block.ndim
    held = jnp.zeros((2,) * levels + block.shape, block.dtype)
    held = lax.dynamic_update_slice(
        held, block.reshape((1,) * levels + block.shape), mine[::-1] + zero
    )
    done = set()
    for step, group in enumerate(groups):
        start = [0 if b in done else mine[b] for b in range(levels)]
        size = [2 if b in done else 1 for b in range(levels)]
        region = lax.dynamic_slice(held, start[::-1] + zero, size[::-1] + list(block.shape))
        if tie is not None and step == tie_at:
            region, tie = lax.optimization_barrier((region, tie))
        arrived = []
        for flip in flips(group):
            mask = sum(f << b for f, b in zip(flip, group))
            place = list(start)
            for f, b in zip(flip, group):
                place[b] = (mine[b] + f) % 2
            arrived.append((partner_swap(region, axis, mask), place))
        for other, place in arrived:
            held = lax.dynamic_update_slice(held, other, place[::-1] + zero)
        done.update(group)
    held = held.reshape((-1,) + block.shape)
    return held if tie is None else (held, tie)


def scatter_by_bits(total, axis, groups):
    levels = lax.axis_size(axis).bit_length() - 1
    mine = [axis_bit(axis, bit) for bit in range(levels)]
    held = total.reshape((2,) * levels + (total.shape[0] // 2**levels,) + total.shape[1:])
    rest = [0] * (held.ndim - levels)
    for group in groups:
        size = [1 if b in group else held.shape[levels - 1 - b] for b in range(levels)]
        size = size[::-1] + list(held.shape[levels:])
        own = [mine[b] if b in group else 0 for b in range(levels)]
        summed = lax.dynamic_slice(held, own[::-1] + rest, size)
        for flip in flips(group):
            mask = sum(f << b for f, b in zip(flip, group))
            place = list(own)
            for f, b in zip(flip, group):
                place[b] = (mine[b] + f) % 2
            send = lax.dynamic_slice(held, place[::-1] + rest, size)
            summed = summed + partner_swap(send, axis, mask)
        held = summed
    return held.reshape(held.shape[levels:])


def gather_weights(w_query, w_keyvalue, w_output, row_groups, tie):
    rows, width = w_query.shape
    kv_pack = w_keyvalue.reshape(rows, 2, width).transpose(1, 0, 2).reshape(2 * rows, width)
    out_rows = w_output.shape[0]
    out_pack = w_output.reshape(out_rows, 2, width).transpose(1, 0, 2).reshape(2 * out_rows, width)
    qo_pack = jnp.concatenate([w_query, out_pack], axis=0)
    own = axis_bit("col", 0)
    packed = jnp.where(own == 0, kv_pack, qo_pack)
    fetched, tie = gather_by_bits(packed, "row", row_groups, tie=tie)
    held = jnp.zeros((2,) + fetched.shape, fetched.dtype)
    held = lax.dynamic_update_slice(held, fetched[None], (own, 0, 0, 0))
    held = lax.dynamic_update_slice(held, partner_swap(fetched, "col", 1)[None], (1 - own, 0, 0, 0))
    count = fetched.shape[0]
    kv = held[0].reshape(count, 2, rows, width).transpose(0, 2, 1, 3).reshape(count * rows, 2 * width)
    query = held[1, :, :rows].reshape(count * rows, width)
    output = held[1, :, rows:].reshape(count, 2, out_rows, width).transpose(0, 2, 1, 3)
    return query, kv, output.reshape(count * out_rows, 2 * width), tie


def normalize(inputs, norm_gain):
    values = inputs.astype(jnp.float32)
    center = values - jnp.mean(values, axis=-1, keepdims=True)
    spread = lax.rsqrt(jnp.mean(center * center, axis=-1, keepdims=True) + EPS)
    standard = center * spread
    return (standard, spread, (standard * norm_gain).astype(jnp.bfloat16))


def window_mask(row_start, col_start, tile_rows, tile_cols, height, map_width):
    ext_rows = tile_rows + 2 * RADIUS
    ext_cols = tile_cols + 2 * RADIUS
    query_pos = jnp.arange(tile_rows * tile_cols, dtype=jnp.int32)
    query_row = query_pos // tile_cols
    query_col = query_pos % tile_cols
    ext_pos = jnp.arange(ext_rows * ext_cols, dtype=jnp.int32)
    ext_row = ext_pos // ext_cols
    ext_col = ext_pos % ext_cols
    nearby = (jnp.abs(ext_row[None, :] - RADIUS - query_row[:, None]) <= RADIUS) & (
        jnp.abs(ext_col[None, :] - RADIUS - query_col[:, None]) <= RADIUS
    )
    global_row = row_start + ext_row - RADIUS
    global_col = col_start + ext_col - RADIUS
    inside = (
        (global_row >= 0) & (global_row < height) & (global_col >= 0) & (global_col < map_width)
    )
    return nearby & inside[None, :]


def tile_forward(queries, keyvalue_ext, allowed):
    batches, query_count, inner_width = queries.shape
    head_size = inner_width // HEADS
    query_heads = queries.reshape(batches, query_count, HEADS, head_size)
    key_heads = keyvalue_ext[:, :, :inner_width].reshape(batches, -1, HEADS, head_size)
    value_heads = keyvalue_ext[:, :, inner_width:].reshape(batches, -1, HEADS, head_size)
    scores = jnp.einsum(
        "bqhd,bkhd->bhqk", query_heads, key_heads, preferred_element_type=jnp.float32
    ) / math.sqrt(head_size)
    scores = jnp.where(allowed, scores, MASKED)
    row_max = jnp.max(scores, axis=-1, keepdims=True)
    exponent = jnp.exp(scores - row_max)
    soft = exponent / jnp.sum(exponent, axis=-1, keepdims=True)
    rounded = soft.astype(jnp.bfloat16)
    attended = jnp.einsum(
        "bhqk,bkhd->bqhd", rounded, value_heads, preferred_element_type=jnp.float32
    )
    return (attended.astype(jnp.bfloat16).reshape(batches, query_count, inner_width), soft, rounded)


def tile_backward(queries, keyvalue_ext, soft, rounded, inner_grad):
    batches, query_count, inner_width = queries.shape
    head_size = inner_width // HEADS
    query_heads = queries.reshape(batches, query_count, HEADS, head_size)
    key_heads = keyvalue_ext[:, :, :inner_width].reshape(batches, -1, HEADS, head_size)
    value_heads = keyvalue_ext[:, :, inner_width:].reshape(batches, -1, HEADS, head_size)
    grad_heads = inner_grad.reshape(batches, query_count, HEADS, head_size)
    prob_grad = jnp.einsum(
        "bqhd,bkhd->bhqk", grad_heads, value_heads, preferred_element_type=jnp.float32
    )
    row_dot = jnp.sum(soft * prob_grad, axis=-1, keepdims=True)
    score_grad = (soft * (prob_grad - row_dot) / math.sqrt(head_size)).astype(jnp.bfloat16)
    query_grad = jnp.einsum(
        "bhqk,bkhd->bqhd", score_grad, key_heads, preferred_element_type=jnp.float32
    )
    key_grad = jnp.einsum(
        "bhqk,bqhd->bkhd", score_grad, query_heads, preferred_element_type=jnp.float32
    )
    value_grad = jnp.einsum(
        "bhqk,bqhd->bkhd", rounded, grad_heads, preferred_element_type=jnp.float32
    )
    ext_count = key_grad.shape[1]
    joined = jnp.concatenate(
        [
            key_grad.reshape(batches, ext_count, inner_width),
            value_grad.reshape(batches, ext_count, inner_width),
        ],
        axis=-1,
    )
    return (query_grad.astype(jnp.bfloat16).reshape(batches, query_count, inner_width), joined)


def fold_cols(extended):
    left_strip = extended[:, :, :RADIUS]
    right_strip = extended[:, :, extended.shape[2] - RADIUS :]
    middle = extended[:, :, RADIUS : extended.shape[2] - RADIUS]
    from_right = shifted(left_strip, "col", -1)
    from_left = shifted(right_strip, "col", 1)
    inner_cols = middle.shape[2]
    return (
        middle
        + jnp.pad(from_left, ((0, 0), (0, 0), (0, inner_cols - RADIUS), (0, 0)))
        + jnp.pad(from_right, ((0, 0), (0, 0), (inner_cols - RADIUS, 0), (0, 0)))
    )


def fold_rows(extended):
    upper_strip = extended[:, :RADIUS]
    lower_strip = extended[:, extended.shape[1] - RADIUS :]
    middle = extended[:, RADIUS : extended.shape[1] - RADIUS]
    from_below = shifted(upper_strip, "row", -1)
    from_above = shifted(lower_strip, "row", 1)
    inner_rows = middle.shape[1]
    return (
        middle
        + jnp.pad(from_above, ((0, 0), (0, inner_rows - RADIUS), (0, 0), (0, 0)))
        + jnp.pad(from_below, ((0, 0), (inner_rows - RADIUS, 0), (0, 0), (0, 0)))
    )


def local(inputs, norm_gain, w_query, w_keyvalue, w_output, out_grad):
    batches, tile_rows, tile_cols, model_width = inputs.shape
    ext_rows = tile_rows + 2 * RADIUS
    ext_cols = tile_cols + 2 * RADIUS
    standard, spread, normed = normalize(inputs, norm_gain)
    flat_norm = normed.reshape(-1, model_width)
    normed_ext = with_halo(normed, (("row", 1), ("col", 2)), RADIUS).reshape(-1, model_width)
    row_levels = lax.axis_size("row").bit_length() - 1
    row_groups = [[b] for b in range(row_levels)]
    full_query, full_keyvalue, full_output, normed_ext = gather_weights(
        w_query, w_keyvalue, w_output, row_groups[::-1], normed_ext
    )
    inner_width = full_query.shape[1]
    queries = jnp.dot(flat_norm, full_query, preferred_element_type=jnp.float32).astype(
        jnp.bfloat16
    )
    queries = queries.reshape(batches, tile_rows * tile_cols, inner_width)
    keyvalue_ext = jnp.dot(normed_ext, full_keyvalue, preferred_element_type=jnp.float32)
    keyvalue_ext = keyvalue_ext.astype(jnp.bfloat16).reshape(
        batches, ext_rows * ext_cols, 2 * inner_width
    )
    allowed = window_mask(
        lax.axis_index("row") * tile_rows,
        lax.axis_index("col") * tile_cols,
        tile_rows,
        tile_cols,
        tile_rows * lax.axis_size("row"),
        tile_cols * lax.axis_size("col"),
    )
    attended, soft, rounded = tile_forward(queries, keyvalue_ext, allowed)
    projected = jnp.dot(
        attended.reshape(-1, inner_width), full_output, preferred_element_type=jnp.float32
    )
    layer_out = (inputs.astype(jnp.float32) + projected.reshape(inputs.shape)).astype(jnp.bfloat16)
    flat_grad = out_grad.reshape(-1, model_width)
    inner_grad = lax.dot_general(
        flat_grad, full_output, (((1,), (1,)), ((), ())), preferred_element_type=jnp.float32
    ).astype(jnp.bfloat16)
    inner_grad = inner_grad.reshape(batches, tile_rows * tile_cols, inner_width)
    query_grad, keyvalue_part = tile_backward(queries, keyvalue_ext, soft, rounded, inner_grad)
    keyvalue_part = keyvalue_part.reshape(batches, ext_rows, ext_cols, 2 * inner_width)
    owned = fold_rows(fold_cols(keyvalue_part))
    token_grad = owned.astype(jnp.bfloat16).reshape(-1, 2 * inner_width)
    row_count, col_count = lax.axis_size("row"), lax.axis_size("col")
    col_levels = col_count.bit_length() - 1
    feature_part = model_width // row_count
    partial = lax.dot_general(
        normed_ext,
        keyvalue_part.reshape(-1, 2 * inner_width).astype(jnp.bfloat16),
        (((0,), (0,)), ((), ())),
        preferred_element_type=jnp.float32,
    )
    half = partial.shape[1] // 2
    own = axis_bit("col", 0)
    halves = partial.reshape(model_width, 2, half)
    pair_part = lax.dynamic_index_in_dim(halves, own, 1, keepdims=False) + partner_swap(
        lax.dynamic_index_in_dim(halves, 1 - own, 1, keepdims=False), "col", 1
    )
    rows_part = scatter_by_bits(
        pair_part.reshape(row_count, feature_part, half), "row", row_groups
    )[0]
    for bit in range(1, col_levels):
        rows_part = rows_part + partner_swap(rows_part, "col", 1 << bit)
    held = jnp.zeros((2,) + rows_part.shape, rows_part.dtype)
    held = lax.dynamic_update_slice(held, rows_part[None], (own, 0, 0))
    held = lax.dynamic_update_slice(held, partner_swap(rows_part, "col", 1)[None], (1 - own, 0, 0))
    keyvalue_grad = held.transpose(1, 0, 2).reshape(feature_part, -1)
    normed_grad = lax.dot_general(
        query_grad.reshape(-1, inner_width),
        full_query,
        (((1,), (1,)), ((), ())),
        preferred_element_type=jnp.float32,
    )
    normed_grad = normed_grad + lax.dot_general(
        token_grad, full_keyvalue, (((1,), (1,)), ((), ())), preferred_element_type=jnp.float32
    )
    gained = normed_grad.reshape(inputs.shape) * norm_gain
    in_grad = out_grad.astype(jnp.float32) + spread * (
        gained
        - jnp.mean(gained, axis=-1, keepdims=True)
        - standard * jnp.mean(gained * standard, axis=-1, keepdims=True)
    )
    return (layer_out, in_grad.astype(jnp.bfloat16), keyvalue_grad)


def solution(mesh):
    return jax.shard_map(
        local,
        mesh=mesh,
        in_specs=(
            P(None, "row", "col", None),
            P(),
            P("row", None),
            P("row", None),
            P("row", None),
            P(None, "row", "col", None),
        ),
        out_specs=(P(None, "row", "col", None), P(None, "row", "col", None), P("row", None)),
        check_vma=False,
    )
```

```python
import math

import jax
import jax.numpy as jnp
from jax import lax
from jax.sharding import PartitionSpec as P

HEADS = 8
RADIUS = 6


EPS = 1e-05
MASKED = -1e30


def shifted(value, axis, steps):
    count = lax.axis_size(axis)
    first, last = (max(0, -steps), min(count, count - steps))
    return lax.ppermute(value, axis, [(source, source + steps) for source in range(first, last)])


def with_halo(block, sides, width):
    for axis, dim in sides:
        count = lax.axis_size(axis)
        forward = [(i, i + 1) for i in range(count - 1)]
        backward = [(target, source) for source, target in forward]
        low = lax.ppermute(
            lax.slice_in_dim(block, block.shape[dim] - width, None, axis=dim), axis, forward
        )
        high = lax.ppermute(lax.slice_in_dim(block, 0, width, axis=dim), axis, backward)
        block = jnp.concatenate([low, block, high], axis=dim)
    return block


def partner_swap(value, axis, mask):
    count = lax.axis_size(axis)
    return lax.ppermute(value, axis, [(i, i ^ mask) for i in range(count)])


def axis_bit(axis, bit):
    return (lax.axis_index(axis) // (1 << bit)) % 2


def flips(group):
    for code in range(1, 1 << len(group)):
        yield [(code >> k) % 2 for k in range(len(group))]


def gather_by_bits(block, axis, groups, tie=None, tie_at=2):
    levels = lax.axis_size(axis).bit_length() - 1
    mine = [axis_bit(axis, bit) for bit in range(levels)]
    zero = [0] * block.ndim
    held = jnp.zeros((2,) * levels + block.shape, block.dtype)
    held = lax.dynamic_update_slice(
        held, block.reshape((1,) * levels + block.shape), mine[::-1] + zero
    )
    done = set()
    for step, group in enumerate(groups):
        start = [0 if b in done else mine[b] for b in range(levels)]
        size = [2 if b in done else 1 for b in range(levels)]
        region = lax.dynamic_slice(held, start[::-1] + zero, size[::-1] + list(block.shape))
        if tie is not None and step == tie_at:
            region, tie = lax.optimization_barrier((region, tie))
        arrived = []
        for flip in flips(group):
            mask = sum(f << b for f, b in zip(flip, group))
            place = list(start)
            for f, b in zip(flip, group):
                place[b] = (mine[b] + f) % 2
            arrived.append((partner_swap(region, axis, mask), place))
        for other, place in arrived:
            held = lax.dynamic_update_slice(held, other, place[::-1] + zero)
        done.update(group)
    held = held.reshape((-1,) + block.shape)
    return held if tie is None else (held, tie)


def scatter_by_bits(total, axis, groups):
    levels = lax.axis_size(axis).bit_length() - 1
    mine = [axis_bit(axis, bit) for bit in range(levels)]
    held = total.reshape((2,) * levels + (total.shape[0] // 2**levels,) + total.shape[1:])
    rest = [0] * (held.ndim - levels)
    for group in groups:
        size = [1 if b in group else held.shape[levels - 1 - b] for b in range(levels)]
        size = size[::-1] + list(held.shape[levels:])
        own = [mine[b] if b in group else 0 for b in range(levels)]
        summed = lax.dynamic_slice(held, own[::-1] + rest, size)
        for flip in flips(group):
            mask = sum(f << b for f, b in zip(flip, group))
            place = list(own)
            for f, b in zip(flip, group):
                place[b] = (mine[b] + f) % 2
            send = lax.dynamic_slice(held, place[::-1] + rest, size)
            summed = summed + partner_swap(send, axis, mask)
        held = summed
    return held.reshape(held.shape[levels:])


def gather_weights(w_query, w_keyvalue, w_output, row_groups, tie):
    rows, width = w_query.shape
    kv_rows, kv_width = w_keyvalue.shape
    out_rows = w_output.shape[0]
    qo_pack = jnp.concatenate([w_query.reshape(-1, kv_width), w_output], axis=0)
    own = axis_bit("col", 0)
    packed = jnp.where(own == 0, w_keyvalue, qo_pack)
    fetched, tie = gather_by_bits(packed, "row", row_groups, tie=tie)
    held = jnp.zeros((2,) + fetched.shape, fetched.dtype)
    held = lax.dynamic_update_slice(held, fetched[None], (own, 0, 0, 0))
    held = lax.dynamic_update_slice(held, partner_swap(fetched, "col", 1)[None], (1 - own, 0, 0, 0))
    count = fetched.shape[0]
    query_rows = kv_rows - out_rows
    kv = held[0].reshape(count * kv_rows, kv_width)
    query = held[1, :, :query_rows].reshape(count * rows, width)
    output = held[1, :, query_rows:].reshape(count * out_rows, kv_width)
    return query, kv, output, tie


def normalize(inputs, norm_gain):
    values = inputs.astype(jnp.float32)
    center = values - jnp.mean(values, axis=-1, keepdims=True)
    spread = lax.rsqrt(jnp.mean(center * center, axis=-1, keepdims=True) + EPS)
    standard = center * spread
    return (standard, spread, (standard * norm_gain).astype(jnp.bfloat16))


def window_mask(row_start, col_start, tile_rows, tile_cols, height, map_width):
    ext_rows = tile_rows + 2 * RADIUS
    ext_cols = tile_cols + 2 * RADIUS
    query_pos = jnp.arange(tile_rows * tile_cols, dtype=jnp.int32)
    query_row = query_pos // tile_cols
    query_col = query_pos % tile_cols
    ext_pos = jnp.arange(ext_rows * ext_cols, dtype=jnp.int32)
    ext_row = ext_pos // ext_cols
    ext_col = ext_pos % ext_cols
    nearby = (jnp.abs(ext_row[None, :] - RADIUS - query_row[:, None]) <= RADIUS) & (
        jnp.abs(ext_col[None, :] - RADIUS - query_col[:, None]) <= RADIUS
    )
    global_row = row_start + ext_row - RADIUS
    global_col = col_start + ext_col - RADIUS
    inside = (
        (global_row >= 0) & (global_row < height) & (global_col >= 0) & (global_col < map_width)
    )
    return nearby & inside[None, :]


def tile_forward(queries, keyvalue_ext, allowed):
    batches, query_count, inner_width = queries.shape
    head_size = inner_width // HEADS
    query_heads = queries.reshape(batches, query_count, HEADS, head_size)
    key_heads = keyvalue_ext[:, :, :inner_width].reshape(batches, -1, HEADS, head_size)
    value_heads = keyvalue_ext[:, :, inner_width:].reshape(batches, -1, HEADS, head_size)
    scores = jnp.einsum(
        "bqhd,bkhd->bhqk", query_heads, key_heads, preferred_element_type=jnp.float32
    ) / math.sqrt(head_size)
    scores = jnp.where(allowed, scores, MASKED)
    row_max = jnp.max(scores, axis=-1, keepdims=True)
    exponent = jnp.exp(scores - row_max)
    soft = exponent / jnp.sum(exponent, axis=-1, keepdims=True)
    rounded = soft.astype(jnp.bfloat16)
    attended = jnp.einsum(
        "bhqk,bkhd->bqhd", rounded, value_heads, preferred_element_type=jnp.float32
    )
    return (attended.astype(jnp.bfloat16).reshape(batches, query_count, inner_width), soft, rounded)


def tile_backward(queries, keyvalue_ext, soft, rounded, inner_grad):
    batches, query_count, inner_width = queries.shape
    head_size = inner_width // HEADS
    query_heads = queries.reshape(batches, query_count, HEADS, head_size)
    key_heads = keyvalue_ext[:, :, :inner_width].reshape(batches, -1, HEADS, head_size)
    value_heads = keyvalue_ext[:, :, inner_width:].reshape(batches, -1, HEADS, head_size)
    grad_heads = inner_grad.reshape(batches, query_count, HEADS, head_size)
    prob_grad = jnp.einsum(
        "bqhd,bkhd->bhqk", grad_heads, value_heads, preferred_element_type=jnp.float32
    )
    row_dot = jnp.sum(soft * prob_grad, axis=-1, keepdims=True)
    score_grad = (soft * (prob_grad - row_dot) / math.sqrt(head_size)).astype(jnp.bfloat16)
    query_grad = jnp.einsum(
        "bhqk,bkhd->bqhd", score_grad, key_heads, preferred_element_type=jnp.float32
    )
    key_grad = jnp.einsum(
        "bhqk,bqhd->bkhd", score_grad, query_heads, preferred_element_type=jnp.float32
    )
    value_grad = jnp.einsum(
        "bhqk,bqhd->bkhd", rounded, grad_heads, preferred_element_type=jnp.float32
    )
    ext_count = key_grad.shape[1]
    joined = jnp.concatenate(
        [
            key_grad.reshape(batches, ext_count, inner_width),
            value_grad.reshape(batches, ext_count, inner_width),
        ],
        axis=-1,
    )
    return (query_grad.astype(jnp.bfloat16).reshape(batches, query_count, inner_width), joined)


def fold_cols(extended):
    left_strip = extended[:, :, :RADIUS]
    right_strip = extended[:, :, extended.shape[2] - RADIUS :]
    middle = extended[:, :, RADIUS : extended.shape[2] - RADIUS]
    from_right = shifted(left_strip, "col", -1)
    from_left = shifted(right_strip, "col", 1)
    inner_cols = middle.shape[2]
    return (
        middle
        + jnp.pad(from_left, ((0, 0), (0, 0), (0, inner_cols - RADIUS), (0, 0)))
        + jnp.pad(from_right, ((0, 0), (0, 0), (inner_cols - RADIUS, 0), (0, 0)))
    )


def fold_rows(extended):
    upper_strip = extended[:, :RADIUS]
    lower_strip = extended[:, extended.shape[1] - RADIUS :]
    middle = extended[:, RADIUS : extended.shape[1] - RADIUS]
    from_below = shifted(upper_strip, "row", -1)
    from_above = shifted(lower_strip, "row", 1)
    inner_rows = middle.shape[1]
    return (
        middle
        + jnp.pad(from_above, ((0, 0), (0, inner_rows - RADIUS), (0, 0), (0, 0)))
        + jnp.pad(from_below, ((0, 0), (inner_rows - RADIUS, 0), (0, 0), (0, 0)))
    )


def local(inputs, norm_gain, w_query, w_keyvalue, w_output, out_grad):
    batches, tile_rows, tile_cols, model_width = inputs.shape
    ext_rows = tile_rows + 2 * RADIUS
    ext_cols = tile_cols + 2 * RADIUS
    standard, spread, normed = normalize(inputs, norm_gain)
    flat_norm = normed.reshape(-1, model_width)
    normed_ext = with_halo(normed, (("row", 1), ("col", 2)), RADIUS).reshape(-1, model_width)
    row_levels = lax.axis_size("row").bit_length() - 1
    row_groups = [[b] for b in range(row_levels)]
    full_query, full_keyvalue, full_output, normed_ext = gather_weights(
        w_query, w_keyvalue, w_output, row_groups[::-1], normed_ext
    )
    inner_width = full_query.shape[1]
    queries = jnp.dot(flat_norm, full_query, preferred_element_type=jnp.float32).astype(
        jnp.bfloat16
    )
    queries = queries.reshape(batches, tile_rows * tile_cols, inner_width)
    keyvalue_ext = jnp.dot(normed_ext, full_keyvalue, preferred_element_type=jnp.float32)
    keyvalue_ext = keyvalue_ext.astype(jnp.bfloat16).reshape(
        batches, ext_rows * ext_cols, 2 * inner_width
    )
    allowed = window_mask(
        lax.axis_index("row") * tile_rows,
        lax.axis_index("col") * tile_cols,
        tile_rows,
        tile_cols,
        tile_rows * lax.axis_size("row"),
        tile_cols * lax.axis_size("col"),
    )
    attended, soft, rounded = tile_forward(queries, keyvalue_ext, allowed)
    projected = jnp.dot(
        attended.reshape(-1, inner_width), full_output, preferred_element_type=jnp.float32
    )
    layer_out = (inputs.astype(jnp.float32) + projected.reshape(inputs.shape)).astype(jnp.bfloat16)
    flat_grad = out_grad.reshape(-1, model_width)
    inner_grad = lax.dot_general(
        flat_grad, full_output, (((1,), (1,)), ((), ())), preferred_element_type=jnp.float32
    ).astype(jnp.bfloat16)
    inner_grad = inner_grad.reshape(batches, tile_rows * tile_cols, inner_width)
    query_grad, keyvalue_part = tile_backward(queries, keyvalue_ext, soft, rounded, inner_grad)
    keyvalue_part = keyvalue_part.reshape(batches, ext_rows, ext_cols, 2 * inner_width)
    owned = fold_rows(fold_cols(keyvalue_part))
    token_grad = owned.astype(jnp.bfloat16).reshape(-1, 2 * inner_width)
    row_count, col_count = lax.axis_size("row"), lax.axis_size("col")
    col_levels = col_count.bit_length() - 1
    feature_part = model_width // row_count
    partial = lax.dot_general(
        normed_ext,
        keyvalue_part.reshape(-1, 2 * inner_width).astype(jnp.bfloat16),
        (((0,), (0,)), ((), ())),
        preferred_element_type=jnp.float32,
    )
    half = partial.shape[1] // 2
    own = axis_bit("col", 0)
    halves = partial.reshape(model_width, 2, half)
    pair_part = lax.dynamic_index_in_dim(halves, own, 1, keepdims=False) + partner_swap(
        lax.dynamic_index_in_dim(halves, 1 - own, 1, keepdims=False), "col", 1
    )
    rows_part = scatter_by_bits(
        pair_part.reshape(row_count, feature_part, half), "row", row_groups
    )[0]
    for bit in range(1, col_levels):
        rows_part = rows_part + partner_swap(rows_part, "col", 1 << bit)
    held = jnp.zeros((2,) + rows_part.shape, rows_part.dtype)
    held = lax.dynamic_update_slice(held, rows_part[None], (own, 0, 0))
    held = lax.dynamic_update_slice(held, partner_swap(rows_part, "col", 1)[None], (1 - own, 0, 0))
    keyvalue_grad = held.transpose(1, 0, 2).reshape(feature_part, -1)
    normed_grad = lax.dot_general(
        query_grad.reshape(-1, inner_width),
        full_query,
        (((1,), (1,)), ((), ())),
        preferred_element_type=jnp.float32,
    )
    normed_grad = normed_grad + lax.dot_general(
        token_grad, full_keyvalue, (((1,), (1,)), ((), ())), preferred_element_type=jnp.float32
    )
    gained = normed_grad.reshape(inputs.shape) * norm_gain
    in_grad = out_grad.astype(jnp.float32) + spread * (
        gained
        - jnp.mean(gained, axis=-1, keepdims=True)
        - standard * jnp.mean(gained * standard, axis=-1, keepdims=True)
    )
    return (layer_out, in_grad.astype(jnp.bfloat16), keyvalue_grad)


def solution(mesh):
    return jax.shard_map(
        local,
        mesh=mesh,
        in_specs=(
            P(None, "row", "col", None),
            P(),
            P("row", None),
            P("row", None),
            P("row", None),
            P(None, "row", "col", None),
        ),
        out_specs=(P(None, "row", "col", None), P(None, "row", "col", None), P("row", None)),
        check_vma=False,
    )
```

```python
import math

import jax
import jax.numpy as jnp
from jax import lax
from jax.sharding import PartitionSpec as P

HEADS = 8
RADIUS = 6


EPS = 1e-05
MASKED = -1e30


def shifted(value, axis, steps):
    count = lax.axis_size(axis)
    first, last = (max(0, -steps), min(count, count - steps))
    return lax.ppermute(value, axis, [(source, source + steps) for source in range(first, last)])


def with_halo(block, sides, width):
    for axis, dim in sides:
        count = lax.axis_size(axis)
        forward = [(i, i + 1) for i in range(count - 1)]
        backward = [(target, source) for source, target in forward]
        low = lax.ppermute(
            lax.slice_in_dim(block, block.shape[dim] - width, None, axis=dim), axis, forward
        )
        high = lax.ppermute(lax.slice_in_dim(block, 0, width, axis=dim), axis, backward)
        block = jnp.concatenate([low, block, high], axis=dim)
    return block


def partner_swap(value, axis, mask):
    count = lax.axis_size(axis)
    return lax.ppermute(value, axis, [(i, i ^ mask) for i in range(count)])


def axis_bit(axis, bit):
    return (lax.axis_index(axis) // (1 << bit)) % 2


def flips(group):
    for code in range(1, 1 << len(group)):
        yield [(code >> k) % 2 for k in range(len(group))]


def gather_by_bits(block, axis, groups, tie=None, tie_at=2):
    levels = lax.axis_size(axis).bit_length() - 1
    mine = [axis_bit(axis, bit) for bit in range(levels)]
    zero = [0] * block.ndim
    held = jnp.zeros((2,) * levels + block.shape, block.dtype)
    held = lax.dynamic_update_slice(
        held, block.reshape((1,) * levels + block.shape), mine[::-1] + zero
    )
    done = set()
    for step, group in enumerate(groups):
        start = [0 if b in done else mine[b] for b in range(levels)]
        size = [2 if b in done else 1 for b in range(levels)]
        region = lax.dynamic_slice(held, start[::-1] + zero, size[::-1] + list(block.shape))
        if tie is not None and step == tie_at:
            region, tie = lax.optimization_barrier((region, tie))
        arrived = []
        for flip in flips(group):
            mask = sum(f << b for f, b in zip(flip, group))
            place = list(start)
            for f, b in zip(flip, group):
                place[b] = (mine[b] + f) % 2
            arrived.append((partner_swap(region, axis, mask), place))
        for other, place in arrived:
            held = lax.dynamic_update_slice(held, other, place[::-1] + zero)
        done.update(group)
    held = held.reshape((-1,) + block.shape)
    return held if tie is None else (held, tie)


def scatter_by_bits(total, axis, groups):
    levels = lax.axis_size(axis).bit_length() - 1
    mine = [axis_bit(axis, bit) for bit in range(levels)]
    held = total.reshape((2,) * levels + (total.shape[0] // 2**levels,) + total.shape[1:])
    rest = [0] * (held.ndim - levels)
    for group in groups:
        size = [1 if b in group else held.shape[levels - 1 - b] for b in range(levels)]
        size = size[::-1] + list(held.shape[levels:])
        own = [mine[b] if b in group else 0 for b in range(levels)]
        summed = lax.dynamic_slice(held, own[::-1] + rest, size)
        for flip in flips(group):
            mask = sum(f << b for f, b in zip(flip, group))
            place = list(own)
            for f, b in zip(flip, group):
                place[b] = (mine[b] + f) % 2
            send = lax.dynamic_slice(held, place[::-1] + rest, size)
            summed = summed + partner_swap(send, axis, mask)
        held = summed
    return held.reshape(held.shape[levels:])


def gather_weights(w_query, w_keyvalue, w_output, row_groups, tie):
    rows, width = w_query.shape
    kv_rows, kv_width = w_keyvalue.shape
    out_rows = w_output.shape[0]
    qo_pack = jnp.concatenate([w_query.reshape(-1, kv_width), w_output], axis=0)
    own = axis_bit("col", 0)
    packed = jnp.where(own == 0, w_keyvalue, qo_pack)
    fetched, tie = gather_by_bits(packed, "row", row_groups, tie=tie)
    held = jnp.zeros((2,) + fetched.shape, fetched.dtype)
    held = lax.dynamic_update_slice(held, fetched[None], (own, 0, 0, 0))
    held = lax.dynamic_update_slice(held, partner_swap(fetched, "col", 1)[None], (1 - own, 0, 0, 0))
    count = fetched.shape[0]
    query_rows = kv_rows - out_rows
    kv = held[0].reshape(count * kv_rows, kv_width)
    query = held[1, :, :query_rows].reshape(count * rows, width)
    output = held[1, :, query_rows:].reshape(count * out_rows, kv_width)
    return query, kv, output, tie


def normalize(inputs, norm_gain):
    values = inputs.astype(jnp.float32)
    center = values - jnp.mean(values, axis=-1, keepdims=True)
    spread = lax.rsqrt(jnp.mean(center * center, axis=-1, keepdims=True) + EPS)
    standard = center * spread
    return (standard, spread, (standard * norm_gain).astype(jnp.bfloat16))


def window_mask(row_start, col_start, tile_rows, tile_cols, height, map_width):
    ext_rows = tile_rows + 2 * RADIUS
    ext_cols = tile_cols + 2 * RADIUS
    query_pos = jnp.arange(tile_rows * tile_cols, dtype=jnp.int32)
    query_row = query_pos // tile_cols
    query_col = query_pos % tile_cols
    ext_pos = jnp.arange(ext_rows * ext_cols, dtype=jnp.int32)
    ext_row = ext_pos // ext_cols
    ext_col = ext_pos % ext_cols
    nearby = (jnp.abs(ext_row[None, :] - RADIUS - query_row[:, None]) <= RADIUS) & (
        jnp.abs(ext_col[None, :] - RADIUS - query_col[:, None]) <= RADIUS
    )
    global_row = row_start + ext_row - RADIUS
    global_col = col_start + ext_col - RADIUS
    inside = (
        (global_row >= 0) & (global_row < height) & (global_col >= 0) & (global_col < map_width)
    )
    return nearby & inside[None, :]


def tile_forward(queries, keyvalue_ext, allowed):
    batches, query_count, inner_width = queries.shape
    head_size = inner_width // HEADS
    query_heads = queries.reshape(batches, query_count, HEADS, head_size)
    key_heads = keyvalue_ext[:HEADS]
    value_heads = keyvalue_ext[HEADS:]
    scores = jnp.einsum(
        "bqhd,hkd->bhqk", query_heads, key_heads, preferred_element_type=jnp.float32
    ) / math.sqrt(head_size)
    scores = jnp.where(allowed, scores, MASKED)
    row_max = jnp.max(scores, axis=-1, keepdims=True)
    exponent = jnp.exp(scores - row_max)
    soft = exponent / jnp.sum(exponent, axis=-1, keepdims=True)
    rounded = soft.astype(jnp.bfloat16)
    attended = jnp.einsum(
        "bhqk,hkd->bqhd", rounded, value_heads, preferred_element_type=jnp.float32
    )
    return (attended.astype(jnp.bfloat16).reshape(batches, query_count, inner_width), soft, rounded)


def tile_backward(queries, keyvalue_ext, soft, rounded, inner_grad):
    batches, query_count, inner_width = queries.shape
    head_size = inner_width // HEADS
    query_heads = queries.reshape(batches, query_count, HEADS, head_size)
    key_heads = keyvalue_ext[:HEADS]
    value_heads = keyvalue_ext[HEADS:]
    grad_heads = inner_grad.reshape(batches, query_count, HEADS, head_size)
    prob_grad = jnp.einsum(
        "bqhd,hkd->bhqk", grad_heads, value_heads, preferred_element_type=jnp.float32
    )
    row_dot = jnp.sum(soft * prob_grad, axis=-1, keepdims=True)
    score_grad = (soft * (prob_grad - row_dot) / math.sqrt(head_size)).astype(jnp.bfloat16)
    query_grad = jnp.einsum(
        "bhqk,hkd->bqhd", score_grad, key_heads, preferred_element_type=jnp.float32
    )
    key_grad = jnp.einsum(
        "bhqk,bqhd->bkhd", score_grad, query_heads, preferred_element_type=jnp.float32
    )
    value_grad = jnp.einsum(
        "bhqk,bqhd->bkhd", rounded, grad_heads, preferred_element_type=jnp.float32
    )
    ext_count = key_grad.shape[1]
    joined = jnp.concatenate(
        [
            key_grad.reshape(batches, ext_count, inner_width),
            value_grad.reshape(batches, ext_count, inner_width),
        ],
        axis=-1,
    )
    return (query_grad.astype(jnp.bfloat16).reshape(batches, query_count, inner_width), joined)


def fold_cols(extended):
    left_strip = extended[:, :, :RADIUS]
    right_strip = extended[:, :, extended.shape[2] - RADIUS :]
    middle = extended[:, :, RADIUS : extended.shape[2] - RADIUS]
    from_right = shifted(left_strip, "col", -1)
    from_left = shifted(right_strip, "col", 1)
    inner_cols = middle.shape[2]
    return (
        middle
        + jnp.pad(from_left, ((0, 0), (0, 0), (0, inner_cols - RADIUS), (0, 0)))
        + jnp.pad(from_right, ((0, 0), (0, 0), (inner_cols - RADIUS, 0), (0, 0)))
    )


def fold_rows(extended):
    upper_strip = extended[:, :RADIUS]
    lower_strip = extended[:, extended.shape[1] - RADIUS :]
    middle = extended[:, RADIUS : extended.shape[1] - RADIUS]
    from_below = shifted(upper_strip, "row", -1)
    from_above = shifted(lower_strip, "row", 1)
    inner_rows = middle.shape[1]
    return (
        middle
        + jnp.pad(from_above, ((0, 0), (0, inner_rows - RADIUS), (0, 0), (0, 0)))
        + jnp.pad(from_below, ((0, 0), (inner_rows - RADIUS, 0), (0, 0), (0, 0)))
    )


def local(inputs, norm_gain, w_query, w_keyvalue, w_output, out_grad):
    batches, tile_rows, tile_cols, model_width = inputs.shape
    ext_rows = tile_rows + 2 * RADIUS
    ext_cols = tile_cols + 2 * RADIUS
    standard, spread, normed = normalize(inputs, norm_gain)
    flat_norm = normed.reshape(-1, model_width)
    normed_ext = with_halo(normed, (("row", 1), ("col", 2)), RADIUS).reshape(-1, model_width)
    row_levels = lax.axis_size("row").bit_length() - 1
    row_groups = [[b] for b in range(row_levels)]
    full_query, full_keyvalue, full_output, normed_ext = gather_weights(
        w_query, w_keyvalue, w_output, row_groups[::-1], normed_ext
    )
    inner_width = full_query.shape[1]
    queries = jnp.dot(flat_norm, full_query, preferred_element_type=jnp.float32).astype(
        jnp.bfloat16
    )
    queries = queries.reshape(batches, tile_rows * tile_cols, inner_width)
    keyvalue_ext = jnp.einsum(
        "tf,fhd->htd",
        normed_ext,
        full_keyvalue.reshape(model_width, 2 * HEADS, -1),
        preferred_element_type=jnp.float32,
    ).astype(jnp.bfloat16)
    allowed = window_mask(
        lax.axis_index("row") * tile_rows,
        lax.axis_index("col") * tile_cols,
        tile_rows,
        tile_cols,
        tile_rows * lax.axis_size("row"),
        tile_cols * lax.axis_size("col"),
    )
    attended, soft, rounded = tile_forward(queries, keyvalue_ext, allowed)
    projected = jnp.dot(
        attended.reshape(-1, inner_width), full_output, preferred_element_type=jnp.float32
    )
    layer_out = (inputs.astype(jnp.float32) + projected.reshape(inputs.shape)).astype(jnp.bfloat16)
    flat_grad = out_grad.reshape(-1, model_width)
    inner_grad = lax.dot_general(
        flat_grad, full_output, (((1,), (1,)), ((), ())), preferred_element_type=jnp.float32
    ).astype(jnp.bfloat16)
    inner_grad = inner_grad.reshape(batches, tile_rows * tile_cols, inner_width)
    query_grad, keyvalue_part = tile_backward(queries, keyvalue_ext, soft, rounded, inner_grad)
    keyvalue_part = keyvalue_part.reshape(batches, ext_rows, ext_cols, 2 * inner_width)
    owned = fold_rows(fold_cols(keyvalue_part))
    token_grad = owned.astype(jnp.bfloat16).reshape(-1, 2 * inner_width)
    row_count, col_count = lax.axis_size("row"), lax.axis_size("col")
    col_levels = col_count.bit_length() - 1
    feature_part = model_width // row_count
    partial = lax.dot_general(
        normed_ext,
        keyvalue_part.reshape(-1, 2 * inner_width).astype(jnp.bfloat16),
        (((0,), (0,)), ((), ())),
        preferred_element_type=jnp.float32,
    )
    half = partial.shape[1] // 2
    own = axis_bit("col", 0)
    halves = partial.reshape(model_width, 2, half)
    pair_part = lax.dynamic_index_in_dim(halves, own, 1, keepdims=False) + partner_swap(
        lax.dynamic_index_in_dim(halves, 1 - own, 1, keepdims=False), "col", 1
    )
    rows_part = scatter_by_bits(
        pair_part.reshape(row_count, feature_part, half), "row", row_groups
    )[0]
    for bit in range(1, col_levels):
        rows_part = rows_part + partner_swap(rows_part, "col", 1 << bit)
    held = jnp.zeros((2,) + rows_part.shape, rows_part.dtype)
    held = lax.dynamic_update_slice(held, rows_part[None], (own, 0, 0))
    held = lax.dynamic_update_slice(held, partner_swap(rows_part, "col", 1)[None], (1 - own, 0, 0))
    keyvalue_grad = held.transpose(1, 0, 2).reshape(feature_part, -1)
    normed_grad = lax.dot_general(
        query_grad.reshape(-1, inner_width),
        full_query,
        (((1,), (1,)), ((), ())),
        preferred_element_type=jnp.float32,
    )
    normed_grad = normed_grad + lax.dot_general(
        token_grad, full_keyvalue, (((1,), (1,)), ((), ())), preferred_element_type=jnp.float32
    )
    gained = normed_grad.reshape(inputs.shape) * norm_gain
    in_grad = out_grad.astype(jnp.float32) + spread * (
        gained
        - jnp.mean(gained, axis=-1, keepdims=True)
        - standard * jnp.mean(gained * standard, axis=-1, keepdims=True)
    )
    return (layer_out, in_grad.astype(jnp.bfloat16), keyvalue_grad)


def solution(mesh):
    return jax.shard_map(
        local,
        mesh=mesh,
        in_specs=(
            P(None, "row", "col", None),
            P(),
            P("row", None),
            P("row", None),
            P("row", None),
            P(None, "row", "col", None),
        ),
        out_specs=(P(None, "row", "col", None), P(None, "row", "col", None), P("row", None)),
        check_vma=False,
    )
```

```python
import math

import jax
import jax.numpy as jnp
from jax import lax
from jax.sharding import PartitionSpec as P

HEADS = 8
RADIUS = 6


EPS = 1e-05
MASKED = -1e30


def shifted(value, axis, steps):
    count = lax.axis_size(axis)
    first, last = (max(0, -steps), min(count, count - steps))
    return lax.ppermute(value, axis, [(source, source + steps) for source in range(first, last)])


def with_halo(block, sides, width):
    for axis, dim in sides:
        count = lax.axis_size(axis)
        forward = [(i, i + 1) for i in range(count - 1)]
        backward = [(target, source) for source, target in forward]
        low = lax.ppermute(
            lax.slice_in_dim(block, block.shape[dim] - width, None, axis=dim), axis, forward
        )
        high = lax.ppermute(lax.slice_in_dim(block, 0, width, axis=dim), axis, backward)
        block = jnp.concatenate([low, block, high], axis=dim)
    return block


def partner_swap(value, axis, mask):
    count = lax.axis_size(axis)
    return lax.ppermute(value, axis, [(i, i ^ mask) for i in range(count)])


def axis_bit(axis, bit):
    return (lax.axis_index(axis) // (1 << bit)) % 2


def flips(group):
    for code in range(1, 1 << len(group)):
        yield [(code >> k) % 2 for k in range(len(group))]


def gather_by_bits(block, axis, groups, tie=None, tie_at=2):
    levels = lax.axis_size(axis).bit_length() - 1
    mine = [axis_bit(axis, bit) for bit in range(levels)]
    zero = [0] * block.ndim
    held = jnp.zeros((2,) * levels + block.shape, block.dtype)
    held = lax.dynamic_update_slice(
        held, block.reshape((1,) * levels + block.shape), mine[::-1] + zero
    )
    done = set()
    for step, group in enumerate(groups):
        start = [0 if b in done else mine[b] for b in range(levels)]
        size = [2 if b in done else 1 for b in range(levels)]
        region = lax.dynamic_slice(held, start[::-1] + zero, size[::-1] + list(block.shape))
        if tie is not None and step == tie_at:
            region, tie = lax.optimization_barrier((region, tie))
        arrived = []
        for flip in flips(group):
            mask = sum(f << b for f, b in zip(flip, group))
            place = list(start)
            for f, b in zip(flip, group):
                place[b] = (mine[b] + f) % 2
            arrived.append((partner_swap(region, axis, mask), place))
        for other, place in arrived:
            held = lax.dynamic_update_slice(held, other, place[::-1] + zero)
        done.update(group)
    held = held.reshape((-1,) + block.shape)
    return held if tie is None else (held, tie)


def scatter_by_bits(total, axis, groups):
    levels = lax.axis_size(axis).bit_length() - 1
    mine = [axis_bit(axis, bit) for bit in range(levels)]
    held = total.reshape((2,) * levels + (total.shape[0] // 2**levels,) + total.shape[1:])
    rest = [0] * (held.ndim - levels)
    for group in groups:
        size = [1 if b in group else held.shape[levels - 1 - b] for b in range(levels)]
        size = size[::-1] + list(held.shape[levels:])
        own = [mine[b] if b in group else 0 for b in range(levels)]
        summed = lax.dynamic_slice(held, own[::-1] + rest, size)
        for flip in flips(group):
            mask = sum(f << b for f, b in zip(flip, group))
            place = list(own)
            for f, b in zip(flip, group):
                place[b] = (mine[b] + f) % 2
            send = lax.dynamic_slice(held, place[::-1] + rest, size)
            summed = summed + partner_swap(send, axis, mask)
        held = summed
    return held.reshape(held.shape[levels:])


def split_swap(value, low_mask, high_mask):
    rows, cols = lax.axis_size("row"), lax.axis_size("col")
    pairs = []
    for r in range(rows):
        for c in range(cols):
            mask = low_mask if c % 2 == 0 else high_mask
            pairs.append((r * cols + c, (r ^ mask) * cols + c))
    return lax.ppermute(value, ("row", "col"), pairs)


def split_scatter(total):
    levels = lax.axis_size("row").bit_length() - 1
    core = axis_bit("col", 0)
    low, high = axis_bit("row", 0), axis_bit("row", 1)
    held = total.reshape((2,) * (levels - 2) + (4,) + total.shape[1:])
    place = levels - 2
    even = core == 0
    keep_at = jnp.where(even, jnp.stack([low, 2 + low]), jnp.stack([2 * high, 2 * high + 1]))
    send_at = jnp.where(
        even, jnp.stack([1 - low, 3 - low]), jnp.stack([2 * (1 - high), 2 * (1 - high) + 1])
    )
    held = jnp.take(held, keep_at, axis=place) + split_swap(
        jnp.take(held, send_at, axis=place), 1, 2
    )
    rest = jnp.where(even, high, low)
    held = lax.dynamic_index_in_dim(held, rest, place) + split_swap(
        lax.dynamic_index_in_dim(held, 1 - rest, place), 2, 1
    )
    for bit in range(2, levels):
        axis = levels - 1 - bit
        own = axis_bit("row", bit)
        keep = lax.dynamic_index_in_dim(held, own, axis)
        send = lax.dynamic_index_in_dim(held, 1 - own, axis)
        held = keep + partner_swap(send, "row", 1 << bit)
    return held.reshape(total.shape[1:])


def gather_weights(w_query, w_keyvalue, w_output, row_groups, tie):
    rows, width = w_query.shape
    kv_rows, kv_width = w_keyvalue.shape
    out_rows = w_output.shape[0]
    qo_pack = jnp.concatenate([w_query.reshape(-1, kv_width), w_output], axis=0)
    own = axis_bit("col", 0)
    packed = jnp.where(own == 0, w_keyvalue, qo_pack)
    fetched, tie = gather_by_bits(packed, "row", row_groups, tie=tie)
    held = jnp.zeros((2,) + fetched.shape, fetched.dtype)
    held = lax.dynamic_update_slice(held, fetched[None], (own, 0, 0, 0))
    held = lax.dynamic_update_slice(held, partner_swap(fetched, "col", 1)[None], (1 - own, 0, 0, 0))
    count = fetched.shape[0]
    query_rows = kv_rows - out_rows
    kv = held[0].reshape(count * kv_rows, kv_width)
    query = held[1, :, :query_rows].reshape(count * rows, width)
    output = held[1, :, query_rows:].reshape(count * out_rows, kv_width)
    return query, kv, output, tie


def normalize(inputs, norm_gain):
    values = inputs.astype(jnp.float32)
    center = values - jnp.mean(values, axis=-1, keepdims=True)
    spread = lax.rsqrt(jnp.mean(center * center, axis=-1, keepdims=True) + EPS)
    standard = center * spread
    return (standard, spread, (standard * norm_gain).astype(jnp.bfloat16))


def window_mask(row_start, col_start, tile_rows, tile_cols, height, map_width):
    ext_rows = tile_rows + 2 * RADIUS
    ext_cols = tile_cols + 2 * RADIUS
    query_pos = jnp.arange(tile_rows * tile_cols, dtype=jnp.int32)
    query_row = query_pos // tile_cols
    query_col = query_pos % tile_cols
    ext_pos = jnp.arange(ext_rows * ext_cols, dtype=jnp.int32)
    ext_row = ext_pos // ext_cols
    ext_col = ext_pos % ext_cols
    nearby = (jnp.abs(ext_row[None, :] - RADIUS - query_row[:, None]) <= RADIUS) & (
        jnp.abs(ext_col[None, :] - RADIUS - query_col[:, None]) <= RADIUS
    )
    global_row = row_start + ext_row - RADIUS
    global_col = col_start + ext_col - RADIUS
    inside = (
        (global_row >= 0) & (global_row < height) & (global_col >= 0) & (global_col < map_width)
    )
    return nearby & inside[None, :]


def tile_forward(queries, keyvalue_ext, allowed):
    batches, query_count, inner_width = queries.shape
    head_size = inner_width // HEADS
    query_heads = queries.reshape(batches, query_count, HEADS, head_size)
    key_heads = keyvalue_ext[:, :, :inner_width].reshape(batches, -1, HEADS, head_size)
    value_heads = keyvalue_ext[:, :, inner_width:].reshape(batches, -1, HEADS, head_size)
    scores = jnp.einsum(
        "bqhd,bkhd->bhqk", query_heads, key_heads, preferred_element_type=jnp.float32
    ) / math.sqrt(head_size)
    scores = jnp.where(allowed, scores, MASKED)
    row_max = jnp.max(scores, axis=-1, keepdims=True)
    exponent = jnp.exp(scores - row_max)
    soft = exponent / jnp.sum(exponent, axis=-1, keepdims=True)
    rounded = soft.astype(jnp.bfloat16)
    attended = jnp.einsum(
        "bhqk,bkhd->bqhd", rounded, value_heads, preferred_element_type=jnp.float32
    )
    return (attended.astype(jnp.bfloat16).reshape(batches, query_count, inner_width), soft, rounded)


def tile_backward(queries, keyvalue_ext, soft, rounded, inner_grad):
    batches, query_count, inner_width = queries.shape
    head_size = inner_width // HEADS
    query_heads = queries.reshape(batches, query_count, HEADS, head_size)
    key_heads = keyvalue_ext[:, :, :inner_width].reshape(batches, -1, HEADS, head_size)
    value_heads = keyvalue_ext[:, :, inner_width:].reshape(batches, -1, HEADS, head_size)
    grad_heads = inner_grad.reshape(batches, query_count, HEADS, head_size)
    prob_grad = jnp.einsum(
        "bqhd,bkhd->bhqk", grad_heads, value_heads, preferred_element_type=jnp.float32
    )
    row_dot = jnp.sum(soft * prob_grad, axis=-1, keepdims=True)
    score_grad = (soft * (prob_grad - row_dot) / math.sqrt(head_size)).astype(jnp.bfloat16)
    query_grad = jnp.einsum(
        "bhqk,bkhd->bqhd", score_grad, key_heads, preferred_element_type=jnp.float32
    )
    key_grad = jnp.einsum(
        "bhqk,bqhd->bkhd", score_grad, query_heads, preferred_element_type=jnp.float32
    )
    value_grad = jnp.einsum(
        "bhqk,bqhd->bkhd", rounded, grad_heads, preferred_element_type=jnp.float32
    )
    ext_count = key_grad.shape[1]
    joined = jnp.concatenate(
        [
            key_grad.reshape(batches, ext_count, inner_width),
            value_grad.reshape(batches, ext_count, inner_width),
        ],
        axis=-1,
    )
    return (query_grad.astype(jnp.bfloat16).reshape(batches, query_count, inner_width), joined)


def fold_cols(extended):
    left_strip = extended[:, :, :RADIUS]
    right_strip = extended[:, :, extended.shape[2] - RADIUS :]
    middle = extended[:, :, RADIUS : extended.shape[2] - RADIUS]
    from_right = shifted(left_strip, "col", -1)
    from_left = shifted(right_strip, "col", 1)
    inner_cols = middle.shape[2]
    return (
        middle
        + jnp.pad(from_left, ((0, 0), (0, 0), (0, inner_cols - RADIUS), (0, 0)))
        + jnp.pad(from_right, ((0, 0), (0, 0), (inner_cols - RADIUS, 0), (0, 0)))
    )


def fold_rows(extended):
    upper_strip = extended[:, :RADIUS]
    lower_strip = extended[:, extended.shape[1] - RADIUS :]
    middle = extended[:, RADIUS : extended.shape[1] - RADIUS]
    from_below = shifted(upper_strip, "row", -1)
    from_above = shifted(lower_strip, "row", 1)
    inner_rows = middle.shape[1]
    return (
        middle
        + jnp.pad(from_above, ((0, 0), (0, inner_rows - RADIUS), (0, 0), (0, 0)))
        + jnp.pad(from_below, ((0, 0), (inner_rows - RADIUS, 0), (0, 0), (0, 0)))
    )


def local(inputs, norm_gain, w_query, w_keyvalue, w_output, out_grad):
    batches, tile_rows, tile_cols, model_width = inputs.shape
    ext_rows = tile_rows + 2 * RADIUS
    ext_cols = tile_cols + 2 * RADIUS
    standard, spread, normed = normalize(inputs, norm_gain)
    flat_norm = normed.reshape(-1, model_width)
    normed_ext = with_halo(normed, (("row", 1), ("col", 2)), RADIUS).reshape(-1, model_width)
    row_levels = lax.axis_size("row").bit_length() - 1
    row_groups = [[b] for b in range(row_levels)]
    full_query, full_keyvalue, full_output, normed_ext = gather_weights(
        w_query, w_keyvalue, w_output, row_groups[::-1], normed_ext
    )
    inner_width = full_query.shape[1]
    queries = jnp.dot(flat_norm, full_query, preferred_element_type=jnp.float32).astype(
        jnp.bfloat16
    )
    queries = queries.reshape(batches, tile_rows * tile_cols, inner_width)
    keyvalue_ext = jnp.dot(normed_ext, full_keyvalue, preferred_element_type=jnp.float32)
    keyvalue_ext = keyvalue_ext.astype(jnp.bfloat16).reshape(
        batches, ext_rows * ext_cols, 2 * inner_width
    )
    allowed = window_mask(
        lax.axis_index("row") * tile_rows,
        lax.axis_index("col") * tile_cols,
        tile_rows,
        tile_cols,
        tile_rows * lax.axis_size("row"),
        tile_cols * lax.axis_size("col"),
    )
    attended, soft, rounded = tile_forward(queries, keyvalue_ext, allowed)
    projected = jnp.dot(
        attended.reshape(-1, inner_width), full_output, preferred_element_type=jnp.float32
    )
    layer_out = (inputs.astype(jnp.float32) + projected.reshape(inputs.shape)).astype(jnp.bfloat16)
    flat_grad = out_grad.reshape(-1, model_width)
    inner_grad = lax.dot_general(
        flat_grad, full_output, (((1,), (1,)), ((), ())), preferred_element_type=jnp.float32
    ).astype(jnp.bfloat16)
    inner_grad = inner_grad.reshape(batches, tile_rows * tile_cols, inner_width)
    query_grad, keyvalue_part = tile_backward(queries, keyvalue_ext, soft, rounded, inner_grad)
    keyvalue_part = keyvalue_part.reshape(batches, ext_rows, ext_cols, 2 * inner_width)
    owned = fold_rows(fold_cols(keyvalue_part))
    token_grad = owned.astype(jnp.bfloat16).reshape(-1, 2 * inner_width)
    row_count, col_count = lax.axis_size("row"), lax.axis_size("col")
    col_levels = col_count.bit_length() - 1
    feature_part = model_width // row_count
    partial = lax.dot_general(
        normed_ext,
        keyvalue_part.reshape(-1, 2 * inner_width).astype(jnp.bfloat16),
        (((0,), (0,)), ((), ())),
        preferred_element_type=jnp.float32,
    )
    half = partial.shape[1] // 2
    own = axis_bit("col", 0)
    halves = partial.reshape(model_width, 2, half)
    pair_part = lax.dynamic_index_in_dim(halves, own, 1, keepdims=False) + partner_swap(
        lax.dynamic_index_in_dim(halves, 1 - own, 1, keepdims=False), "col", 1
    )
    rows_part = split_scatter(pair_part.reshape(row_count, feature_part, half))
    for bit in range(1, col_levels):
        rows_part = rows_part + partner_swap(rows_part, "col", 1 << bit)
    held = jnp.zeros((2,) + rows_part.shape, rows_part.dtype)
    held = lax.dynamic_update_slice(held, rows_part[None], (own, 0, 0))
    held = lax.dynamic_update_slice(held, partner_swap(rows_part, "col", 1)[None], (1 - own, 0, 0))
    keyvalue_grad = held.transpose(1, 0, 2).reshape(feature_part, -1)
    normed_grad = lax.dot_general(
        query_grad.reshape(-1, inner_width),
        full_query,
        (((1,), (1,)), ((), ())),
        preferred_element_type=jnp.float32,
    )
    normed_grad = normed_grad + lax.dot_general(
        token_grad, full_keyvalue, (((1,), (1,)), ((), ())), preferred_element_type=jnp.float32
    )
    gained = normed_grad.reshape(inputs.shape) * norm_gain
    in_grad = out_grad.astype(jnp.float32) + spread * (
        gained
        - jnp.mean(gained, axis=-1, keepdims=True)
        - standard * jnp.mean(gained * standard, axis=-1, keepdims=True)
    )
    return (layer_out, in_grad.astype(jnp.bfloat16), keyvalue_grad)


def solution(mesh):
    return jax.shard_map(
        local,
        mesh=mesh,
        in_specs=(
            P(None, "row", "col", None),
            P(),
            P("row", None),
            P("row", None),
            P("row", None),
            P(None, "row", "col", None),
        ),
        out_specs=(P(None, "row", "col", None), P(None, "row", "col", None), P("row", None)),
        check_vma=False,
    )
```

```python
import math

import jax
import jax.numpy as jnp
from jax import lax
from jax.sharding import PartitionSpec as P

HEADS = 8
RADIUS = 6


EPS = 1e-05
MASKED = -1e30


def shifted(value, axis, steps):
    count = lax.axis_size(axis)
    first, last = (max(0, -steps), min(count, count - steps))
    return lax.ppermute(value, axis, [(source, source + steps) for source in range(first, last)])


def with_halo(block, sides, width):
    for axis, dim in sides:
        count = lax.axis_size(axis)
        forward = [(i, i + 1) for i in range(count - 1)]
        backward = [(target, source) for source, target in forward]
        low = lax.ppermute(
            lax.slice_in_dim(block, block.shape[dim] - width, None, axis=dim), axis, forward
        )
        high = lax.ppermute(lax.slice_in_dim(block, 0, width, axis=dim), axis, backward)
        block = jnp.concatenate([low, block, high], axis=dim)
    return block


def partner_swap(value, axis, mask):
    count = lax.axis_size(axis)
    return lax.ppermute(value, axis, [(i, i ^ mask) for i in range(count)])


def axis_bit(axis, bit):
    return (lax.axis_index(axis) // (1 << bit)) % 2


def flips(group):
    for code in range(1, 1 << len(group)):
        yield [(code >> k) % 2 for k in range(len(group))]


def gather_by_bits(block, axis, groups, tie=None, tie_at=3):
    levels = lax.axis_size(axis).bit_length() - 1
    mine = [axis_bit(axis, bit) for bit in range(levels)]
    zero = [0] * block.ndim
    held = jnp.zeros((2,) * levels + block.shape, block.dtype)
    held = lax.dynamic_update_slice(
        held, block.reshape((1,) * levels + block.shape), mine[::-1] + zero
    )
    done = set()
    for step, group in enumerate(groups):
        start = [0 if b in done else mine[b] for b in range(levels)]
        size = [2 if b in done else 1 for b in range(levels)]
        region = lax.dynamic_slice(held, start[::-1] + zero, size[::-1] + list(block.shape))
        if tie is not None and step == tie_at:
            region, tie = lax.optimization_barrier((region, tie))
        arrived = []
        for flip in flips(group):
            mask = sum(f << b for f, b in zip(flip, group))
            place = list(start)
            for f, b in zip(flip, group):
                place[b] = (mine[b] + f) % 2
            arrived.append((partner_swap(region, axis, mask), place))
        for other, place in arrived:
            held = lax.dynamic_update_slice(held, other, place[::-1] + zero)
        done.update(group)
    held = held.reshape((-1,) + block.shape)
    return held if tie is None else (held, tie)


def scatter_by_bits(total, axis, groups):
    levels = lax.axis_size(axis).bit_length() - 1
    mine = [axis_bit(axis, bit) for bit in range(levels)]
    held = total.reshape((2,) * levels + (total.shape[0] // 2**levels,) + total.shape[1:])
    rest = [0] * (held.ndim - levels)
    for group in groups:
        size = [1 if b in group else held.shape[levels - 1 - b] for b in range(levels)]
        size = size[::-1] + list(held.shape[levels:])
        own = [mine[b] if b in group else 0 for b in range(levels)]
        summed = lax.dynamic_slice(held, own[::-1] + rest, size)
        for flip in flips(group):
            mask = sum(f << b for f, b in zip(flip, group))
            place = list(own)
            for f, b in zip(flip, group):
                place[b] = (mine[b] + f) % 2
            send = lax.dynamic_slice(held, place[::-1] + rest, size)
            summed = summed + partner_swap(send, axis, mask)
        held = summed
    return held.reshape(held.shape[levels:])


def gather_weights(w_query, w_keyvalue, w_output, row_groups, tie):
    rows, width = w_query.shape
    kv_rows, kv_width = w_keyvalue.shape
    out_rows = w_output.shape[0]
    qo_pack = jnp.concatenate([w_query.reshape(-1, kv_width), w_output], axis=0)
    own = axis_bit("col", 0)
    packed = jnp.where(own == 0, w_keyvalue, qo_pack)
    fetched, tie = gather_by_bits(packed, "row", row_groups, tie=tie)
    held = jnp.zeros((2,) + fetched.shape, fetched.dtype)
    held = lax.dynamic_update_slice(held, fetched[None], (own, 0, 0, 0))
    held = lax.dynamic_update_slice(held, partner_swap(fetched, "col", 1)[None], (1 - own, 0, 0, 0))
    count = fetched.shape[0]
    query_rows = kv_rows - out_rows
    kv = held[0].reshape(count * kv_rows, kv_width)
    query = held[1, :, :query_rows].reshape(count * rows, width)
    output = held[1, :, query_rows:].reshape(count * out_rows, kv_width)
    return query, kv, output, tie


def normalize(inputs, norm_gain):
    values = inputs.astype(jnp.float32)
    center = values - jnp.mean(values, axis=-1, keepdims=True)
    spread = lax.rsqrt(jnp.mean(center * center, axis=-1, keepdims=True) + EPS)
    standard = center * spread
    return (standard, spread, (standard * norm_gain).astype(jnp.bfloat16))


def window_mask(row_start, col_start, tile_rows, tile_cols, height, map_width):
    ext_rows = tile_rows + 2 * RADIUS
    ext_cols = tile_cols + 2 * RADIUS
    query_pos = jnp.arange(tile_rows * tile_cols, dtype=jnp.int32)
    query_row = query_pos // tile_cols
    query_col = query_pos % tile_cols
    ext_pos = jnp.arange(ext_rows * ext_cols, dtype=jnp.int32)
    ext_row = ext_pos // ext_cols
    ext_col = ext_pos % ext_cols
    nearby = (jnp.abs(ext_row[None, :] - RADIUS - query_row[:, None]) <= RADIUS) & (
        jnp.abs(ext_col[None, :] - RADIUS - query_col[:, None]) <= RADIUS
    )
    global_row = row_start + ext_row - RADIUS
    global_col = col_start + ext_col - RADIUS
    inside = (
        (global_row >= 0) & (global_row < height) & (global_col >= 0) & (global_col < map_width)
    )
    return nearby & inside[None, :]


def tile_forward(queries, keyvalue_ext, allowed):
    batches, query_count, inner_width = queries.shape
    head_size = inner_width // HEADS
    query_heads = queries.reshape(batches, query_count, HEADS, head_size)
    key_heads = keyvalue_ext[:, :, :inner_width].reshape(batches, -1, HEADS, head_size)
    value_heads = keyvalue_ext[:, :, inner_width:].reshape(batches, -1, HEADS, head_size)
    scores = jnp.einsum(
        "bqhd,bkhd->bhqk", query_heads, key_heads, preferred_element_type=jnp.float32
    ) / math.sqrt(head_size)
    scores = jnp.where(allowed, scores, MASKED)
    row_max = jnp.max(scores, axis=-1, keepdims=True)
    exponent = jnp.exp(scores - row_max)
    soft = exponent / jnp.sum(exponent, axis=-1, keepdims=True)
    rounded = soft.astype(jnp.bfloat16)
    attended = jnp.einsum(
        "bhqk,bkhd->bqhd", rounded, value_heads, preferred_element_type=jnp.float32
    )
    return (attended.astype(jnp.bfloat16).reshape(batches, query_count, inner_width), soft, rounded)


def tile_backward(queries, keyvalue_ext, soft, rounded, inner_grad):
    batches, query_count, inner_width = queries.shape
    head_size = inner_width // HEADS
    query_heads = queries.reshape(batches, query_count, HEADS, head_size)
    key_heads = keyvalue_ext[:, :, :inner_width].reshape(batches, -1, HEADS, head_size)
    value_heads = keyvalue_ext[:, :, inner_width:].reshape(batches, -1, HEADS, head_size)
    grad_heads = inner_grad.reshape(batches, query_count, HEADS, head_size)
    prob_grad = jnp.einsum(
        "bqhd,bkhd->bhqk", grad_heads, value_heads, preferred_element_type=jnp.float32
    )
    row_dot = jnp.sum(soft * prob_grad, axis=-1, keepdims=True)
    score_grad = (soft * (prob_grad - row_dot) / math.sqrt(head_size)).astype(jnp.bfloat16)
    query_grad = jnp.einsum(
        "bhqk,bkhd->bqhd", score_grad, key_heads, preferred_element_type=jnp.float32
    )
    key_grad = jnp.einsum(
        "bhqk,bqhd->bkhd", score_grad, query_heads, preferred_element_type=jnp.float32
    )
    value_grad = jnp.einsum(
        "bhqk,bqhd->bkhd", rounded, grad_heads, preferred_element_type=jnp.float32
    )
    ext_count = key_grad.shape[1]
    joined = jnp.concatenate(
        [
            key_grad.reshape(batches, ext_count, inner_width),
            value_grad.reshape(batches, ext_count, inner_width),
        ],
        axis=-1,
    )
    return (query_grad.astype(jnp.bfloat16).reshape(batches, query_count, inner_width), joined)


def fold_cols(extended):
    left_strip = extended[:, :, :RADIUS]
    right_strip = extended[:, :, extended.shape[2] - RADIUS :]
    middle = extended[:, :, RADIUS : extended.shape[2] - RADIUS]
    from_right = shifted(left_strip, "col", -1)
    from_left = shifted(right_strip, "col", 1)
    inner_cols = middle.shape[2]
    return (
        middle
        + jnp.pad(from_left, ((0, 0), (0, 0), (0, inner_cols - RADIUS), (0, 0)))
        + jnp.pad(from_right, ((0, 0), (0, 0), (inner_cols - RADIUS, 0), (0, 0)))
    )


def fold_rows(extended):
    upper_strip = extended[:, :RADIUS]
    lower_strip = extended[:, extended.shape[1] - RADIUS :]
    middle = extended[:, RADIUS : extended.shape[1] - RADIUS]
    from_below = shifted(upper_strip, "row", -1)
    from_above = shifted(lower_strip, "row", 1)
    inner_rows = middle.shape[1]
    return (
        middle
        + jnp.pad(from_above, ((0, 0), (0, inner_rows - RADIUS), (0, 0), (0, 0)))
        + jnp.pad(from_below, ((0, 0), (inner_rows - RADIUS, 0), (0, 0), (0, 0)))
    )


def local(inputs, norm_gain, w_query, w_keyvalue, w_output, out_grad):
    batches, tile_rows, tile_cols, model_width = inputs.shape
    ext_rows = tile_rows + 2 * RADIUS
    ext_cols = tile_cols + 2 * RADIUS
    standard, spread, normed = normalize(inputs, norm_gain)
    flat_norm = normed.reshape(-1, model_width)
    normed_ext = with_halo(normed, (("row", 1), ("col", 2)), RADIUS).reshape(-1, model_width)
    row_levels = lax.axis_size("row").bit_length() - 1
    row_groups = [[b] for b in range(row_levels)]
    full_query, full_keyvalue, full_output, normed_ext = gather_weights(
        w_query, w_keyvalue, w_output, row_groups[::-1], normed_ext
    )
    inner_width = full_query.shape[1]
    queries = jnp.dot(flat_norm, full_query, preferred_element_type=jnp.float32).astype(
        jnp.bfloat16
    )
    queries = queries.reshape(batches, tile_rows * tile_cols, inner_width)
    keyvalue_ext = jnp.dot(normed_ext, full_keyvalue, preferred_element_type=jnp.float32)
    keyvalue_ext = keyvalue_ext.astype(jnp.bfloat16).reshape(
        batches, ext_rows * ext_cols, 2 * inner_width
    )
    allowed = window_mask(
        lax.axis_index("row") * tile_rows,
        lax.axis_index("col") * tile_cols,
        tile_rows,
        tile_cols,
        tile_rows * lax.axis_size("row"),
        tile_cols * lax.axis_size("col"),
    )
    attended, soft, rounded = tile_forward(queries, keyvalue_ext, allowed)
    projected = jnp.dot(
        attended.reshape(-1, inner_width), full_output, preferred_element_type=jnp.float32
    )
    layer_out = (inputs.astype(jnp.float32) + projected.reshape(inputs.shape)).astype(jnp.bfloat16)
    flat_grad = out_grad.reshape(-1, model_width)
    inner_grad = lax.dot_general(
        flat_grad, full_output, (((1,), (1,)), ((), ())), preferred_element_type=jnp.float32
    ).astype(jnp.bfloat16)
    inner_grad = inner_grad.reshape(batches, tile_rows * tile_cols, inner_width)
    query_grad, keyvalue_part = tile_backward(queries, keyvalue_ext, soft, rounded, inner_grad)
    keyvalue_part = keyvalue_part.reshape(batches, ext_rows, ext_cols, 2 * inner_width)
    owned = fold_rows(fold_cols(keyvalue_part))
    token_grad = owned.astype(jnp.bfloat16).reshape(-1, 2 * inner_width)
    row_count, col_count = lax.axis_size("row"), lax.axis_size("col")
    col_levels = col_count.bit_length() - 1
    feature_part = model_width // row_count
    partial = lax.dot_general(
        normed_ext,
        keyvalue_part.reshape(-1, 2 * inner_width).astype(jnp.bfloat16),
        (((0,), (0,)), ((), ())),
        preferred_element_type=jnp.float32,
    )
    half = partial.shape[1] // 2
    own = axis_bit("col", 0)
    halves = partial.reshape(model_width, 2, half)
    pair_part = lax.dynamic_index_in_dim(halves, own, 1, keepdims=False) + partner_swap(
        lax.dynamic_index_in_dim(halves, 1 - own, 1, keepdims=False), "col", 1
    )
    rows_part = scatter_by_bits(
        pair_part.reshape(row_count, feature_part, half), "row", row_groups
    )[0]
    for bit in range(1, col_levels):
        rows_part = rows_part + partner_swap(rows_part, "col", 1 << bit)
    held = jnp.zeros((2,) + rows_part.shape, rows_part.dtype)
    held = lax.dynamic_update_slice(held, rows_part[None], (own, 0, 0))
    held = lax.dynamic_update_slice(held, partner_swap(rows_part, "col", 1)[None], (1 - own, 0, 0))
    keyvalue_grad = held.transpose(1, 0, 2).reshape(feature_part, -1)
    normed_grad = lax.dot_general(
        query_grad.reshape(-1, inner_width),
        full_query,
        (((1,), (1,)), ((), ())),
        preferred_element_type=jnp.float32,
    )
    normed_grad = normed_grad + lax.dot_general(
        token_grad, full_keyvalue, (((1,), (1,)), ((), ())), preferred_element_type=jnp.float32
    )
    gained = normed_grad.reshape(inputs.shape) * norm_gain
    in_grad = out_grad.astype(jnp.float32) + spread * (
        gained
        - jnp.mean(gained, axis=-1, keepdims=True)
        - standard * jnp.mean(gained * standard, axis=-1, keepdims=True)
    )
    return (layer_out, in_grad.astype(jnp.bfloat16), keyvalue_grad)


def solution(mesh):
    return jax.shard_map(
        local,
        mesh=mesh,
        in_specs=(
            P(None, "row", "col", None),
            P(),
            P("row", None),
            P("row", None),
            P("row", None),
            P(None, "row", "col", None),
        ),
        out_specs=(P(None, "row", "col", None), P(None, "row", "col", None), P("row", None)),
        check_vma=False,
    )
```

```python
import math

import jax
import jax.numpy as jnp
from jax import lax
from jax.sharding import PartitionSpec as P

HEADS = 8
RADIUS = 6


EPS = 1e-05
MASKED = -1e30


def shifted(value, axis, steps):
    count = lax.axis_size(axis)
    first, last = (max(0, -steps), min(count, count - steps))
    return lax.ppermute(value, axis, [(source, source + steps) for source in range(first, last)])


def with_halo(block, sides, width):
    for axis, dim in sides:
        count = lax.axis_size(axis)
        forward = [(i, i + 1) for i in range(count - 1)]
        backward = [(target, source) for source, target in forward]
        low = lax.ppermute(
            lax.slice_in_dim(block, block.shape[dim] - width, None, axis=dim), axis, forward
        )
        high = lax.ppermute(lax.slice_in_dim(block, 0, width, axis=dim), axis, backward)
        block = jnp.concatenate([low, block, high], axis=dim)
    return block


def partner_swap(value, axis, mask):
    count = lax.axis_size(axis)
    return lax.ppermute(value, axis, [(i, i ^ mask) for i in range(count)])


def axis_bit(axis, bit):
    return (lax.axis_index(axis) // (1 << bit)) % 2


def flips(group):
    for code in range(1, 1 << len(group)):
        yield [(code >> k) % 2 for k in range(len(group))]


def gather_by_bits(block, axis, groups, tie=None, tie_at=3):
    levels = lax.axis_size(axis).bit_length() - 1
    mine = [axis_bit(axis, bit) for bit in range(levels)]
    zero = [0] * block.ndim
    held = jnp.zeros((2,) * levels + block.shape, block.dtype)
    held = lax.dynamic_update_slice(
        held, block.reshape((1,) * levels + block.shape), mine[::-1] + zero
    )
    done = set()
    for step, group in enumerate(groups):
        start = [0 if b in done else mine[b] for b in range(levels)]
        size = [2 if b in done else 1 for b in range(levels)]
        region = lax.dynamic_slice(held, start[::-1] + zero, size[::-1] + list(block.shape))
        if tie is not None and step == tie_at:
            region, tie = lax.optimization_barrier((region, tie))
        arrived = []
        for flip in flips(group):
            mask = sum(f << b for f, b in zip(flip, group))
            place = list(start)
            for f, b in zip(flip, group):
                place[b] = (mine[b] + f) % 2
            arrived.append((partner_swap(region, axis, mask), place))
        for other, place in arrived:
            held = lax.dynamic_update_slice(held, other, place[::-1] + zero)
        done.update(group)
    held = held.reshape((-1,) + block.shape)
    return held if tie is None else (held, tie)


def scatter_by_bits(total, axis, groups):
    levels = lax.axis_size(axis).bit_length() - 1
    mine = [axis_bit(axis, bit) for bit in range(levels)]
    held = total.reshape((2,) * levels + (total.shape[0] // 2**levels,) + total.shape[1:])
    rest = [0] * (held.ndim - levels)
    for group in groups:
        size = [1 if b in group else held.shape[levels - 1 - b] for b in range(levels)]
        size = size[::-1] + list(held.shape[levels:])
        own = [mine[b] if b in group else 0 for b in range(levels)]
        summed = lax.dynamic_slice(held, own[::-1] + rest, size)
        for flip in flips(group):
            mask = sum(f << b for f, b in zip(flip, group))
            place = list(own)
            for f, b in zip(flip, group):
                place[b] = (mine[b] + f) % 2
            send = lax.dynamic_slice(held, place[::-1] + rest, size)
            summed = summed + partner_swap(send, axis, mask)
        held = summed
    return held.reshape(held.shape[levels:])


def gather_weights(w_query, w_keyvalue, w_output, row_groups, tie):
    rows, width = w_query.shape
    kv_rows, kv_width = w_keyvalue.shape
    out_rows = w_output.shape[0]
    qo_pack = jnp.concatenate([w_query.reshape(-1, kv_width), w_output], axis=0)
    own = axis_bit("col", 0)
    packed = jnp.where(own == 0, w_keyvalue, qo_pack)
    fetched, tie = gather_by_bits(packed, "row", row_groups, tie=tie)
    swapped = partner_swap(fetched, "col", 1)
    count = fetched.shape[0]
    query_rows = kv_rows - out_rows
    kv = jnp.where(own == 0, fetched, swapped).reshape(count * kv_rows, kv_width)
    qo = jnp.where(own == 0, swapped, fetched)
    query = qo[:, :query_rows].reshape(count * rows, width)
    output = qo[:, query_rows:].reshape(count * out_rows, kv_width)
    return query, kv, output, tie


def normalize(inputs, norm_gain):
    values = inputs.astype(jnp.float32)
    center = values - jnp.mean(values, axis=-1, keepdims=True)
    spread = lax.rsqrt(jnp.mean(center * center, axis=-1, keepdims=True) + EPS)
    standard = center * spread
    return (standard, spread, (standard * norm_gain).astype(jnp.bfloat16))


def window_mask(row_start, col_start, tile_rows, tile_cols, height, map_width):
    ext_rows = tile_rows + 2 * RADIUS
    ext_cols = tile_cols + 2 * RADIUS
    query_pos = jnp.arange(tile_rows * tile_cols, dtype=jnp.int32)
    query_row = query_pos // tile_cols
    query_col = query_pos % tile_cols
    ext_pos = jnp.arange(ext_rows * ext_cols, dtype=jnp.int32)
    ext_row = ext_pos // ext_cols
    ext_col = ext_pos % ext_cols
    nearby = (jnp.abs(ext_row[None, :] - RADIUS - query_row[:, None]) <= RADIUS) & (
        jnp.abs(ext_col[None, :] - RADIUS - query_col[:, None]) <= RADIUS
    )
    global_row = row_start + ext_row - RADIUS
    global_col = col_start + ext_col - RADIUS
    inside = (
        (global_row >= 0) & (global_row < height) & (global_col >= 0) & (global_col < map_width)
    )
    return nearby & inside[None, :]


def tile_forward(queries, keyvalue_ext, allowed):
    batches, query_count, inner_width = queries.shape
    head_size = inner_width // HEADS
    query_heads = queries.reshape(batches, query_count, HEADS, head_size)
    key_heads = keyvalue_ext[:, :, :inner_width].reshape(batches, -1, HEADS, head_size)
    value_heads = keyvalue_ext[:, :, inner_width:].reshape(batches, -1, HEADS, head_size)
    scores = jnp.einsum(
        "bqhd,bkhd->bhqk", query_heads, key_heads, preferred_element_type=jnp.float32
    ) / math.sqrt(head_size)
    scores = jnp.where(allowed, scores, MASKED)
    row_max = jnp.max(scores, axis=-1, keepdims=True)
    exponent = jnp.exp(scores - row_max)
    soft = exponent / jnp.sum(exponent, axis=-1, keepdims=True)
    rounded = soft.astype(jnp.bfloat16)
    attended = jnp.einsum(
        "bhqk,bkhd->bqhd", rounded, value_heads, preferred_element_type=jnp.float32
    )
    return (attended.astype(jnp.bfloat16).reshape(batches, query_count, inner_width), soft, rounded)


def tile_backward(queries, keyvalue_ext, soft, rounded, inner_grad):
    batches, query_count, inner_width = queries.shape
    head_size = inner_width // HEADS
    query_heads = queries.reshape(batches, query_count, HEADS, head_size)
    key_heads = keyvalue_ext[:, :, :inner_width].reshape(batches, -1, HEADS, head_size)
    value_heads = keyvalue_ext[:, :, inner_width:].reshape(batches, -1, HEADS, head_size)
    grad_heads = inner_grad.reshape(batches, query_count, HEADS, head_size)
    prob_grad = jnp.einsum(
        "bqhd,bkhd->bhqk", grad_heads, value_heads, preferred_element_type=jnp.float32
    )
    row_dot = jnp.sum(soft * prob_grad, axis=-1, keepdims=True)
    score_grad = (soft * (prob_grad - row_dot) / math.sqrt(head_size)).astype(jnp.bfloat16)
    query_grad = jnp.einsum(
        "bhqk,bkhd->bqhd", score_grad, key_heads, preferred_element_type=jnp.float32
    )
    key_grad = jnp.einsum(
        "bhqk,bqhd->bkhd", score_grad, query_heads, preferred_element_type=jnp.float32
    )
    value_grad = jnp.einsum(
        "bhqk,bqhd->bkhd", rounded, grad_heads, preferred_element_type=jnp.float32
    )
    ext_count = key_grad.shape[1]
    joined = jnp.concatenate(
        [
            key_grad.reshape(batches, ext_count, inner_width),
            value_grad.reshape(batches, ext_count, inner_width),
        ],
        axis=-1,
    )
    return (query_grad.astype(jnp.bfloat16).reshape(batches, query_count, inner_width), joined)


def fold_cols(extended):
    left_strip = extended[:, :, :RADIUS]
    right_strip = extended[:, :, extended.shape[2] - RADIUS :]
    middle = extended[:, :, RADIUS : extended.shape[2] - RADIUS]
    from_right = shifted(left_strip, "col", -1)
    from_left = shifted(right_strip, "col", 1)
    inner_cols = middle.shape[2]
    return (
        middle
        + jnp.pad(from_left, ((0, 0), (0, 0), (0, inner_cols - RADIUS), (0, 0)))
        + jnp.pad(from_right, ((0, 0), (0, 0), (inner_cols - RADIUS, 0), (0, 0)))
    )


def fold_rows(extended):
    upper_strip = extended[:, :RADIUS]
    lower_strip = extended[:, extended.shape[1] - RADIUS :]
    middle = extended[:, RADIUS : extended.shape[1] - RADIUS]
    from_below = shifted(upper_strip, "row", -1)
    from_above = shifted(lower_strip, "row", 1)
    inner_rows = middle.shape[1]
    return (
        middle
        + jnp.pad(from_above, ((0, 0), (0, inner_rows - RADIUS), (0, 0), (0, 0)))
        + jnp.pad(from_below, ((0, 0), (inner_rows - RADIUS, 0), (0, 0), (0, 0)))
    )


def local(inputs, norm_gain, w_query, w_keyvalue, w_output, out_grad):
    batches, tile_rows, tile_cols, model_width = inputs.shape
    ext_rows = tile_rows + 2 * RADIUS
    ext_cols = tile_cols + 2 * RADIUS
    standard, spread, normed = normalize(inputs, norm_gain)
    flat_norm = normed.reshape(-1, model_width)
    normed_ext = with_halo(normed, (("row", 1), ("col", 2)), RADIUS).reshape(-1, model_width)
    row_levels = lax.axis_size("row").bit_length() - 1
    row_groups = [[b] for b in range(row_levels)]
    full_query, full_keyvalue, full_output, normed_ext = gather_weights(
        w_query, w_keyvalue, w_output, row_groups[::-1], normed_ext
    )
    inner_width = full_query.shape[1]
    queries = jnp.dot(flat_norm, full_query, preferred_element_type=jnp.float32).astype(
        jnp.bfloat16
    )
    queries = queries.reshape(batches, tile_rows * tile_cols, inner_width)
    keyvalue_ext = jnp.dot(normed_ext, full_keyvalue, preferred_element_type=jnp.float32)
    keyvalue_ext = keyvalue_ext.astype(jnp.bfloat16).reshape(
        batches, ext_rows * ext_cols, 2 * inner_width
    )
    allowed = window_mask(
        lax.axis_index("row") * tile_rows,
        lax.axis_index("col") * tile_cols,
        tile_rows,
        tile_cols,
        tile_rows * lax.axis_size("row"),
        tile_cols * lax.axis_size("col"),
    )
    attended, soft, rounded = tile_forward(queries, keyvalue_ext, allowed)
    projected = jnp.dot(
        attended.reshape(-1, inner_width), full_output, preferred_element_type=jnp.float32
    )
    layer_out = (inputs.astype(jnp.float32) + projected.reshape(inputs.shape)).astype(jnp.bfloat16)
    flat_grad = out_grad.reshape(-1, model_width)
    inner_grad = lax.dot_general(
        flat_grad, full_output, (((1,), (1,)), ((), ())), preferred_element_type=jnp.float32
    ).astype(jnp.bfloat16)
    inner_grad = inner_grad.reshape(batches, tile_rows * tile_cols, inner_width)
    query_grad, keyvalue_part = tile_backward(queries, keyvalue_ext, soft, rounded, inner_grad)
    keyvalue_part = keyvalue_part.reshape(batches, ext_rows, ext_cols, 2 * inner_width)
    owned = fold_rows(fold_cols(keyvalue_part))
    token_grad = owned.astype(jnp.bfloat16).reshape(-1, 2 * inner_width)
    row_count, col_count = lax.axis_size("row"), lax.axis_size("col")
    col_levels = col_count.bit_length() - 1
    feature_part = model_width // row_count
    partial = lax.dot_general(
        normed_ext,
        keyvalue_part.reshape(-1, 2 * inner_width).astype(jnp.bfloat16),
        (((0,), (0,)), ((), ())),
        preferred_element_type=jnp.float32,
    )
    half = partial.shape[1] // 2
    own = axis_bit("col", 0)
    halves = partial.reshape(model_width, 2, half)
    pair_part = lax.dynamic_index_in_dim(halves, own, 1, keepdims=False) + partner_swap(
        lax.dynamic_index_in_dim(halves, 1 - own, 1, keepdims=False), "col", 1
    )
    rows_part = scatter_by_bits(
        pair_part.reshape(row_count, feature_part, half), "row", row_groups
    )[0]
    for bit in range(1, col_levels):
        rows_part = rows_part + partner_swap(rows_part, "col", 1 << bit)
    held = jnp.zeros((2,) + rows_part.shape, rows_part.dtype)
    held = lax.dynamic_update_slice(held, rows_part[None], (own, 0, 0))
    held = lax.dynamic_update_slice(held, partner_swap(rows_part, "col", 1)[None], (1 - own, 0, 0))
    keyvalue_grad = held.transpose(1, 0, 2).reshape(feature_part, -1)
    normed_grad = lax.dot_general(
        query_grad.reshape(-1, inner_width),
        full_query,
        (((1,), (1,)), ((), ())),
        preferred_element_type=jnp.float32,
    )
    normed_grad = normed_grad + lax.dot_general(
        token_grad, full_keyvalue, (((1,), (1,)), ((), ())), preferred_element_type=jnp.float32
    )
    gained = normed_grad.reshape(inputs.shape) * norm_gain
    in_grad = out_grad.astype(jnp.float32) + spread * (
        gained
        - jnp.mean(gained, axis=-1, keepdims=True)
        - standard * jnp.mean(gained * standard, axis=-1, keepdims=True)
    )
    return (layer_out, in_grad.astype(jnp.bfloat16), keyvalue_grad)


def solution(mesh):
    return jax.shard_map(
        local,
        mesh=mesh,
        in_specs=(
            P(None, "row", "col", None),
            P(),
            P("row", None),
            P("row", None),
            P("row", None),
            P(None, "row", "col", None),
        ),
        out_specs=(P(None, "row", "col", None), P(None, "row", "col", None), P("row", None)),
        check_vma=False,
    )
```

```python
import math

import jax
import jax.numpy as jnp
from jax import lax
from jax.sharding import PartitionSpec as P

HEADS = 8
RADIUS = 6


EPS = 1e-05
MASKED = -1e30


def shifted(value, axis, steps):
    count = lax.axis_size(axis)
    first, last = (max(0, -steps), min(count, count - steps))
    return lax.ppermute(value, axis, [(source, source + steps) for source in range(first, last)])


def with_halo(block, sides, width):
    for axis, dim in sides:
        count = lax.axis_size(axis)
        forward = [(i, i + 1) for i in range(count - 1)]
        backward = [(target, source) for source, target in forward]
        low = lax.ppermute(
            lax.slice_in_dim(block, block.shape[dim] - width, None, axis=dim), axis, forward
        )
        high = lax.ppermute(lax.slice_in_dim(block, 0, width, axis=dim), axis, backward)
        block = jnp.concatenate([low, block, high], axis=dim)
    return block


def partner_swap(value, axis, mask):
    count = lax.axis_size(axis)
    return lax.ppermute(value, axis, [(i, i ^ mask) for i in range(count)])


def axis_bit(axis, bit):
    return (lax.axis_index(axis) // (1 << bit)) % 2


def flips(group):
    for code in range(1, 1 << len(group)):
        yield [(code >> k) % 2 for k in range(len(group))]


def gather_by_bits(block, axis, groups, tie=None, tie_at=3):
    levels = lax.axis_size(axis).bit_length() - 1
    mine = [axis_bit(axis, bit) for bit in range(levels)]
    zero = [0] * block.ndim
    held = jnp.zeros((2,) * levels + block.shape, block.dtype)
    held = lax.dynamic_update_slice(
        held, block.reshape((1,) * levels + block.shape), mine[::-1] + zero
    )
    done = set()
    for step, group in enumerate(groups):
        start = [0 if b in done else mine[b] for b in range(levels)]
        size = [2 if b in done else 1 for b in range(levels)]
        region = lax.dynamic_slice(held, start[::-1] + zero, size[::-1] + list(block.shape))
        if tie is not None and step == tie_at:
            region, tie = lax.optimization_barrier((region, tie))
        arrived = []
        for flip in flips(group):
            mask = sum(f << b for f, b in zip(flip, group))
            place = list(start)
            for f, b in zip(flip, group):
                place[b] = (mine[b] + f) % 2
            arrived.append((partner_swap(region, axis, mask), place))
        for other, place in arrived:
            held = lax.dynamic_update_slice(held, other, place[::-1] + zero)
        done.update(group)
    held = held.reshape((-1,) + block.shape)
    return held if tie is None else (held, tie)


def scatter_by_bits(total, axis, groups):
    levels = lax.axis_size(axis).bit_length() - 1
    mine = [axis_bit(axis, bit) for bit in range(levels)]
    held = total.reshape((2,) * levels + (total.shape[0] // 2**levels,) + total.shape[1:])
    rest = [0] * (held.ndim - levels)
    for group in groups:
        size = [1 if b in group else held.shape[levels - 1 - b] for b in range(levels)]
        size = size[::-1] + list(held.shape[levels:])
        own = [mine[b] if b in group else 0 for b in range(levels)]
        summed = lax.dynamic_slice(held, own[::-1] + rest, size)
        for flip in flips(group):
            mask = sum(f << b for f, b in zip(flip, group))
            place = list(own)
            for f, b in zip(flip, group):
                place[b] = (mine[b] + f) % 2
            send = lax.dynamic_slice(held, place[::-1] + rest, size)
            summed = summed + partner_swap(send, axis, mask)
        held = summed
    return held.reshape(held.shape[levels:])


def gather_weights(w_query, w_keyvalue, w_output, row_groups, tie):
    rows, width = w_query.shape
    kv_rows, kv_width = w_keyvalue.shape
    out_rows = w_output.shape[0]
    qo_pack = jnp.concatenate([w_query.reshape(-1, kv_width), w_output], axis=0)
    own = axis_bit("col", 0)
    packed = jnp.where(own == 0, w_keyvalue, qo_pack)
    fetched, tie = gather_by_bits(packed, "row", row_groups, tie=tie)
    held = jnp.zeros((2,) + fetched.shape, fetched.dtype)
    held = lax.dynamic_update_slice(held, fetched[None], (own, 0, 0, 0))
    held = lax.dynamic_update_slice(held, partner_swap(fetched, "col", 1)[None], (1 - own, 0, 0, 0))
    count = fetched.shape[0]
    query_rows = kv_rows - out_rows
    kv = held[0].reshape(count * kv_rows, kv_width)
    query = held[1, :, :query_rows].reshape(count * rows, width)
    output = held[1, :, query_rows:].reshape(count * out_rows, kv_width)
    return query, kv, output, tie


def normalize(inputs, norm_gain):
    values = inputs.astype(jnp.float32)
    center = values - jnp.mean(values, axis=-1, keepdims=True)
    spread = lax.rsqrt(jnp.mean(center * center, axis=-1, keepdims=True) + EPS)
    standard = center * spread
    return (standard, spread, (standard * norm_gain).astype(jnp.bfloat16))


def window_mask(row_start, col_start, tile_rows, tile_cols, height, map_width):
    ext_rows = tile_rows + 2 * RADIUS
    ext_cols = tile_cols + 2 * RADIUS
    query_pos = jnp.arange(tile_rows * tile_cols, dtype=jnp.int32)
    query_row = query_pos // tile_cols
    query_col = query_pos % tile_cols
    ext_pos = jnp.arange(ext_rows * ext_cols, dtype=jnp.int32)
    ext_row = ext_pos // ext_cols
    ext_col = ext_pos % ext_cols
    nearby = (jnp.abs(ext_row[None, :] - RADIUS - query_row[:, None]) <= RADIUS) & (
        jnp.abs(ext_col[None, :] - RADIUS - query_col[:, None]) <= RADIUS
    )
    global_row = row_start + ext_row - RADIUS
    global_col = col_start + ext_col - RADIUS
    inside = (
        (global_row >= 0) & (global_row < height) & (global_col >= 0) & (global_col < map_width)
    )
    return nearby & inside[None, :]


def tile_forward(queries, keyvalue_ext, allowed):
    batches, query_count, inner_width = queries.shape
    head_size = inner_width // HEADS
    query_heads = queries.reshape(batches, query_count, HEADS, head_size)
    key_heads = keyvalue_ext[:, :, :inner_width].reshape(batches, -1, HEADS, head_size)
    value_heads = keyvalue_ext[:, :, inner_width:].reshape(batches, -1, HEADS, head_size)
    scores = jnp.einsum(
        "bqhd,bkhd->bhqk", query_heads, key_heads, preferred_element_type=jnp.float32
    ) / math.sqrt(head_size)
    scores = jnp.where(allowed, scores, MASKED)
    row_max = jnp.max(scores, axis=-1, keepdims=True)
    exponent = jnp.exp(scores - row_max)
    soft = exponent / jnp.sum(exponent, axis=-1, keepdims=True)
    rounded = soft.astype(jnp.bfloat16)
    attended = jnp.einsum(
        "bhqk,bkhd->bqhd", rounded, value_heads, preferred_element_type=jnp.float32
    )
    return (attended.astype(jnp.bfloat16).reshape(batches, query_count, inner_width), soft, rounded)


def tile_backward(queries, keyvalue_ext, soft, rounded, inner_grad):
    batches, query_count, inner_width = queries.shape
    head_size = inner_width // HEADS
    query_heads = queries.reshape(batches, query_count, HEADS, head_size)
    key_heads = keyvalue_ext[:, :, :inner_width].reshape(batches, -1, HEADS, head_size)
    value_heads = keyvalue_ext[:, :, inner_width:].reshape(batches, -1, HEADS, head_size)
    grad_heads = inner_grad.reshape(batches, query_count, HEADS, head_size)
    prob_grad = jnp.einsum(
        "bqhd,bkhd->bhqk", grad_heads, value_heads, preferred_element_type=jnp.float32
    )
    row_dot = jnp.sum(soft * prob_grad, axis=-1, keepdims=True)
    score_grad = (soft * (prob_grad - row_dot) / math.sqrt(head_size)).astype(jnp.bfloat16)
    query_grad = jnp.einsum(
        "bhqk,bkhd->bqhd", score_grad, key_heads, preferred_element_type=jnp.float32
    )
    key_grad = jnp.einsum(
        "bhqk,bqhd->bkhd", score_grad, query_heads, preferred_element_type=jnp.float32
    )
    value_grad = jnp.einsum(
        "bhqk,bqhd->bkhd", rounded, grad_heads, preferred_element_type=jnp.float32
    )
    ext_count = key_grad.shape[1]
    joined = jnp.concatenate(
        [
            key_grad.reshape(batches, ext_count, inner_width),
            value_grad.reshape(batches, ext_count, inner_width),
        ],
        axis=-1,
    )
    return (query_grad.astype(jnp.bfloat16).reshape(batches, query_count, inner_width), joined)


def fold_cols(extended):
    left_strip = extended[:, :, :RADIUS]
    right_strip = extended[:, :, extended.shape[2] - RADIUS :]
    middle = extended[:, :, RADIUS : extended.shape[2] - RADIUS]
    from_right = shifted(left_strip, "col", -1)
    from_left = shifted(right_strip, "col", 1)
    inner_cols = middle.shape[2]
    return (
        middle
        + jnp.pad(from_left, ((0, 0), (0, 0), (0, inner_cols - RADIUS), (0, 0)))
        + jnp.pad(from_right, ((0, 0), (0, 0), (inner_cols - RADIUS, 0), (0, 0)))
    )


def fold_rows(extended):
    upper_strip = extended[:, :RADIUS]
    lower_strip = extended[:, extended.shape[1] - RADIUS :]
    middle = extended[:, RADIUS : extended.shape[1] - RADIUS]
    from_below = shifted(upper_strip, "row", -1)
    from_above = shifted(lower_strip, "row", 1)
    inner_rows = middle.shape[1]
    return (
        middle
        + jnp.pad(from_above, ((0, 0), (0, inner_rows - RADIUS), (0, 0), (0, 0)))
        + jnp.pad(from_below, ((0, 0), (inner_rows - RADIUS, 0), (0, 0), (0, 0)))
    )


def local(inputs, norm_gain, w_query, w_keyvalue, w_output, out_grad):
    batches, tile_rows, tile_cols, model_width = inputs.shape
    ext_rows = tile_rows + 2 * RADIUS
    ext_cols = tile_cols + 2 * RADIUS
    standard, spread, normed = normalize(inputs, norm_gain)
    flat_norm = normed.reshape(-1, model_width)
    normed_ext = with_halo(normed, (("row", 1), ("col", 2)), RADIUS).reshape(-1, model_width)
    row_levels = lax.axis_size("row").bit_length() - 1
    row_groups = [[b] for b in range(row_levels)]
    full_query, full_keyvalue, full_output, normed_ext = gather_weights(
        w_query, w_keyvalue, w_output, row_groups[::-1], normed_ext
    )
    inner_width = full_query.shape[1]
    queries = jnp.dot(flat_norm, full_query, preferred_element_type=jnp.float32).astype(
        jnp.bfloat16
    )
    queries = queries.reshape(batches, tile_rows * tile_cols, inner_width)
    keyvalue_ext = jnp.dot(normed_ext, full_keyvalue, preferred_element_type=jnp.float32)
    keyvalue_ext = keyvalue_ext.astype(jnp.bfloat16).reshape(
        batches, ext_rows * ext_cols, 2 * inner_width
    )
    allowed = window_mask(
        lax.axis_index("row") * tile_rows,
        lax.axis_index("col") * tile_cols,
        tile_rows,
        tile_cols,
        tile_rows * lax.axis_size("row"),
        tile_cols * lax.axis_size("col"),
    )
    attended, soft, rounded = tile_forward(queries, keyvalue_ext, allowed)
    projected = jnp.dot(
        attended.reshape(-1, inner_width), full_output, preferred_element_type=jnp.float32
    )
    layer_out = (inputs.astype(jnp.float32) + projected.reshape(inputs.shape)).astype(jnp.bfloat16)
    flat_grad = out_grad.reshape(-1, model_width)
    inner_grad = lax.dot_general(
        flat_grad, full_output, (((1,), (1,)), ((), ())), preferred_element_type=jnp.float32
    ).astype(jnp.bfloat16)
    inner_grad = inner_grad.reshape(batches, tile_rows * tile_cols, inner_width)
    query_grad, keyvalue_part = tile_backward(queries, keyvalue_ext, soft, rounded, inner_grad)
    keyvalue_part = keyvalue_part.reshape(batches, ext_rows, ext_cols, 2 * inner_width)
    owned = fold_rows(fold_cols(keyvalue_part))
    token_grad = owned.astype(jnp.bfloat16).reshape(-1, 2 * inner_width)
    row_count, col_count = lax.axis_size("row"), lax.axis_size("col")
    col_levels = col_count.bit_length() - 1
    feature_part = model_width // row_count
    partial = lax.dot_general(
        normed_ext,
        keyvalue_part.reshape(-1, 2 * inner_width).astype(jnp.bfloat16),
        (((0,), (0,)), ((), ())),
        preferred_element_type=jnp.float32,
    )
    half = partial.shape[1] // 2
    own = axis_bit("col", 0)
    halves = partial.reshape(model_width, 2, half)
    pair_part = lax.dynamic_index_in_dim(halves, own, 1, keepdims=False) + partner_swap(
        lax.dynamic_index_in_dim(halves, 1 - own, 1, keepdims=False), "col", 1
    )
    rows_part = scatter_by_bits(
        pair_part.reshape(row_count, feature_part, half), "row", row_groups
    )[0]
    for bit in range(1, col_levels):
        rows_part = rows_part + partner_swap(rows_part, "col", 1 << bit)
    normed_grad = lax.dot_general(
        query_grad.reshape(-1, inner_width),
        full_query,
        (((1,), (1,)), ((), ())),
        preferred_element_type=jnp.float32,
    )
    normed_grad = normed_grad + lax.dot_general(
        token_grad, full_keyvalue, (((1,), (1,)), ((), ())), preferred_element_type=jnp.float32
    )
    gained = normed_grad.reshape(inputs.shape) * norm_gain
    in_grad = out_grad.astype(jnp.float32) + spread * (
        gained
        - jnp.mean(gained, axis=-1, keepdims=True)
        - standard * jnp.mean(gained * standard, axis=-1, keepdims=True)
    )
    in_grad = in_grad.astype(jnp.bfloat16)
    rows_part, in_grad = lax.optimization_barrier((rows_part, in_grad))
    other = partner_swap(rows_part, "col", 1)
    keyvalue_grad = jnp.where(
        own == 0,
        jnp.concatenate([rows_part, other], axis=1),
        jnp.concatenate([other, rows_part], axis=1),
    )
    return (layer_out, in_grad, keyvalue_grad)


def solution(mesh):
    return jax.shard_map(
        local,
        mesh=mesh,
        in_specs=(
            P(None, "row", "col", None),
            P(),
            P("row", None),
            P("row", None),
            P("row", None),
            P(None, "row", "col", None),
        ),
        out_specs=(P(None, "row", "col", None), P(None, "row", "col", None), P("row", None)),
        check_vma=False,
    )
```

```python
import math

import jax
import jax.numpy as jnp
from jax import lax
from jax.sharding import PartitionSpec as P

HEADS = 8
RADIUS = 6


EPS = 1e-05
MASKED = -1e30


def shifted(value, axis, steps):
    count = lax.axis_size(axis)
    first, last = (max(0, -steps), min(count, count - steps))
    return lax.ppermute(value, axis, [(source, source + steps) for source in range(first, last)])


def with_halo(block, sides, width):
    for axis, dim in sides:
        count = lax.axis_size(axis)
        forward = [(i, i + 1) for i in range(count - 1)]
        backward = [(target, source) for source, target in forward]
        low = lax.ppermute(
            lax.slice_in_dim(block, block.shape[dim] - width, None, axis=dim), axis, forward
        )
        high = lax.ppermute(lax.slice_in_dim(block, 0, width, axis=dim), axis, backward)
        block = jnp.concatenate([low, block, high], axis=dim)
    return block


def partner_swap(value, axis, mask):
    count = lax.axis_size(axis)
    return lax.ppermute(value, axis, [(i, i ^ mask) for i in range(count)])


def axis_bit(axis, bit):
    return (lax.axis_index(axis) // (1 << bit)) % 2


def flips(group):
    for code in range(1, 1 << len(group)):
        yield [(code >> k) % 2 for k in range(len(group))]


def gather_by_bits(block, axis, groups, tie=None, tie_at=3):
    levels = lax.axis_size(axis).bit_length() - 1
    mine = [axis_bit(axis, bit) for bit in range(levels)]
    zero = [0] * block.ndim
    held = jnp.zeros((2,) * levels + block.shape, block.dtype)
    held = lax.dynamic_update_slice(
        held, block.reshape((1,) * levels + block.shape), mine[::-1] + zero
    )
    done = set()
    for step, group in enumerate(groups):
        start = [0 if b in done else mine[b] for b in range(levels)]
        size = [2 if b in done else 1 for b in range(levels)]
        region = lax.dynamic_slice(held, start[::-1] + zero, size[::-1] + list(block.shape))
        if tie is not None and step == tie_at:
            region, tie = lax.optimization_barrier((region, tie))
        arrived = []
        for flip in flips(group):
            mask = sum(f << b for f, b in zip(flip, group))
            place = list(start)
            for f, b in zip(flip, group):
                place[b] = (mine[b] + f) % 2
            arrived.append((partner_swap(region, axis, mask), place))
        for other, place in arrived:
            held = lax.dynamic_update_slice(held, other, place[::-1] + zero)
        done.update(group)
    held = held.reshape((-1,) + block.shape)
    return held if tie is None else (held, tie)


def scatter_by_bits(total, axis, groups, tie=None, tie_at=2):
    levels = lax.axis_size(axis).bit_length() - 1
    mine = [axis_bit(axis, bit) for bit in range(levels)]
    held = total.reshape((2,) * levels + (total.shape[0] // 2**levels,) + total.shape[1:])
    rest = [0] * (held.ndim - levels)
    for step, group in enumerate(groups):
        if tie is not None and step == tie_at:
            held, tie = lax.optimization_barrier((held, tie))
        size = [1 if b in group else held.shape[levels - 1 - b] for b in range(levels)]
        size = size[::-1] + list(held.shape[levels:])
        own = [mine[b] if b in group else 0 for b in range(levels)]
        summed = lax.dynamic_slice(held, own[::-1] + rest, size)
        for flip in flips(group):
            mask = sum(f << b for f, b in zip(flip, group))
            place = list(own)
            for f, b in zip(flip, group):
                place[b] = (mine[b] + f) % 2
            send = lax.dynamic_slice(held, place[::-1] + rest, size)
            summed = summed + partner_swap(send, axis, mask)
        held = summed
    held = held.reshape(held.shape[levels:])
    return held if tie is None else (held, tie)


def gather_weights(w_query, w_keyvalue, w_output, row_groups, tie):
    rows, width = w_query.shape
    kv_rows, kv_width = w_keyvalue.shape
    out_rows = w_output.shape[0]
    qo_pack = jnp.concatenate([w_query.reshape(-1, kv_width), w_output], axis=0)
    own = axis_bit("col", 0)
    packed = jnp.where(own == 0, w_keyvalue, qo_pack)
    fetched, tie = gather_by_bits(packed, "row", row_groups, tie=tie)
    held = jnp.zeros((2,) + fetched.shape, fetched.dtype)
    held = lax.dynamic_update_slice(held, fetched[None], (own, 0, 0, 0))
    held = lax.dynamic_update_slice(held, partner_swap(fetched, "col", 1)[None], (1 - own, 0, 0, 0))
    count = fetched.shape[0]
    query_rows = kv_rows - out_rows
    kv = held[0].reshape(count * kv_rows, kv_width)
    query = held[1, :, :query_rows].reshape(count * rows, width)
    output = held[1, :, query_rows:].reshape(count * out_rows, kv_width)
    return query, kv, output, tie


def normalize(inputs, norm_gain):
    values = inputs.astype(jnp.float32)
    center = values - jnp.mean(values, axis=-1, keepdims=True)
    spread = lax.rsqrt(jnp.mean(center * center, axis=-1, keepdims=True) + EPS)
    standard = center * spread
    return (standard, spread, (standard * norm_gain).astype(jnp.bfloat16))


def window_mask(row_start, col_start, tile_rows, tile_cols, height, map_width):
    ext_rows = tile_rows + 2 * RADIUS
    ext_cols = tile_cols + 2 * RADIUS
    query_pos = jnp.arange(tile_rows * tile_cols, dtype=jnp.int32)
    query_row = query_pos // tile_cols
    query_col = query_pos % tile_cols
    ext_pos = jnp.arange(ext_rows * ext_cols, dtype=jnp.int32)
    ext_row = ext_pos // ext_cols
    ext_col = ext_pos % ext_cols
    nearby = (jnp.abs(ext_row[None, :] - RADIUS - query_row[:, None]) <= RADIUS) & (
        jnp.abs(ext_col[None, :] - RADIUS - query_col[:, None]) <= RADIUS
    )
    global_row = row_start + ext_row - RADIUS
    global_col = col_start + ext_col - RADIUS
    inside = (
        (global_row >= 0) & (global_row < height) & (global_col >= 0) & (global_col < map_width)
    )
    return nearby & inside[None, :]


def tile_forward(queries, keyvalue_ext, allowed):
    batches, query_count, inner_width = queries.shape
    head_size = inner_width // HEADS
    query_heads = queries.reshape(batches, query_count, HEADS, head_size)
    key_heads = keyvalue_ext[:, :, :inner_width].reshape(batches, -1, HEADS, head_size)
    value_heads = keyvalue_ext[:, :, inner_width:].reshape(batches, -1, HEADS, head_size)
    scores = jnp.einsum(
        "bqhd,bkhd->bhqk", query_heads, key_heads, preferred_element_type=jnp.float32
    ) / math.sqrt(head_size)
    scores = jnp.where(allowed, scores, MASKED)
    row_max = jnp.max(scores, axis=-1, keepdims=True)
    exponent = jnp.exp(scores - row_max)
    soft = exponent / jnp.sum(exponent, axis=-1, keepdims=True)
    rounded = soft.astype(jnp.bfloat16)
    attended = jnp.einsum(
        "bhqk,bkhd->bqhd", rounded, value_heads, preferred_element_type=jnp.float32
    )
    return (attended.astype(jnp.bfloat16).reshape(batches, query_count, inner_width), soft, rounded)


def tile_backward(queries, keyvalue_ext, soft, rounded, inner_grad):
    batches, query_count, inner_width = queries.shape
    head_size = inner_width // HEADS
    query_heads = queries.reshape(batches, query_count, HEADS, head_size)
    key_heads = keyvalue_ext[:, :, :inner_width].reshape(batches, -1, HEADS, head_size)
    value_heads = keyvalue_ext[:, :, inner_width:].reshape(batches, -1, HEADS, head_size)
    grad_heads = inner_grad.reshape(batches, query_count, HEADS, head_size)
    prob_grad = jnp.einsum(
        "bqhd,bkhd->bhqk", grad_heads, value_heads, preferred_element_type=jnp.float32
    )
    row_dot = jnp.sum(soft * prob_grad, axis=-1, keepdims=True)
    score_grad = (soft * (prob_grad - row_dot) / math.sqrt(head_size)).astype(jnp.bfloat16)
    query_grad = jnp.einsum(
        "bhqk,bkhd->bqhd", score_grad, key_heads, preferred_element_type=jnp.float32
    )
    key_grad = jnp.einsum(
        "bhqk,bqhd->bkhd", score_grad, query_heads, preferred_element_type=jnp.float32
    )
    value_grad = jnp.einsum(
        "bhqk,bqhd->bkhd", rounded, grad_heads, preferred_element_type=jnp.float32
    )
    ext_count = key_grad.shape[1]
    joined = jnp.concatenate(
        [
            key_grad.reshape(batches, ext_count, inner_width),
            value_grad.reshape(batches, ext_count, inner_width),
        ],
        axis=-1,
    )
    return (query_grad.astype(jnp.bfloat16).reshape(batches, query_count, inner_width), joined)


def fold_cols(extended):
    left_strip = extended[:, :, :RADIUS]
    right_strip = extended[:, :, extended.shape[2] - RADIUS :]
    middle = extended[:, :, RADIUS : extended.shape[2] - RADIUS]
    from_right = shifted(left_strip, "col", -1)
    from_left = shifted(right_strip, "col", 1)
    inner_cols = middle.shape[2]
    return (
        middle
        + jnp.pad(from_left, ((0, 0), (0, 0), (0, inner_cols - RADIUS), (0, 0)))
        + jnp.pad(from_right, ((0, 0), (0, 0), (inner_cols - RADIUS, 0), (0, 0)))
    )


def fold_rows(extended):
    upper_strip = extended[:, :RADIUS]
    lower_strip = extended[:, extended.shape[1] - RADIUS :]
    middle = extended[:, RADIUS : extended.shape[1] - RADIUS]
    from_below = shifted(upper_strip, "row", -1)
    from_above = shifted(lower_strip, "row", 1)
    inner_rows = middle.shape[1]
    return (
        middle
        + jnp.pad(from_above, ((0, 0), (0, inner_rows - RADIUS), (0, 0), (0, 0)))
        + jnp.pad(from_below, ((0, 0), (inner_rows - RADIUS, 0), (0, 0), (0, 0)))
    )


def local(inputs, norm_gain, w_query, w_keyvalue, w_output, out_grad):
    batches, tile_rows, tile_cols, model_width = inputs.shape
    ext_rows = tile_rows + 2 * RADIUS
    ext_cols = tile_cols + 2 * RADIUS
    standard, spread, normed = normalize(inputs, norm_gain)
    flat_norm = normed.reshape(-1, model_width)
    normed_ext = with_halo(normed, (("row", 1), ("col", 2)), RADIUS).reshape(-1, model_width)
    row_levels = lax.axis_size("row").bit_length() - 1
    row_groups = [[b] for b in range(row_levels)]
    full_query, full_keyvalue, full_output, normed_ext = gather_weights(
        w_query, w_keyvalue, w_output, row_groups[::-1], normed_ext
    )
    inner_width = full_query.shape[1]
    queries = jnp.dot(flat_norm, full_query, preferred_element_type=jnp.float32).astype(
        jnp.bfloat16
    )
    queries = queries.reshape(batches, tile_rows * tile_cols, inner_width)
    keyvalue_ext = jnp.dot(normed_ext, full_keyvalue, preferred_element_type=jnp.float32)
    keyvalue_ext = keyvalue_ext.astype(jnp.bfloat16).reshape(
        batches, ext_rows * ext_cols, 2 * inner_width
    )
    allowed = window_mask(
        lax.axis_index("row") * tile_rows,
        lax.axis_index("col") * tile_cols,
        tile_rows,
        tile_cols,
        tile_rows * lax.axis_size("row"),
        tile_cols * lax.axis_size("col"),
    )
    attended, soft, rounded = tile_forward(queries, keyvalue_ext, allowed)
    projected = jnp.dot(
        attended.reshape(-1, inner_width), full_output, preferred_element_type=jnp.float32
    )
    layer_out = (inputs.astype(jnp.float32) + projected.reshape(inputs.shape)).astype(jnp.bfloat16)
    flat_grad = out_grad.reshape(-1, model_width)
    inner_grad = lax.dot_general(
        flat_grad, full_output, (((1,), (1,)), ((), ())), preferred_element_type=jnp.float32
    ).astype(jnp.bfloat16)
    inner_grad = inner_grad.reshape(batches, tile_rows * tile_cols, inner_width)
    query_grad, keyvalue_part = tile_backward(queries, keyvalue_ext, soft, rounded, inner_grad)
    keyvalue_part = keyvalue_part.reshape(batches, ext_rows, ext_cols, 2 * inner_width)
    cols_folded = fold_cols(keyvalue_part)
    row_count, col_count = lax.axis_size("row"), lax.axis_size("col")
    col_levels = col_count.bit_length() - 1
    feature_part = model_width // row_count
    partial = lax.dot_general(
        normed_ext,
        keyvalue_part.reshape(-1, 2 * inner_width).astype(jnp.bfloat16),
        (((0,), (0,)), ((), ())),
        preferred_element_type=jnp.float32,
    )
    half = partial.shape[1] // 2
    own = axis_bit("col", 0)
    halves = partial.reshape(model_width, 2, half)
    pair_part = lax.dynamic_index_in_dim(halves, own, 1, keepdims=False) + partner_swap(
        lax.dynamic_index_in_dim(halves, 1 - own, 1, keepdims=False), "col", 1
    )
    rows_part, cols_folded = scatter_by_bits(
        pair_part.reshape(row_count, feature_part, half), "row", row_groups, tie=cols_folded
    )
    rows_part = rows_part[0]
    owned = fold_rows(cols_folded)
    token_grad = owned.astype(jnp.bfloat16).reshape(-1, 2 * inner_width)
    for bit in range(1, col_levels):
        rows_part = rows_part + partner_swap(rows_part, "col", 1 << bit)
    held = jnp.zeros((2,) + rows_part.shape, rows_part.dtype)
    held = lax.dynamic_update_slice(held, rows_part[None], (own, 0, 0))
    held = lax.dynamic_update_slice(held, partner_swap(rows_part, "col", 1)[None], (1 - own, 0, 0))
    keyvalue_grad = held.transpose(1, 0, 2).reshape(feature_part, -1)
    normed_grad = lax.dot_general(
        query_grad.reshape(-1, inner_width),
        full_query,
        (((1,), (1,)), ((), ())),
        preferred_element_type=jnp.float32,
    )
    normed_grad = normed_grad + lax.dot_general(
        token_grad, full_keyvalue, (((1,), (1,)), ((), ())), preferred_element_type=jnp.float32
    )
    gained = normed_grad.reshape(inputs.shape) * norm_gain
    in_grad = out_grad.astype(jnp.float32) + spread * (
        gained
        - jnp.mean(gained, axis=-1, keepdims=True)
        - standard * jnp.mean(gained * standard, axis=-1, keepdims=True)
    )
    return (layer_out, in_grad.astype(jnp.bfloat16), keyvalue_grad)


def solution(mesh):
    return jax.shard_map(
        local,
        mesh=mesh,
        in_specs=(
            P(None, "row", "col", None),
            P(),
            P("row", None),
            P("row", None),
            P("row", None),
            P(None, "row", "col", None),
        ),
        out_specs=(P(None, "row", "col", None), P(None, "row", "col", None), P("row", None)),
        check_vma=False,
    )
```

```python
import math

import jax
import jax.numpy as jnp
from jax import lax
from jax.sharding import PartitionSpec as P

HEADS = 8
RADIUS = 6


EPS = 1e-05
MASKED = -1e30


def shifted(value, axis, steps):
    count = lax.axis_size(axis)
    first, last = (max(0, -steps), min(count, count - steps))
    return lax.ppermute(value, axis, [(source, source + steps) for source in range(first, last)])


def with_halo(block, sides, width):
    for axis, dim in sides:
        count = lax.axis_size(axis)
        forward = [(i, i + 1) for i in range(count - 1)]
        backward = [(target, source) for source, target in forward]
        low = lax.ppermute(
            lax.slice_in_dim(block, block.shape[dim] - width, None, axis=dim), axis, forward
        )
        high = lax.ppermute(lax.slice_in_dim(block, 0, width, axis=dim), axis, backward)
        block = jnp.concatenate([low, block, high], axis=dim)
    return block


def partner_swap(value, axis, mask):
    count = lax.axis_size(axis)
    return lax.ppermute(value, axis, [(i, i ^ mask) for i in range(count)])


def axis_bit(axis, bit):
    return (lax.axis_index(axis) // (1 << bit)) % 2


def flips(group):
    for code in range(1, 1 << len(group)):
        yield [(code >> k) % 2 for k in range(len(group))]


def gather_by_bits(block, axis, groups, tie=None, tie_at=3):
    levels = lax.axis_size(axis).bit_length() - 1
    mine = [axis_bit(axis, bit) for bit in range(levels)]
    zero = [0] * block.ndim
    held = jnp.zeros((2,) * levels + block.shape, block.dtype)
    held = lax.dynamic_update_slice(
        held, block.reshape((1,) * levels + block.shape), mine[::-1] + zero
    )
    done = set()
    for step, group in enumerate(groups):
        start = [0 if b in done else mine[b] for b in range(levels)]
        size = [2 if b in done else 1 for b in range(levels)]
        region = lax.dynamic_slice(held, start[::-1] + zero, size[::-1] + list(block.shape))
        if tie is not None and step == tie_at:
            region, tie = lax.optimization_barrier((region, tie))
        arrived = []
        for flip in flips(group):
            mask = sum(f << b for f, b in zip(flip, group))
            place = list(start)
            for f, b in zip(flip, group):
                place[b] = (mine[b] + f) % 2
            arrived.append((partner_swap(region, axis, mask), place))
        for other, place in arrived:
            held = lax.dynamic_update_slice(held, other, place[::-1] + zero)
        done.update(group)
    held = held.reshape((-1,) + block.shape)
    return held if tie is None else (held, tie)


def scatter_by_bits(total, axis, groups, tie=None, tie_at=3):
    levels = lax.axis_size(axis).bit_length() - 1
    mine = [axis_bit(axis, bit) for bit in range(levels)]
    held = total.reshape((2,) * levels + (total.shape[0] // 2**levels,) + total.shape[1:])
    rest = [0] * (held.ndim - levels)
    for step, group in enumerate(groups):
        if tie is not None and step == tie_at:
            held, tie = lax.optimization_barrier((held, tie))
        size = [1 if b in group else held.shape[levels - 1 - b] for b in range(levels)]
        size = size[::-1] + list(held.shape[levels:])
        own = [mine[b] if b in group else 0 for b in range(levels)]
        summed = lax.dynamic_slice(held, own[::-1] + rest, size)
        for flip in flips(group):
            mask = sum(f << b for f, b in zip(flip, group))
            place = list(own)
            for f, b in zip(flip, group):
                place[b] = (mine[b] + f) % 2
            send = lax.dynamic_slice(held, place[::-1] + rest, size)
            summed = summed + partner_swap(send, axis, mask)
        held = summed
    held = held.reshape(held.shape[levels:])
    return held if tie is None else (held, tie)


def gather_weights(w_query, w_keyvalue, w_output, row_groups, tie):
    rows, width = w_query.shape
    kv_rows, kv_width = w_keyvalue.shape
    out_rows = w_output.shape[0]
    qo_pack = jnp.concatenate([w_query.reshape(-1, kv_width), w_output], axis=0)
    own = axis_bit("col", 0)
    packed = jnp.where(own == 0, w_keyvalue, qo_pack)
    fetched, tie = gather_by_bits(packed, "row", row_groups, tie=tie)
    held = jnp.zeros((2,) + fetched.shape, fetched.dtype)
    held = lax.dynamic_update_slice(held, fetched[None], (own, 0, 0, 0))
    held = lax.dynamic_update_slice(held, partner_swap(fetched, "col", 1)[None], (1 - own, 0, 0, 0))
    count = fetched.shape[0]
    query_rows = kv_rows - out_rows
    kv = held[0].reshape(count * kv_rows, kv_width)
    query = held[1, :, :query_rows].reshape(count * rows, width)
    output = held[1, :, query_rows:].reshape(count * out_rows, kv_width)
    return query, kv, output, tie


def normalize(inputs, norm_gain):
    values = inputs.astype(jnp.float32)
    center = values - jnp.mean(values, axis=-1, keepdims=True)
    spread = lax.rsqrt(jnp.mean(center * center, axis=-1, keepdims=True) + EPS)
    standard = center * spread
    return (standard, spread, (standard * norm_gain).astype(jnp.bfloat16))


def window_mask(row_start, col_start, tile_rows, tile_cols, height, map_width):
    ext_rows = tile_rows + 2 * RADIUS
    ext_cols = tile_cols + 2 * RADIUS
    query_pos = jnp.arange(tile_rows * tile_cols, dtype=jnp.int32)
    query_row = query_pos // tile_cols
    query_col = query_pos % tile_cols
    ext_pos = jnp.arange(ext_rows * ext_cols, dtype=jnp.int32)
    ext_row = ext_pos // ext_cols
    ext_col = ext_pos % ext_cols
    nearby = (jnp.abs(ext_row[None, :] - RADIUS - query_row[:, None]) <= RADIUS) & (
        jnp.abs(ext_col[None, :] - RADIUS - query_col[:, None]) <= RADIUS
    )
    global_row = row_start + ext_row - RADIUS
    global_col = col_start + ext_col - RADIUS
    inside = (
        (global_row >= 0) & (global_row < height) & (global_col >= 0) & (global_col < map_width)
    )
    return nearby & inside[None, :]


def tile_forward(queries, keyvalue_ext, allowed):
    batches, query_count, inner_width = queries.shape
    head_size = inner_width // HEADS
    query_heads = queries.reshape(batches, query_count, HEADS, head_size)
    key_heads = keyvalue_ext[:, :, :inner_width].reshape(batches, -1, HEADS, head_size)
    value_heads = keyvalue_ext[:, :, inner_width:].reshape(batches, -1, HEADS, head_size)
    scores = jnp.einsum(
        "bqhd,bkhd->bhqk", query_heads, key_heads, preferred_element_type=jnp.float32
    ) / math.sqrt(head_size)
    scores = jnp.where(allowed, scores, MASKED)
    row_max = jnp.max(scores, axis=-1, keepdims=True)
    exponent = jnp.exp(scores - row_max)
    soft = exponent / jnp.sum(exponent, axis=-1, keepdims=True)
    rounded = soft.astype(jnp.bfloat16)
    attended = jnp.einsum(
        "bhqk,bkhd->bqhd", rounded, value_heads, preferred_element_type=jnp.float32
    )
    return (attended.astype(jnp.bfloat16).reshape(batches, query_count, inner_width), soft, rounded)


def tile_backward(queries, keyvalue_ext, soft, rounded, inner_grad):
    batches, query_count, inner_width = queries.shape
    head_size = inner_width // HEADS
    query_heads = queries.reshape(batches, query_count, HEADS, head_size)
    key_heads = keyvalue_ext[:, :, :inner_width].reshape(batches, -1, HEADS, head_size)
    value_heads = keyvalue_ext[:, :, inner_width:].reshape(batches, -1, HEADS, head_size)
    grad_heads = inner_grad.reshape(batches, query_count, HEADS, head_size)
    prob_grad = jnp.einsum(
        "bqhd,bkhd->bhqk", grad_heads, value_heads, preferred_element_type=jnp.float32
    )
    row_dot = jnp.sum(soft * prob_grad, axis=-1, keepdims=True)
    score_grad = (soft * (prob_grad - row_dot) / math.sqrt(head_size)).astype(jnp.bfloat16)
    query_grad = jnp.einsum(
        "bhqk,bkhd->bqhd", score_grad, key_heads, preferred_element_type=jnp.float32
    )
    key_grad = jnp.einsum(
        "bhqk,bqhd->bkhd", score_grad, query_heads, preferred_element_type=jnp.float32
    )
    value_grad = jnp.einsum(
        "bhqk,bqhd->bkhd", rounded, grad_heads, preferred_element_type=jnp.float32
    )
    ext_count = key_grad.shape[1]
    joined = jnp.concatenate(
        [
            key_grad.reshape(batches, ext_count, inner_width),
            value_grad.reshape(batches, ext_count, inner_width),
        ],
        axis=-1,
    )
    return (query_grad.astype(jnp.bfloat16).reshape(batches, query_count, inner_width), joined)


def fold_cols(extended):
    left_strip = extended[:, :, :RADIUS]
    right_strip = extended[:, :, extended.shape[2] - RADIUS :]
    middle = extended[:, :, RADIUS : extended.shape[2] - RADIUS]
    from_right = shifted(left_strip, "col", -1)
    from_left = shifted(right_strip, "col", 1)
    inner_cols = middle.shape[2]
    return (
        middle
        + jnp.pad(from_left, ((0, 0), (0, 0), (0, inner_cols - RADIUS), (0, 0)))
        + jnp.pad(from_right, ((0, 0), (0, 0), (inner_cols - RADIUS, 0), (0, 0)))
    )


def fold_rows(extended):
    upper_strip = extended[:, :RADIUS]
    lower_strip = extended[:, extended.shape[1] - RADIUS :]
    middle = extended[:, RADIUS : extended.shape[1] - RADIUS]
    from_below = shifted(upper_strip, "row", -1)
    from_above = shifted(lower_strip, "row", 1)
    inner_rows = middle.shape[1]
    return (
        middle
        + jnp.pad(from_above, ((0, 0), (0, inner_rows - RADIUS), (0, 0), (0, 0)))
        + jnp.pad(from_below, ((0, 0), (inner_rows - RADIUS, 0), (0, 0), (0, 0)))
    )


def local(inputs, norm_gain, w_query, w_keyvalue, w_output, out_grad):
    batches, tile_rows, tile_cols, model_width = inputs.shape
    ext_rows = tile_rows + 2 * RADIUS
    ext_cols = tile_cols + 2 * RADIUS
    standard, spread, normed = normalize(inputs, norm_gain)
    flat_norm = normed.reshape(-1, model_width)
    normed_ext = with_halo(normed, (("row", 1), ("col", 2)), RADIUS).reshape(-1, model_width)
    row_levels = lax.axis_size("row").bit_length() - 1
    row_groups = [[b] for b in range(row_levels)]
    full_query, full_keyvalue, full_output, normed_ext = gather_weights(
        w_query, w_keyvalue, w_output, row_groups[::-1], normed_ext
    )
    inner_width = full_query.shape[1]
    queries = jnp.dot(flat_norm, full_query, preferred_element_type=jnp.float32).astype(
        jnp.bfloat16
    )
    queries = queries.reshape(batches, tile_rows * tile_cols, inner_width)
    keyvalue_ext = jnp.dot(normed_ext, full_keyvalue, preferred_element_type=jnp.float32)
    keyvalue_ext = keyvalue_ext.astype(jnp.bfloat16).reshape(
        batches, ext_rows * ext_cols, 2 * inner_width
    )
    allowed = window_mask(
        lax.axis_index("row") * tile_rows,
        lax.axis_index("col") * tile_cols,
        tile_rows,
        tile_cols,
        tile_rows * lax.axis_size("row"),
        tile_cols * lax.axis_size("col"),
    )
    attended, soft, rounded = tile_forward(queries, keyvalue_ext, allowed)
    projected = jnp.dot(
        attended.reshape(-1, inner_width), full_output, preferred_element_type=jnp.float32
    )
    layer_out = (inputs.astype(jnp.float32) + projected.reshape(inputs.shape)).astype(jnp.bfloat16)
    flat_grad = out_grad.reshape(-1, model_width)
    inner_grad = lax.dot_general(
        flat_grad, full_output, (((1,), (1,)), ((), ())), preferred_element_type=jnp.float32
    ).astype(jnp.bfloat16)
    inner_grad = inner_grad.reshape(batches, tile_rows * tile_cols, inner_width)
    query_grad, keyvalue_part = tile_backward(queries, keyvalue_ext, soft, rounded, inner_grad)
    keyvalue_part = keyvalue_part.reshape(batches, ext_rows, ext_cols, 2 * inner_width)
    cols_folded = fold_cols(keyvalue_part)
    row_count, col_count = lax.axis_size("row"), lax.axis_size("col")
    col_levels = col_count.bit_length() - 1
    feature_part = model_width // row_count
    partial = lax.dot_general(
        normed_ext,
        keyvalue_part.reshape(-1, 2 * inner_width).astype(jnp.bfloat16),
        (((0,), (0,)), ((), ())),
        preferred_element_type=jnp.float32,
    )
    half = partial.shape[1] // 2
    own = axis_bit("col", 0)
    halves = partial.reshape(model_width, 2, half)
    pair_part = lax.dynamic_index_in_dim(halves, own, 1, keepdims=False) + partner_swap(
        lax.dynamic_index_in_dim(halves, 1 - own, 1, keepdims=False), "col", 1
    )
    rows_part, cols_folded = scatter_by_bits(
        pair_part.reshape(row_count, feature_part, half), "row", row_groups, tie=cols_folded
    )
    rows_part = rows_part[0]
    owned = fold_rows(cols_folded)
    token_grad = owned.astype(jnp.bfloat16).reshape(-1, 2 * inner_width)
    for bit in range(1, col_levels):
        rows_part = rows_part + partner_swap(rows_part, "col", 1 << bit)
    held = jnp.zeros((2,) + rows_part.shape, rows_part.dtype)
    held = lax.dynamic_update_slice(held, rows_part[None], (own, 0, 0))
    held = lax.dynamic_update_slice(held, partner_swap(rows_part, "col", 1)[None], (1 - own, 0, 0))
    keyvalue_grad = held.transpose(1, 0, 2).reshape(feature_part, -1)
    normed_grad = lax.dot_general(
        query_grad.reshape(-1, inner_width),
        full_query,
        (((1,), (1,)), ((), ())),
        preferred_element_type=jnp.float32,
    )
    normed_grad = normed_grad + lax.dot_general(
        token_grad, full_keyvalue, (((1,), (1,)), ((), ())), preferred_element_type=jnp.float32
    )
    gained = normed_grad.reshape(inputs.shape) * norm_gain
    in_grad = out_grad.astype(jnp.float32) + spread * (
        gained
        - jnp.mean(gained, axis=-1, keepdims=True)
        - standard * jnp.mean(gained * standard, axis=-1, keepdims=True)
    )
    return (layer_out, in_grad.astype(jnp.bfloat16), keyvalue_grad)


def solution(mesh):
    return jax.shard_map(
        local,
        mesh=mesh,
        in_specs=(
            P(None, "row", "col", None),
            P(),
            P("row", None),
            P("row", None),
            P("row", None),
            P(None, "row", "col", None),
        ),
        out_specs=(P(None, "row", "col", None), P(None, "row", "col", None), P("row", None)),
        check_vma=False,
    )
```

```python
import math

import jax
import jax.numpy as jnp
from jax import lax
from jax.sharding import PartitionSpec as P

HEADS = 8
RADIUS = 6


EPS = 1e-05
MASKED = -1e30


def shifted(value, axis, steps):
    count = lax.axis_size(axis)
    first, last = (max(0, -steps), min(count, count - steps))
    return lax.ppermute(value, axis, [(source, source + steps) for source in range(first, last)])


def with_halo(block, sides, width):
    for axis, dim in sides:
        count = lax.axis_size(axis)
        forward = [(i, i + 1) for i in range(count - 1)]
        backward = [(target, source) for source, target in forward]
        low = lax.ppermute(
            lax.slice_in_dim(block, block.shape[dim] - width, None, axis=dim), axis, forward
        )
        high = lax.ppermute(lax.slice_in_dim(block, 0, width, axis=dim), axis, backward)
        block = jnp.concatenate([low, block, high], axis=dim)
    return block


def partner_swap(value, axis, mask):
    count = lax.axis_size(axis)
    return lax.ppermute(value, axis, [(i, i ^ mask) for i in range(count)])


def axis_bit(axis, bit):
    return (lax.axis_index(axis) // (1 << bit)) % 2


def flips(group):
    for code in range(1, 1 << len(group)):
        yield [(code >> k) % 2 for k in range(len(group))]


def gather_by_bits(block, axis, groups, tie=None, tie_at=3):
    levels = lax.axis_size(axis).bit_length() - 1
    mine = [axis_bit(axis, bit) for bit in range(levels)]
    zero = [0] * block.ndim
    held = jnp.zeros((2,) * levels + block.shape, block.dtype)
    held = lax.dynamic_update_slice(
        held, block.reshape((1,) * levels + block.shape), mine[::-1] + zero
    )
    done = set()
    for step, group in enumerate(groups):
        start = [0 if b in done else mine[b] for b in range(levels)]
        size = [2 if b in done else 1 for b in range(levels)]
        region = lax.dynamic_slice(held, start[::-1] + zero, size[::-1] + list(block.shape))
        if tie is not None and step == tie_at:
            region, tie = lax.optimization_barrier((region, tie))
        arrived = []
        for flip in flips(group):
            mask = sum(f << b for f, b in zip(flip, group))
            place = list(start)
            for f, b in zip(flip, group):
                place[b] = (mine[b] + f) % 2
            arrived.append((partner_swap(region, axis, mask), place))
        for other, place in arrived:
            held = lax.dynamic_update_slice(held, other, place[::-1] + zero)
        done.update(group)
    held = held.reshape((-1,) + block.shape)
    return held if tie is None else (held, tie)


def scatter_by_bits(total, axis, groups, tie=None, tie_at=1):
    levels = lax.axis_size(axis).bit_length() - 1
    mine = [axis_bit(axis, bit) for bit in range(levels)]
    held = total.reshape((2,) * levels + (total.shape[0] // 2**levels,) + total.shape[1:])
    rest = [0] * (held.ndim - levels)
    for step, group in enumerate(groups):
        if tie is not None and step == tie_at:
            held, tie = lax.optimization_barrier((held, tie))
        size = [1 if b in group else held.shape[levels - 1 - b] for b in range(levels)]
        size = size[::-1] + list(held.shape[levels:])
        own = [mine[b] if b in group else 0 for b in range(levels)]
        summed = lax.dynamic_slice(held, own[::-1] + rest, size)
        for flip in flips(group):
            mask = sum(f << b for f, b in zip(flip, group))
            place = list(own)
            for f, b in zip(flip, group):
                place[b] = (mine[b] + f) % 2
            send = lax.dynamic_slice(held, place[::-1] + rest, size)
            summed = summed + partner_swap(send, axis, mask)
        held = summed
    held = held.reshape(held.shape[levels:])
    return held if tie is None else (held, tie)


def gather_weights(w_query, w_keyvalue, w_output, row_groups, tie):
    rows, width = w_query.shape
    kv_rows, kv_width = w_keyvalue.shape
    out_rows = w_output.shape[0]
    qo_pack = jnp.concatenate([w_query.reshape(-1, kv_width), w_output], axis=0)
    own = axis_bit("col", 0)
    packed = jnp.where(own == 0, w_keyvalue, qo_pack)
    fetched, tie = gather_by_bits(packed, "row", row_groups, tie=tie)
    held = jnp.zeros((2,) + fetched.shape, fetched.dtype)
    held = lax.dynamic_update_slice(held, fetched[None], (own, 0, 0, 0))
    held = lax.dynamic_update_slice(held, partner_swap(fetched, "col", 1)[None], (1 - own, 0, 0, 0))
    count = fetched.shape[0]
    query_rows = kv_rows - out_rows
    kv = held[0].reshape(count * kv_rows, kv_width)
    query = held[1, :, :query_rows].reshape(count * rows, width)
    output = held[1, :, query_rows:].reshape(count * out_rows, kv_width)
    return query, kv, output, tie


def normalize(inputs, norm_gain):
    values = inputs.astype(jnp.float32)
    center = values - jnp.mean(values, axis=-1, keepdims=True)
    spread = lax.rsqrt(jnp.mean(center * center, axis=-1, keepdims=True) + EPS)
    standard = center * spread
    return (standard, spread, (standard * norm_gain).astype(jnp.bfloat16))


def window_mask(row_start, col_start, tile_rows, tile_cols, height, map_width):
    ext_rows = tile_rows + 2 * RADIUS
    ext_cols = tile_cols + 2 * RADIUS
    query_pos = jnp.arange(tile_rows * tile_cols, dtype=jnp.int32)
    query_row = query_pos // tile_cols
    query_col = query_pos % tile_cols
    ext_pos = jnp.arange(ext_rows * ext_cols, dtype=jnp.int32)
    ext_row = ext_pos // ext_cols
    ext_col = ext_pos % ext_cols
    nearby = (jnp.abs(ext_row[None, :] - RADIUS - query_row[:, None]) <= RADIUS) & (
        jnp.abs(ext_col[None, :] - RADIUS - query_col[:, None]) <= RADIUS
    )
    global_row = row_start + ext_row - RADIUS
    global_col = col_start + ext_col - RADIUS
    inside = (
        (global_row >= 0) & (global_row < height) & (global_col >= 0) & (global_col < map_width)
    )
    return nearby & inside[None, :]


def tile_forward(queries, keyvalue_ext, allowed):
    batches, query_count, inner_width = queries.shape
    head_size = inner_width // HEADS
    query_heads = queries.reshape(batches, query_count, HEADS, head_size)
    key_heads = keyvalue_ext[:, :, :inner_width].reshape(batches, -1, HEADS, head_size)
    value_heads = keyvalue_ext[:, :, inner_width:].reshape(batches, -1, HEADS, head_size)
    scores = jnp.einsum(
        "bqhd,bkhd->bhqk", query_heads, key_heads, preferred_element_type=jnp.float32
    ) / math.sqrt(head_size)
    scores = jnp.where(allowed, scores, MASKED)
    row_max = jnp.max(scores, axis=-1, keepdims=True)
    exponent = jnp.exp(scores - row_max)
    soft = exponent / jnp.sum(exponent, axis=-1, keepdims=True)
    rounded = soft.astype(jnp.bfloat16)
    attended = jnp.einsum(
        "bhqk,bkhd->bqhd", rounded, value_heads, preferred_element_type=jnp.float32
    )
    return (attended.astype(jnp.bfloat16).reshape(batches, query_count, inner_width), soft, rounded)


def tile_backward(queries, keyvalue_ext, soft, rounded, inner_grad):
    batches, query_count, inner_width = queries.shape
    head_size = inner_width // HEADS
    query_heads = queries.reshape(batches, query_count, HEADS, head_size)
    key_heads = keyvalue_ext[:, :, :inner_width].reshape(batches, -1, HEADS, head_size)
    value_heads = keyvalue_ext[:, :, inner_width:].reshape(batches, -1, HEADS, head_size)
    grad_heads = inner_grad.reshape(batches, query_count, HEADS, head_size)
    prob_grad = jnp.einsum(
        "bqhd,bkhd->bhqk", grad_heads, value_heads, preferred_element_type=jnp.float32
    )
    row_dot = jnp.sum(soft * prob_grad, axis=-1, keepdims=True)
    score_grad = (soft * (prob_grad - row_dot) / math.sqrt(head_size)).astype(jnp.bfloat16)
    query_grad = jnp.einsum(
        "bhqk,bkhd->bqhd", score_grad, key_heads, preferred_element_type=jnp.float32
    )
    key_grad = jnp.einsum(
        "bhqk,bqhd->bkhd", score_grad, query_heads, preferred_element_type=jnp.float32
    )
    value_grad = jnp.einsum(
        "bhqk,bqhd->bkhd", rounded, grad_heads, preferred_element_type=jnp.float32
    )
    ext_count = key_grad.shape[1]
    joined = jnp.concatenate(
        [
            key_grad.reshape(batches, ext_count, inner_width),
            value_grad.reshape(batches, ext_count, inner_width),
        ],
        axis=-1,
    )
    return (query_grad.astype(jnp.bfloat16).reshape(batches, query_count, inner_width), joined)


def fold_cols(extended):
    left_strip = extended[:, :, :RADIUS]
    right_strip = extended[:, :, extended.shape[2] - RADIUS :]
    middle = extended[:, :, RADIUS : extended.shape[2] - RADIUS]
    from_right = shifted(left_strip, "col", -1)
    from_left = shifted(right_strip, "col", 1)
    inner_cols = middle.shape[2]
    return (
        middle
        + jnp.pad(from_left, ((0, 0), (0, 0), (0, inner_cols - RADIUS), (0, 0)))
        + jnp.pad(from_right, ((0, 0), (0, 0), (inner_cols - RADIUS, 0), (0, 0)))
    )


def fold_rows(extended):
    upper_strip = extended[:, :RADIUS]
    lower_strip = extended[:, extended.shape[1] - RADIUS :]
    middle = extended[:, RADIUS : extended.shape[1] - RADIUS]
    from_below = shifted(upper_strip, "row", -1)
    from_above = shifted(lower_strip, "row", 1)
    inner_rows = middle.shape[1]
    return (
        middle
        + jnp.pad(from_above, ((0, 0), (0, inner_rows - RADIUS), (0, 0), (0, 0)))
        + jnp.pad(from_below, ((0, 0), (inner_rows - RADIUS, 0), (0, 0), (0, 0)))
    )


def local(inputs, norm_gain, w_query, w_keyvalue, w_output, out_grad):
    batches, tile_rows, tile_cols, model_width = inputs.shape
    ext_rows = tile_rows + 2 * RADIUS
    ext_cols = tile_cols + 2 * RADIUS
    standard, spread, normed = normalize(inputs, norm_gain)
    flat_norm = normed.reshape(-1, model_width)
    normed_ext = with_halo(normed, (("row", 1), ("col", 2)), RADIUS).reshape(-1, model_width)
    row_levels = lax.axis_size("row").bit_length() - 1
    row_groups = [[b] for b in range(row_levels)]
    full_query, full_keyvalue, full_output, normed_ext = gather_weights(
        w_query, w_keyvalue, w_output, row_groups[::-1], normed_ext
    )
    inner_width = full_query.shape[1]
    queries = jnp.dot(flat_norm, full_query, preferred_element_type=jnp.float32).astype(
        jnp.bfloat16
    )
    queries = queries.reshape(batches, tile_rows * tile_cols, inner_width)
    keyvalue_ext = jnp.dot(normed_ext, full_keyvalue, preferred_element_type=jnp.float32)
    keyvalue_ext = keyvalue_ext.astype(jnp.bfloat16).reshape(
        batches, ext_rows * ext_cols, 2 * inner_width
    )
    allowed = window_mask(
        lax.axis_index("row") * tile_rows,
        lax.axis_index("col") * tile_cols,
        tile_rows,
        tile_cols,
        tile_rows * lax.axis_size("row"),
        tile_cols * lax.axis_size("col"),
    )
    attended, soft, rounded = tile_forward(queries, keyvalue_ext, allowed)
    projected = jnp.dot(
        attended.reshape(-1, inner_width), full_output, preferred_element_type=jnp.float32
    )
    layer_out = (inputs.astype(jnp.float32) + projected.reshape(inputs.shape)).astype(jnp.bfloat16)
    flat_grad = out_grad.reshape(-1, model_width)
    inner_grad = lax.dot_general(
        flat_grad, full_output, (((1,), (1,)), ((), ())), preferred_element_type=jnp.float32
    ).astype(jnp.bfloat16)
    inner_grad = inner_grad.reshape(batches, tile_rows * tile_cols, inner_width)
    query_grad, keyvalue_part = tile_backward(queries, keyvalue_ext, soft, rounded, inner_grad)
    keyvalue_part = keyvalue_part.reshape(batches, ext_rows, ext_cols, 2 * inner_width)
    cols_folded = fold_cols(keyvalue_part)
    row_count, col_count = lax.axis_size("row"), lax.axis_size("col")
    col_levels = col_count.bit_length() - 1
    feature_part = model_width // row_count
    partial = lax.dot_general(
        normed_ext,
        keyvalue_part.reshape(-1, 2 * inner_width).astype(jnp.bfloat16),
        (((0,), (0,)), ((), ())),
        preferred_element_type=jnp.float32,
    )
    half = partial.shape[1] // 2
    own = axis_bit("col", 0)
    halves = partial.reshape(model_width, 2, half)
    pair_part = lax.dynamic_index_in_dim(halves, own, 1, keepdims=False) + partner_swap(
        lax.dynamic_index_in_dim(halves, 1 - own, 1, keepdims=False), "col", 1
    )
    rows_part, cols_folded = scatter_by_bits(
        pair_part.reshape(row_count, feature_part, half), "row", row_groups, tie=cols_folded
    )
    rows_part = rows_part[0]
    owned = fold_rows(cols_folded)
    token_grad = owned.astype(jnp.bfloat16).reshape(-1, 2 * inner_width)
    for bit in range(1, col_levels):
        rows_part = rows_part + partner_swap(rows_part, "col", 1 << bit)
    held = jnp.zeros((2,) + rows_part.shape, rows_part.dtype)
    held = lax.dynamic_update_slice(held, rows_part[None], (own, 0, 0))
    held = lax.dynamic_update_slice(held, partner_swap(rows_part, "col", 1)[None], (1 - own, 0, 0))
    keyvalue_grad = held.transpose(1, 0, 2).reshape(feature_part, -1)
    normed_grad = lax.dot_general(
        query_grad.reshape(-1, inner_width),
        full_query,
        (((1,), (1,)), ((), ())),
        preferred_element_type=jnp.float32,
    )
    normed_grad = normed_grad + lax.dot_general(
        token_grad, full_keyvalue, (((1,), (1,)), ((), ())), preferred_element_type=jnp.float32
    )
    gained = normed_grad.reshape(inputs.shape) * norm_gain
    in_grad = out_grad.astype(jnp.float32) + spread * (
        gained
        - jnp.mean(gained, axis=-1, keepdims=True)
        - standard * jnp.mean(gained * standard, axis=-1, keepdims=True)
    )
    return (layer_out, in_grad.astype(jnp.bfloat16), keyvalue_grad)


def solution(mesh):
    return jax.shard_map(
        local,
        mesh=mesh,
        in_specs=(
            P(None, "row", "col", None),
            P(),
            P("row", None),
            P("row", None),
            P("row", None),
            P(None, "row", "col", None),
        ),
        out_specs=(P(None, "row", "col", None), P(None, "row", "col", None), P("row", None)),
        check_vma=False,
    )
```
